256 devices in a mesh: seq: 64 (over y, z_lo, x), tp: 4 (over z_hi, core).
Axes of the slice: x: 4, y: 4, z: 8 (z_hi: 2, z_lo: 4; z = z_hi * 4 + z_lo), core: 2. Of those that a mesh axis runs over, the one named last changes fastest.
Arguments:
- hidden: bfloat16 [16384, 1024], P('seq'), may hold values from -6 to 6
- segment_ids: int32 [16384], replicated, may hold values from 0 to 7, never falling along the last dimension, each value on 1 to 12288 neighbouring positions
- routes: int32 [16384, 8], P('seq'), may hold values from 0 to 31, all different within a row; in each aligned block of 128 rows (0 to 127, 128 to 255, ...) at most 64 rows name the same one
- gates: float32 [16384, 8], P('seq'), may hold values from 0.02 to 0.25
- norm_attn: bfloat16 [1024], replicated, may hold values from 0.5 to 1.5
- norm_moe: bfloat16 [1024], replicated, may hold values from 0.5 to 1.5
- w_query: bfloat16 [1024, 1024], P(None, 'tp')
- w_key: bfloat16 [1024, 512], P(None, 'tp')
- w_value: bfloat16 [1024, 512], P(None, 'tp'), may hold values from -0.1875 to 0.1875
- w_out: bfloat16 [1024, 1024], P('tp'), may hold values from -1 to 1
- w_gate: bfloat16 [64, 1024, 512], P('seq', None, 'tp'), as said below
- w_up: bfloat16 [64, 1024, 512], P('seq', None, 'tp'), as said below
- w_down: bfloat16 [64, 512, 1024], P('seq', 'tp'), as said below
Outputs:
- hidden_out: bfloat16 [16384, 1024], P('seq')
- kv_cache: bfloat16 [16384, 2, 512], P('seq', None, 'tp')
The draws below stay inside these ranges and needn't reach their ends.
Inputs may be any that keep to these rules, and one draw needn't show every extreme that they name: `segment_ids`: segment numbers start at 0, never fall and rise by one at each new segment; no segment is longer than 12288 tokens and one has exactly 12288. `routes`: each row names 8 different experts. In each aligned block of 128 rows no expert is named by more than 64 rows, a bound that some block reaches. Slot s holds the weights of expert s mod 32: w_gate[s] equals w_gate[s mod 32]. w_up[s] equals w_up[s mod 32]. w_down[s] equals w_down[s mod 32].
All inputs are finite; a program needn't handle non-finite values.
Results may differ from the reference program's by a relative error of at most 0.018.
Values may be sent and summed in bfloat16 or wider, within the bound.
No kernel may reach another device: no remote copies, remote signals or barrier semaphores. Data moves between devices by JAX's collectives and lax.ppermute only.
A program may use at most 64 MiB of HBM per device.

```python
import math
import jax
import jax.numpy as jnp
import numpy as np
from jax import lax

D = 1024
HEADS = 16
KV_HEADS = 8
HEAD_DIM = 64
EXPERTS = 32
FF = 512
TOPK = 8
TOK_DEV = 256
TOKENS = 16384
SLOTS = 64
COPIES = 2
CAP = 64
SEG_MAX = 12288
SEGS = 8
N_TP = 4


def expert_table(key, rows, cols, fan):
    base = jax.random.normal(key, (EXPERTS, rows, cols), jnp.float32) * fan ** (-0.5)
    return jnp.tile(base, (SLOTS // EXPERTS, 1, 1)).astype(jnp.bfloat16)


def draw_w_gate(key, part):
    return expert_table(jax.random.fold_in(key, 11), D, FF, D)


def draw_w_up(key, part):
    return expert_table(jax.random.fold_in(key, 23), D, FF, D)


def draw_w_down(key, part):
    return expert_table(jax.random.fold_in(key, 37), FF, D, FF)


def draw_hidden(key, part):
    values = jnp.clip(jax.random.normal(jax.random.fold_in(key, 1), (TOKENS, D), jnp.float32), -6.0, 6.0)
    return values.astype(jnp.bfloat16)


def drawn_projection(key, salt, columns):
    values = jax.random.normal(jax.random.fold_in(key, salt), (D, columns), jnp.float32) * D ** (-0.5) * 2.0
    return values.astype(jnp.bfloat16)


def draw_w_query(key, part):
    return drawn_projection(key, 41, HEADS * HEAD_DIM)


def draw_w_key(key, part):
    return drawn_projection(key, 53, KV_HEADS * HEAD_DIM)


def shard_levels(rng, dims, cuts, smallest, high):
    def one(dim, parts):
        heights = jax.random.uniform(jax.random.fold_in(jax.random.fold_in(rng, 6), dim), (parts,), jnp.float32, smallest / len(cuts), high / len(cuts))
        return jnp.repeat(jnp.exp(heights), dims[dim] // parts).reshape((-1,) + (1,) * (len(dims) - dim - 1))

    factor_of = one(*cuts[0])
    for cut in cuts[1:]:
        factor_of = factor_of * one(*cut)
    return factor_of


def length_profile(number_of, total, limit, lean):
    loads = [(1 << 20) // math.isqrt(rank ** lean) + 1 for rank in range(2, number_of + 1)]
    spare, holding = total - limit - (number_of - 1), [1] * (number_of - 1)
    while spare > 0:
        candidates = [i for i in range(number_of - 1) if holding[i] < limit]
        pool, left = sum([loads[i] for i in candidates]), spare
        for i in candidates:
            extra = min(limit - holding[i], max(1, left * loads[i] // pool), spare)
            holding[i] = holding[i] + extra
            spare = spare - extra
    return np.array([limit] + holding)


def uneven_parts(stream_key, amount, total, most, slope):
    if amount == 2:
        one = jax.random.randint(stream_key, (), max(1, total - most), min(most, total - 1) + 1)
        return jnp.stack([one, total - one])
    sizes = jnp.asarray(length_profile(amount, total, most, slope), jnp.int32)
    twos = (amount - 1) // 2
    giver, sink = sizes[1:1 + 2 * twos:2], sizes[2:2 + 2 * twos:2]
    margin = jnp.minimum(giver - 1, most - sink)
    moved = jax.random.randint(jax.random.fold_in(stream_key, 1), (twos,), 0, 1 << 20) % (margin + 1)
    sizes = sizes.at[1:1 + 2 * twos:2].set(giver - moved).at[2:2 + 2 * twos:2].set(sink + moved)
    return sizes[jax.random.permutation(jax.random.fold_in(stream_key, 2), amount)]


def assign_block(key, own, number, rows, amount, top, reach, slope):
    order = jax.random.permutation(key, amount)
    crowded, ordinary = load_shares(amount, rows * top, reach, slope, True), load_shares(amount, rows * top, reach, slope, False)
    places = jnp.arange(amount)

    def named(lengths, offset_by):
        used = int((lengths > 0).sum())
        fixed = max(1, used // 4)
        passed = fixed + (places - fixed + offset_by * (used - fixed)) % max(1, amount - fixed)
        return jnp.zeros((amount,), jnp.int32).at[order[jnp.where(places < fixed, places, passed)]].set(jnp.asarray(lengths, jnp.int32))

    lengths = jnp.where(number % 4 == 0, named(crowded, number // 4), named(ordinary, number - number // 4 - 1))
    mixed = jax.random.permutation(jax.random.fold_in(own, 3), amount)
    source_of, receiver = mixed[0:amount // 2 * 2:2], mixed[1:amount // 2 * 2:2]
    margin = jnp.minimum(lengths[source_of] - 1, reach - lengths[receiver]) // 2
    margin = jnp.where((source_of == order[0]) | (receiver == order[0]) | (lengths[receiver] == 0), 0, jnp.maximum(margin, 0))
    passed = jax.random.randint(jax.random.fold_in(own, 4), (amount // 2,), 0, 1 << 20) % (margin + 1)
    lengths = lengths.at[source_of].add(-passed).at[receiver].add(passed)
    labels = jnp.searchsorted(jnp.cumsum(lengths), jnp.arange(rows * top), side="right").astype(jnp.int32)
    grid = labels.reshape(top, rows).T
    grid = grid[jax.random.permutation(jax.random.fold_in(own, 1), rows)]
    offset_by = jax.random.randint(jax.random.fold_in(own, 2), (rows, 1), 0, top)
    return jnp.take_along_axis(grid, (jnp.arange(top)[None, :] + offset_by) % top, axis=1)


def load_shares(number_of, total, bound, skew, full):
    weights = [(1 << 20) // math.isqrt(rank ** skew) + 1 for rank in range(1, number_of + 1)]
    largest = bound if full else min(bound, max(-(-total // number_of), total * weights[0] // sum(weights)))
    least = 1 if total - largest >= number_of - 1 else 0
    holding, rest = [largest] + [least] * (number_of - 1), total - largest - least * (number_of - 1)
    while rest > 0:
        movable = [i for i in range(1, number_of) if holding[i] < largest] or [i for i in range(1, number_of) if holding[i] < bound]
        whole, budget = sum([weights[i] for i in movable]), rest
        for i in movable:
            addition = min(bound - holding[i], max(1, budget * weights[i] // whole), rest)
            holding[i] = holding[i] + addition
            rest = rest - addition
    return np.array(holding)


def scatter_about(rng, extent, spread, bound, pieces=(), kind=jnp.bfloat16):
    drawn = jax.random.normal(rng, extent, jnp.float32) * spread
    if len(pieces) > 0:
        drawn = shard_levels(rng, extent, pieces, -0.22, 0.18) * drawn
    return jnp.clip(drawn, min=-bound, max=bound).astype(kind)


def setup_inputs(seed: int = 0) -> dict:
    key_of = jax.random.split(jax.random.key(seed), 14)
    hidden = draw_hidden(jax.random.fold_in(key_of[13], 71), 0)
    segment_ids = jnp.searchsorted(jnp.cumsum(uneven_parts(key_of[1], SEGS, TOKENS, SEG_MAX, 2)), jnp.arange(TOKENS), side="right").astype(jnp.int32)
    routes_keys = jax.random.split(jax.random.fold_in(key_of[2], 1), TOKENS // (TOK_DEV // COPIES))
    routes_turns = jax.random.permutation(jax.random.fold_in(key_of[2], 3), TOKENS // (TOK_DEV // COPIES))
    routes = jax.vmap(lambda own, number: assign_block(jax.random.fold_in(key_of[2], 2), own, number, TOK_DEV // COPIES, EXPERTS, TOPK, CAP, 1))(routes_keys, routes_turns).reshape((TOKENS, TOPK))
    gates = jnp.clip(0.02 + 0.23 * jax.random.uniform(key_of[3], (TOKENS, TOPK), jnp.float32) ** shard_levels(key_of[3], (TOKENS, TOPK), ((0, 64),), -0.2, 0.2), 0.02, 0.25)
    norm_attn = jnp.clip(1.0 + 0.1 * jax.random.normal(key_of[4], (D,), jnp.float32), 0.5, 1.5).astype(jnp.bfloat16)
    norm_moe = jnp.clip(1.0 + 0.1 * jax.random.normal(key_of[5], (D,), jnp.float32), 0.5, 1.5).astype(jnp.bfloat16)
    w_query = draw_w_query(jax.random.fold_in(key_of[13], 71), 0)
    w_key = draw_w_key(jax.random.fold_in(key_of[13], 71), 0)
    w_value = scatter_about(key_of[8], (D, KV_HEADS * HEAD_DIM), D ** -0.5, 0.1875, ((1, 4),))
    w_out = scatter_about(key_of[9], (HEADS * HEAD_DIM, D), (HEAD_DIM // 2) ** -0.5, 1.0, ((0, 4),))
    w_gate = draw_w_gate(jax.random.fold_in(key_of[13], 71), 0)
    w_up = draw_w_up(jax.random.fold_in(key_of[13], 71), 0)
    w_down = draw_w_down(jax.random.fold_in(key_of[13], 71), 0)
    return {"hidden": hidden, "segment_ids": segment_ids, "routes": routes, "gates": gates, "norm_attn": norm_attn, "norm_moe": norm_moe, "w_query": w_query, "w_key": w_key, "w_value": w_value, "w_out": w_out, "w_gate": w_gate, "w_up": w_up, "w_down": w_down}


EPS = 1e-06
SCORE_SCALE = 0.015625

def normalize(values, gain):
    widened = values.astype(jnp.float32)
    return widened * lax.rsqrt(lax.optimization_barrier(jnp.mean(widened * widened, axis=-1, keepdims=True)) + EPS) * gain.astype(jnp.float32)

def rotary(tensor, positions):
    half_dim = tensor.shape[-1] // 2
    frequencies = 10000.0 ** (-jnp.arange(half_dim, dtype=jnp.float32) * 2.0 / tensor.shape[-1])
    angles = positions.astype(jnp.float32)[:, None] * frequencies[None, :]
    cosine = jnp.cos(angles)[:, None, :]
    sine_part = jnp.sin(angles)[:, None, :]
    lower_half = tensor[..., :half_dim]
    upper_half = tensor[..., half_dim:]
    return jnp.concatenate([lower_half * cosine - upper_half * sine_part, upper_half * cosine + lower_half * sine_part], axis=-1)

def segment_positions(segment_ids):
    index_all = jnp.arange(segment_ids.shape[0], dtype=jnp.int32)
    changed = jnp.concatenate([jnp.ones((1,), jnp.bool_), segment_ids[1:] != segment_ids[:-1]])
    starts = lax.cummax(jnp.where(changed, index_all, 0), axis=0)
    return index_all - starts

def attention(queries, key_rot, value_heads, segment_ids):
    total_rows = queries.shape[0]
    block_rows = min(512, total_rows)
    group_size = HEADS // KV_HEADS
    block_count = total_rows // block_rows
    grouped = queries.reshape(block_count, block_rows, KV_HEADS, group_size, HEAD_DIM)

    def one_block(query_block):
        query_rows = lax.dynamic_index_in_dim(grouped, query_block, 0, keepdims=False).astype(jnp.float32)
        query_start = query_block * block_rows
        query_index = query_start + jnp.arange(block_rows, dtype=jnp.int32)
        query_segs = lax.dynamic_slice_in_dim(segment_ids, query_start, block_rows)

        def visit_block(key_block, carried):
            key_start = key_block * block_rows
            key_segs = lax.dynamic_slice_in_dim(segment_ids, key_start, block_rows)

            def update(state):
                running_max, weight_sum, accumulated = state
                key_rows = lax.dynamic_slice_in_dim(key_rot, key_start, block_rows).astype(jnp.float32)
                value_rows = lax.dynamic_slice_in_dim(value_heads, key_start, block_rows).astype(jnp.float32)
                scores = jnp.einsum('tkgd,skd->kgts', query_rows, key_rows) * SCORE_SCALE
                key_index = key_start + jnp.arange(block_rows, dtype=jnp.int32)
                allowed = (query_segs[:, None] == key_segs[None, :]) & (query_index[:, None] >= key_index[None, :])
                masked = jnp.where(allowed, scores, -1e+30)
                new_max = jnp.maximum(running_max, lax.optimization_barrier(jnp.max(masked, axis=-1)))
                weights = jnp.where(allowed, jnp.exp(masked - new_max[..., None]), 0.0)
                factor = jnp.exp(running_max - new_max)
                weight_sum = weight_sum * factor + lax.optimization_barrier(jnp.sum(weights, axis=-1))
                rounded = lax.optimization_barrier(weights.astype(jnp.bfloat16)).astype(jnp.float32)
                accumulated = accumulated * factor[..., None] + jnp.einsum('kgts,skd->kgtd', rounded, value_rows)
                return (new_max, weight_sum, accumulated)
            relevant = key_segs[block_rows - 1] >= query_segs[0]
            return lax.cond(relevant, update, lambda state: state, carried)
        start_state = (jnp.full((KV_HEADS, group_size, block_rows), -1e+30, jnp.float32), jnp.zeros((KV_HEADS, group_size, block_rows), jnp.float32), jnp.zeros((KV_HEADS, group_size, block_rows, HEAD_DIM), jnp.float32))
        running_max, weight_sum, accumulated = lax.fori_loop(0, query_block + 1, visit_block, start_state)
        result = accumulated / weight_sum[..., None]
        return result.transpose(2, 0, 1, 3).reshape(block_rows, HEADS * HEAD_DIM).astype(jnp.bfloat16)
    blocks = lax.map(one_block, jnp.arange(block_count, dtype=jnp.int32))
    return blocks.reshape(total_rows, HEADS * HEAD_DIM)

def experts_reference(normed_rows, routes, gates, w_gate, w_up, w_down):
    total_rows, route_count = routes.shape
    flat = routes.reshape(-1)
    items = flat.shape[0]
    tile_rows = 256
    order = jnp.argsort(flat, stable=True).astype(jnp.int32)
    sorted_experts = flat[order]
    counts = lax.optimization_barrier(jnp.sum((flat[:, None] == jnp.arange(EXPERTS, dtype=jnp.int32)[None, :]).astype(jnp.int32), axis=0))
    padded_counts = (counts + tile_rows - 1) // tile_rows * tile_rows
    pad_starts = jnp.cumsum(padded_counts) - padded_counts
    plain_starts = jnp.cumsum(counts) - counts
    slot_index = pad_starts[sorted_experts] + jnp.arange(items, dtype=jnp.int32) - plain_starts[sorted_experts]
    tile_total = (items + tile_rows - 1) // tile_rows + EXPERTS
    capacity_rows = tile_total * tile_rows
    token_of = jnp.full((capacity_rows,), total_rows, jnp.int32).at[slot_index].set((order // route_count).astype(jnp.int32))
    gate_of = jnp.zeros((capacity_rows,), jnp.float32).at[slot_index].set(gates.reshape(-1)[order])
    tile_starts = jnp.arange(tile_total, dtype=jnp.int32) * tile_rows
    tile_expert = lax.optimization_barrier(jnp.sum((pad_starts[None, :] <= tile_starts[:, None]).astype(jnp.int32), axis=1)) - 1
    padded_rows = jnp.concatenate([normed_rows, jnp.zeros((1, normed_rows.shape[1]), normed_rows.dtype)])
    group_units = FF // N_TP

    def tile_step(accumulated, tile):
        rows_index = lax.dynamic_slice_in_dim(token_of, tile * tile_rows, tile_rows)
        tile_gates = lax.dynamic_slice_in_dim(gate_of, tile * tile_rows, tile_rows)
        expert = tile_expert[tile]
        rows = padded_rows[rows_index].astype(jnp.float32)
        gate_val = jnp.dot(rows, w_gate[expert].astype(jnp.float32))
        up_val = jnp.dot(rows, w_up[expert].astype(jnp.float32))
        activated = lax.optimization_barrier((jax.nn.silu(gate_val) * up_val).astype(jnp.bfloat16)).astype(jnp.float32)
        split_act = activated.reshape(tile_rows, N_TP, group_units)
        split_down = w_down[expert].astype(jnp.float32).reshape(N_TP, group_units, D)
        partial_value = jnp.einsum('tqf,qfd->tqd', split_act, split_down).astype(jnp.bfloat16)
        partial_value = lax.optimization_barrier(partial_value).astype(jnp.float32)
        output_rows = lax.optimization_barrier(jnp.sum(partial_value, axis=1)) * tile_gates[:, None]
        return (accumulated.at[rows_index].add(output_rows), None)
    start_sum = jnp.zeros((total_rows + 1, normed_rows.shape[1]), jnp.float32)
    result, unused = lax.scan(tile_step, start_sum, jnp.arange(tile_total, dtype=jnp.int32))
    return result[:total_rows]

def reference(hidden, segment_ids, routes, gates, norm_attn, norm_moe, w_query, w_key, w_value, w_out, w_gate, w_up, w_down):
    positions = segment_positions(segment_ids)
    normed = normalize(hidden, norm_attn).astype(jnp.bfloat16)
    queries = jnp.dot(normed, w_query, preferred_element_type=jnp.float32).reshape(TOKENS, HEADS, HEAD_DIM)
    queries = rotary(queries, positions).astype(jnp.bfloat16)
    key_raw = jnp.dot(normed, w_key, preferred_element_type=jnp.float32).reshape(TOKENS, KV_HEADS, HEAD_DIM)
    value_proj = jnp.dot(normed, w_value, preferred_element_type=jnp.float32).astype(jnp.bfloat16)
    kv_cache = jnp.stack([key_raw.reshape(TOKENS, KV_HEADS * HEAD_DIM).astype(jnp.bfloat16), value_proj], axis=1)
    key_rot = rotary(key_raw, positions).astype(jnp.bfloat16)
    value_heads = value_proj.reshape(TOKENS, KV_HEADS, HEAD_DIM)
    attended = attention(queries, key_rot, value_heads, segment_ids)
    mixed = jnp.dot(attended, w_out, preferred_element_type=jnp.float32)
    residual = (hidden.astype(jnp.float32) + mixed).astype(jnp.bfloat16)
    normed_moe = normalize(residual, norm_moe).astype(jnp.bfloat16)
    expert_sum = experts_reference(normed_moe, routes, gates, w_gate, w_up, w_down)
    hidden_out = (residual.astype(jnp.float32) + expert_sum).astype(jnp.bfloat16)
    return (hidden_out, kv_cache)
```

```python
import jax
import jax.numpy as jnp
from jax import lax
from jax.sharding import Mesh
from jax.sharding import PartitionSpec as P

HEAD_DIM = 64
EXPERTS = 32
SEG_VALUES = 8
KEY_CHUNK = 1024

EPS = 1e-06
SCORE_SCALE = 0.015625
SUB_AXES = ("sy", "sz", "sx")


def normalize(values, gain):
    widened = values.astype(jnp.float32)
    return (
        widened
        * lax.rsqrt(jnp.mean(widened * widened, axis=-1, keepdims=True) + EPS)
        * gain.astype(jnp.float32)
    )


def rotary(tensor, positions):
    half_dim = tensor.shape[-1] // 2
    frequencies = 10000.0 ** (-jnp.arange(half_dim, dtype=jnp.float32) * 2.0 / tensor.shape[-1])
    angles = positions.astype(jnp.float32)[:, None] * frequencies[None, :]
    cosine = jnp.cos(angles)[:, None, :]
    sine_part = jnp.sin(angles)[:, None, :]
    lower_half = tensor[..., :half_dim]
    upper_half = tensor[..., half_dim:]
    return jnp.concatenate(
        [
            lower_half * cosine - upper_half * sine_part,
            upper_half * cosine + lower_half * sine_part,
        ],
        axis=-1,
    )


def per_device(
    hidden,
    segment_ids,
    routes,
    gates,
    norm_attn,
    norm_moe,
    w_query,
    w_key,
    w_value,
    w_out,
    w_gate,
    w_up,
    w_down,
):
    tokens = hidden.shape[0]
    model_width = hidden.shape[1]
    total_tokens = segment_ids.shape[0]
    first_row = lax.axis_index(SUB_AXES) * tokens
    own_segs = lax.dynamic_slice_in_dim(segment_ids, first_row, tokens)
    seg_starts = jnp.sum(
        (segment_ids[None, :] < jnp.arange(SEG_VALUES, dtype=jnp.int32)[:, None]).astype(jnp.int32),
        axis=1,
    )
    query_index = first_row + jnp.arange(tokens, dtype=jnp.int32)
    positions = query_index - seg_starts[own_segs]
    normed = normalize(hidden, norm_attn).astype(jnp.bfloat16)
    query_heads = w_query.shape[1] // HEAD_DIM
    kv_heads = w_key.shape[1] // HEAD_DIM
    group_size = query_heads // kv_heads
    queries = jnp.dot(normed, w_query, preferred_element_type=jnp.float32).reshape(
        tokens, query_heads, HEAD_DIM
    )
    queries = (
        rotary(queries, positions)
        .astype(jnp.bfloat16)
        .reshape(tokens, kv_heads, group_size, HEAD_DIM)
        .transpose(1, 2, 0, 3)
    )
    key_raw = jnp.dot(normed, w_key, preferred_element_type=jnp.float32).reshape(
        tokens, kv_heads, HEAD_DIM
    )
    value_proj = jnp.dot(normed, w_value, preferred_element_type=jnp.float32).astype(jnp.bfloat16)
    kv_cache = jnp.stack(
        [key_raw.reshape(tokens, kv_heads * HEAD_DIM).astype(jnp.bfloat16), value_proj], axis=1
    )
    key_rot = rotary(key_raw, positions).astype(jnp.bfloat16)
    kv_width = kv_heads * HEAD_DIM
    joined = jnp.concatenate([key_rot.reshape(tokens, kv_width), value_proj], axis=1)
    for axis_name in SUB_AXES[::-1]:
        joined = lax.all_gather(joined, axis_name, axis=0, tiled=True)
    keys_all = joined[:, :kv_width].reshape(total_tokens, kv_heads, HEAD_DIM).transpose(1, 0, 2)
    values_all = joined[:, kv_width:].reshape(total_tokens, kv_heads, HEAD_DIM).transpose(1, 0, 2)
    last_query = first_row + tokens - 1
    lowest_seg = own_segs[0]
    chunk_ends = segment_ids[KEY_CHUNK - 1 :: KEY_CHUNK]
    first_chunk = jnp.sum((chunk_ends < lowest_seg).astype(jnp.int32))
    last_chunk = last_query // KEY_CHUNK

    def visit_chunk(chunk, carried):
        running_max, weight_sum, accumulated = carried
        key_start = chunk * KEY_CHUNK
        key_rows = lax.dynamic_slice_in_dim(keys_all, key_start, KEY_CHUNK, axis=1)
        value_rows = lax.dynamic_slice_in_dim(values_all, key_start, KEY_CHUNK, axis=1)
        key_segs = lax.dynamic_slice_in_dim(segment_ids, key_start, KEY_CHUNK)
        scores = (
            jnp.einsum("kgtd,ksd->kgts", queries, key_rows, preferred_element_type=jnp.float32)
            * SCORE_SCALE
        )
        key_index = key_start + jnp.arange(KEY_CHUNK, dtype=jnp.int32)
        allowed = (own_segs[:, None] == key_segs[None, :]) & (
            query_index[:, None] >= key_index[None, :]
        )
        masked = jnp.where(allowed, scores, -1e30)
        new_max = jnp.maximum(running_max, jnp.max(masked, axis=-1))
        weights = jnp.where(allowed, jnp.exp(masked - new_max[..., None]), 0.0)
        factor = jnp.exp(running_max - new_max)
        weight_sum = weight_sum * factor + jnp.sum(weights, axis=-1)
        accumulated = accumulated * factor[..., None] + jnp.einsum(
            "kgts,ksd->kgtd",
            weights.astype(jnp.bfloat16),
            value_rows,
            preferred_element_type=jnp.float32,
        )
        return (new_max, weight_sum, accumulated)

    start_state = (
        jnp.full((kv_heads, group_size, tokens), -1e30, jnp.float32),
        jnp.zeros((kv_heads, group_size, tokens), jnp.float32),
        jnp.zeros((kv_heads, group_size, tokens, HEAD_DIM), jnp.float32),
    )
    running_max, weight_sum, accumulated = lax.fori_loop(
        first_chunk, last_chunk + 1, visit_chunk, start_state
    )
    attended = (
        (accumulated / weight_sum[..., None])
        .transpose(2, 0, 1, 3)
        .reshape(tokens, query_heads * HEAD_DIM)
    )
    attended = attended.astype(jnp.bfloat16)
    partial_out = jnp.dot(attended, w_out, preferred_element_type=jnp.float32)
    attn_mixed = lax.psum(partial_out.astype(jnp.bfloat16), "tp").astype(jnp.float32)
    residual = (hidden.astype(jnp.float32) + attn_mixed).astype(jnp.bfloat16)
    normed_moe = normalize(residual, norm_moe).astype(jnp.bfloat16)
    route_count = routes.shape[1]
    slots_dev = w_gate.shape[0]
    seq_count = lax.axis_size(SUB_AXES)
    slot_total = slots_dev * seq_count
    copies = slot_total // EXPERTS
    block_rows = tokens // copies
    capacity = 2 * block_rows * route_count // EXPERTS
    copy_of = (jnp.arange(tokens, dtype=jnp.int32) // block_rows)[:, None]
    slot_of = routes + EXPERTS * copy_of
    flat_expert = routes.reshape(copies, block_rows * route_count)
    onehot = (
        flat_expert[:, :, None] == jnp.arange(EXPERTS, dtype=jnp.int32)[None, None, :]
    ).astype(jnp.int32)
    before = jnp.cumsum(onehot, axis=1) - onehot
    slot_rank = jnp.sum(before * onehot, axis=2).reshape(tokens, route_count)
    target = slot_of * capacity + slot_rank
    token_ids = jnp.broadcast_to(
        jnp.arange(tokens, dtype=jnp.int32)[:, None], (tokens, route_count)
    )
    source = (
        jnp.full((slot_total * capacity,), tokens, jnp.int32)
        .at[target.reshape(-1)]
        .set(token_ids.reshape(-1))
    )
    padded_rows = jnp.concatenate([normed_moe, jnp.zeros((1, normed_moe.shape[1]), jnp.bfloat16)])
    outbound = padded_rows[source].reshape(seq_count, slots_dev, capacity, normed_moe.shape[1])
    arrived = lax.all_to_all(outbound, SUB_AXES, split_axis=0, concat_axis=0, tiled=True)
    gate_val = jnp.einsum("jsrd,sdf->jsrf", arrived, w_gate, preferred_element_type=jnp.float32)
    up_val = jnp.einsum("jsrd,sdf->jsrf", arrived, w_up, preferred_element_type=jnp.float32)
    activated = (jax.nn.silu(gate_val) * up_val).astype(jnp.bfloat16)
    group_part = jnp.einsum("jsrf,sfd->jsrd", activated, w_down, preferred_element_type=jnp.float32)
    result = group_part.astype(jnp.bfloat16)
    returned = lax.all_to_all(result, SUB_AXES, split_axis=0, concat_axis=0, tiled=True).reshape(
        slot_total * capacity, model_width
    )
    picked = returned[target]
    combined = jnp.einsum(
        "tk,tkd->td",
        gates,
        picked,
        preferred_element_type=jnp.float32,
        precision=lax.Precision.HIGHEST,
    )
    expert_sum = lax.psum(combined.astype(jnp.bfloat16), "tp").astype(jnp.float32)
    hidden_out = (residual.astype(jnp.float32) + expert_sum).astype(jnp.bfloat16)
    return (hidden_out, kv_cache)


def solution(mesh):
    seq_size, tp_size = mesh.devices.shape
    side = round(seq_size ** (1 / 3))
    sub_mesh = Mesh(mesh.devices.reshape(side, side, seq_size // side // side, tp_size), SUB_AXES + ("tp",))
    return jax.shard_map(
        per_device,
        mesh=sub_mesh,
        in_specs=(
            P(SUB_AXES, None),
            P(),
            P(SUB_AXES, None),
            P(SUB_AXES, None),
            P(),
            P(),
            P(None, "tp"),
            P(None, "tp"),
            P(None, "tp"),
            P("tp", None),
            P(SUB_AXES, None, "tp"),
            P(SUB_AXES, None, "tp"),
            P(SUB_AXES, "tp", None),
        ),
        out_specs=(P(SUB_AXES, None), P(SUB_AXES, None, "tp")),
        check_vma=False,
    )
```

```python
import jax
import jax.numpy as jnp
from jax import lax
from jax.sharding import Mesh
from jax.sharding import PartitionSpec as P

HEAD_DIM = 64
EXPERTS = 32
SEG_VALUES = 8
KEY_CHUNK = 1024

EPS = 1e-06
SCORE_SCALE = 0.015625
SUB_AXES = ("sy", "sz", "sx")
TP_AXES = ("tz", "tc")


def normalize(values, gain):
    widened = values.astype(jnp.float32)
    return (
        widened
        * lax.rsqrt(jnp.mean(widened * widened, axis=-1, keepdims=True) + EPS)
        * gain.astype(jnp.float32)
    )


def rotary(tensor, positions):
    half_dim = tensor.shape[-1] // 2
    frequencies = 10000.0 ** (-jnp.arange(half_dim, dtype=jnp.float32) * 2.0 / tensor.shape[-1])
    angles = positions.astype(jnp.float32)[:, None] * frequencies[None, :]
    cosine = jnp.cos(angles)[:, None, :]
    sine_part = jnp.sin(angles)[:, None, :]
    lower_half = tensor[..., :half_dim]
    upper_half = tensor[..., half_dim:]
    return jnp.concatenate(
        [
            lower_half * cosine - upper_half * sine_part,
            upper_half * cosine + lower_half * sine_part,
        ],
        axis=-1,
    )


def per_device(
    hidden,
    segment_ids,
    routes,
    gates,
    norm_attn,
    norm_moe,
    w_query,
    w_key,
    w_value,
    w_out,
    w_gate,
    w_up,
    w_down,
):
    tokens = hidden.shape[0]
    model_width = hidden.shape[1]
    total_tokens = segment_ids.shape[0]
    first_row = lax.axis_index(SUB_AXES) * tokens
    own_segs = lax.dynamic_slice_in_dim(segment_ids, first_row, tokens)
    seg_starts = jnp.sum(
        (segment_ids[None, :] < jnp.arange(SEG_VALUES, dtype=jnp.int32)[:, None]).astype(jnp.int32),
        axis=1,
    )
    query_index = first_row + jnp.arange(tokens, dtype=jnp.int32)
    positions = query_index - seg_starts[own_segs]
    normed = normalize(hidden, norm_attn).astype(jnp.bfloat16)
    query_heads = w_query.shape[1] // HEAD_DIM
    kv_heads = w_key.shape[1] // HEAD_DIM
    group_size = query_heads // kv_heads
    queries = jnp.dot(normed, w_query, preferred_element_type=jnp.float32).reshape(
        tokens, query_heads, HEAD_DIM
    )
    queries = (
        rotary(queries, positions)
        .astype(jnp.bfloat16)
        .reshape(tokens, kv_heads, group_size, HEAD_DIM)
        .transpose(1, 2, 0, 3)
    )
    key_raw = jnp.dot(normed, w_key, preferred_element_type=jnp.float32).reshape(
        tokens, kv_heads, HEAD_DIM
    )
    value_proj = jnp.dot(normed, w_value, preferred_element_type=jnp.float32).astype(jnp.bfloat16)
    kv_cache = jnp.stack(
        [key_raw.reshape(tokens, kv_heads * HEAD_DIM).astype(jnp.bfloat16), value_proj], axis=1
    )
    key_rot = rotary(key_raw, positions).astype(jnp.bfloat16)
    kv_width = kv_heads * HEAD_DIM
    joined = jnp.concatenate([key_rot.reshape(tokens, kv_width), value_proj], axis=1)
    for axis_name in SUB_AXES[::-1]:
        joined = lax.all_gather(joined, axis_name, axis=0, tiled=True)
    keys_all = joined[:, :kv_width].reshape(total_tokens, kv_heads, HEAD_DIM).transpose(1, 0, 2)
    values_all = joined[:, kv_width:].reshape(total_tokens, kv_heads, HEAD_DIM).transpose(1, 0, 2)
    last_query = first_row + tokens - 1
    lowest_seg = own_segs[0]
    chunk_ends = segment_ids[KEY_CHUNK - 1 :: KEY_CHUNK]
    first_chunk = jnp.sum((chunk_ends < lowest_seg).astype(jnp.int32))
    last_chunk = last_query // KEY_CHUNK

    def visit_chunk(chunk, carried):
        running_max, weight_sum, accumulated = carried
        key_start = chunk * KEY_CHUNK
        key_rows = lax.dynamic_slice_in_dim(keys_all, key_start, KEY_CHUNK, axis=1)
        value_rows = lax.dynamic_slice_in_dim(values_all, key_start, KEY_CHUNK, axis=1)
        key_segs = lax.dynamic_slice_in_dim(segment_ids, key_start, KEY_CHUNK)
        scores = (
            jnp.einsum("kgtd,ksd->kgts", queries, key_rows, preferred_element_type=jnp.float32)
            * SCORE_SCALE
        )
        key_index = key_start + jnp.arange(KEY_CHUNK, dtype=jnp.int32)
        allowed = (own_segs[:, None] == key_segs[None, :]) & (
            query_index[:, None] >= key_index[None, :]
        )
        masked = jnp.where(allowed, scores, -1e30)
        new_max = jnp.maximum(running_max, jnp.max(masked, axis=-1))
        weights = jnp.where(allowed, jnp.exp(masked - new_max[..., None]), 0.0)
        factor = jnp.exp(running_max - new_max)
        weight_sum = weight_sum * factor + jnp.sum(weights, axis=-1)
        accumulated = accumulated * factor[..., None] + jnp.einsum(
            "kgts,ksd->kgtd",
            weights.astype(jnp.bfloat16),
            value_rows,
            preferred_element_type=jnp.float32,
        )
        return (new_max, weight_sum, accumulated)

    start_state = (
        jnp.full((kv_heads, group_size, tokens), -1e30, jnp.float32),
        jnp.zeros((kv_heads, group_size, tokens), jnp.float32),
        jnp.zeros((kv_heads, group_size, tokens, HEAD_DIM), jnp.float32),
    )
    running_max, weight_sum, accumulated = lax.fori_loop(
        first_chunk, last_chunk + 1, visit_chunk, start_state
    )
    attended = (
        (accumulated / weight_sum[..., None])
        .transpose(2, 0, 1, 3)
        .reshape(tokens, query_heads * HEAD_DIM)
    )
    attended = attended.astype(jnp.bfloat16)
    partial_out = jnp.dot(attended, w_out, preferred_element_type=jnp.float32)
    attn_mixed = lax.psum(partial_out.astype(jnp.bfloat16), TP_AXES).astype(jnp.float32)
    residual = (hidden.astype(jnp.float32) + attn_mixed).astype(jnp.bfloat16)
    normed_moe = normalize(residual, norm_moe).astype(jnp.bfloat16)
    route_count = routes.shape[1]
    slots_dev = w_gate.shape[0]
    seq_count = lax.axis_size(SUB_AXES)
    slot_total = slots_dev * seq_count
    copies = slot_total // EXPERTS
    block_rows = tokens // copies
    capacity = 2 * block_rows * route_count // EXPERTS
    copy_of = (jnp.arange(tokens, dtype=jnp.int32) // block_rows)[:, None]
    slot_of = routes + EXPERTS * copy_of
    flat_expert = routes.reshape(copies, block_rows * route_count)
    onehot = (
        flat_expert[:, :, None] == jnp.arange(EXPERTS, dtype=jnp.int32)[None, None, :]
    ).astype(jnp.int32)
    before = jnp.cumsum(onehot, axis=1) - onehot
    slot_rank = jnp.sum(before * onehot, axis=2).reshape(tokens, route_count)
    target = slot_of * capacity + slot_rank
    token_ids = jnp.broadcast_to(
        jnp.arange(tokens, dtype=jnp.int32)[:, None], (tokens, route_count)
    )
    source = (
        jnp.full((slot_total * capacity,), tokens, jnp.int32)
        .at[target.reshape(-1)]
        .set(token_ids.reshape(-1))
    )
    half = capacity // 2
    core = lax.axis_index("tc")
    swap = [(0, 1), (1, 0)]
    own_source = lax.dynamic_slice_in_dim(
        source.reshape(seq_count, slots_dev, capacity), core * half, half, axis=2
    )
    padded_rows = jnp.concatenate([normed_moe, jnp.zeros((1, normed_moe.shape[1]), jnp.bfloat16)])
    outbound = padded_rows[own_source]
    arrived_own = lax.all_to_all(outbound, SUB_AXES, split_axis=0, concat_axis=0, tiled=True)
    arrived_other = lax.ppermute(arrived_own, "tc", swap)
    arrived = jnp.concatenate([arrived_own, arrived_other], axis=2)
    gate_val = jnp.einsum("jsrd,sdf->jsrf", arrived, w_gate, preferred_element_type=jnp.float32)
    up_val = jnp.einsum("jsrd,sdf->jsrf", arrived, w_up, preferred_element_type=jnp.float32)
    activated = (jax.nn.silu(gate_val) * up_val).astype(jnp.bfloat16)
    group_part = jnp.einsum("jsrf,sfd->jsrd", activated, w_down, preferred_element_type=jnp.float32)
    result = group_part.astype(jnp.bfloat16)
    sibling_part = lax.ppermute(result[:, :, half:], "tc", swap)
    pair_sum = (result[:, :, :half].astype(jnp.float32) + sibling_part.astype(jnp.float32)).astype(
        jnp.bfloat16
    )
    returned = lax.all_to_all(pair_sum, SUB_AXES, split_axis=0, concat_axis=0, tiled=True).reshape(
        slot_total * half, model_width
    )
    returned = jnp.concatenate([returned, jnp.zeros((1, model_width), jnp.bfloat16)])
    own_route = (slot_rank // half) == core
    local_target = jnp.where(own_route, slot_of * half + slot_rank - core * half, slot_total * half)
    picked = returned[local_target]
    combined = jnp.einsum(
        "tk,tkd->td",
        gates,
        picked,
        preferred_element_type=jnp.float32,
        precision=lax.Precision.HIGHEST,
    )
    expert_sum = lax.psum(combined.astype(jnp.bfloat16), TP_AXES).astype(jnp.float32)
    hidden_out = (residual.astype(jnp.float32) + expert_sum).astype(jnp.bfloat16)
    return (hidden_out, kv_cache)


def solution(mesh):
    seq_size, tp_size = mesh.devices.shape
    side = round(seq_size ** (1 / 3))
    sub_mesh = Mesh(
        mesh.devices.reshape(side, side, seq_size // side // side, tp_size // 2, 2), SUB_AXES + TP_AXES
    )
    return jax.shard_map(
        per_device,
        mesh=sub_mesh,
        in_specs=(
            P(SUB_AXES, None),
            P(),
            P(SUB_AXES, None),
            P(SUB_AXES, None),
            P(),
            P(),
            P(None, TP_AXES),
            P(None, TP_AXES),
            P(None, TP_AXES),
            P(TP_AXES, None),
            P(SUB_AXES, None, TP_AXES),
            P(SUB_AXES, None, TP_AXES),
            P(SUB_AXES, TP_AXES, None),
        ),
        out_specs=(P(SUB_AXES, None), P(SUB_AXES, None, TP_AXES)),
        check_vma=False,
    )
```

```python
import jax
import jax.numpy as jnp
from jax import lax
from jax.sharding import Mesh
from jax.sharding import PartitionSpec as P

HEAD_DIM = 64
EXPERTS = 32
SEG_VALUES = 8
KEY_CHUNK = 1024

EPS = 1e-06
SCORE_SCALE = 0.015625
SUB_AXES = ("sy", "sz", "sx")
TP_AXES = ("tz", "tc")


def normalize(values, gain):
    widened = values.astype(jnp.float32)
    return (
        widened
        * lax.rsqrt(jnp.mean(widened * widened, axis=-1, keepdims=True) + EPS)
        * gain.astype(jnp.float32)
    )


def rotary(tensor, positions):
    half_dim = tensor.shape[-1] // 2
    frequencies = 10000.0 ** (-jnp.arange(half_dim, dtype=jnp.float32) * 2.0 / tensor.shape[-1])
    angles = positions.astype(jnp.float32)[:, None] * frequencies[None, :]
    cosine = jnp.cos(angles)[:, None, :]
    sine_part = jnp.sin(angles)[:, None, :]
    lower_half = tensor[..., :half_dim]
    upper_half = tensor[..., half_dim:]
    return jnp.concatenate(
        [
            lower_half * cosine - upper_half * sine_part,
            upper_half * cosine + lower_half * sine_part,
        ],
        axis=-1,
    )


def tp_sum(partial):
    swap = [(0, 1), (1, 0)]
    pair = partial.astype(jnp.float32) + lax.ppermute(partial, "tc", swap).astype(jnp.float32)
    pair = pair.astype(jnp.bfloat16)
    return pair.astype(jnp.float32) + lax.ppermute(pair, "tz", swap).astype(jnp.float32)


def per_device(
    hidden,
    segment_ids,
    routes,
    gates,
    norm_attn,
    norm_moe,
    w_query,
    w_key,
    w_value,
    w_out,
    w_gate,
    w_up,
    w_down,
):
    tokens = hidden.shape[0]
    model_width = hidden.shape[1]
    total_tokens = segment_ids.shape[0]
    first_row = lax.axis_index(SUB_AXES) * tokens
    own_segs = lax.dynamic_slice_in_dim(segment_ids, first_row, tokens)
    seg_starts = jnp.sum(
        (segment_ids[None, :] < jnp.arange(SEG_VALUES, dtype=jnp.int32)[:, None]).astype(jnp.int32),
        axis=1,
    )
    query_index = first_row + jnp.arange(tokens, dtype=jnp.int32)
    positions = query_index - seg_starts[own_segs]
    normed = normalize(hidden, norm_attn).astype(jnp.bfloat16)
    query_heads = w_query.shape[1] // HEAD_DIM
    kv_heads = w_key.shape[1] // HEAD_DIM
    group_size = query_heads // kv_heads
    queries = jnp.dot(normed, w_query, preferred_element_type=jnp.float32).reshape(
        tokens, query_heads, HEAD_DIM
    )
    queries = (
        rotary(queries, positions)
        .astype(jnp.bfloat16)
        .reshape(tokens, kv_heads, group_size, HEAD_DIM)
        .transpose(1, 2, 0, 3)
    )
    key_raw = jnp.dot(normed, w_key, preferred_element_type=jnp.float32).reshape(
        tokens, kv_heads, HEAD_DIM
    )
    value_proj = jnp.dot(normed, w_value, preferred_element_type=jnp.float32).astype(jnp.bfloat16)
    kv_cache = jnp.stack(
        [key_raw.reshape(tokens, kv_heads * HEAD_DIM).astype(jnp.bfloat16), value_proj], axis=1
    )
    key_rot = rotary(key_raw, positions).astype(jnp.bfloat16)
    kv_width = kv_heads * HEAD_DIM
    joined = jnp.concatenate([key_rot.reshape(tokens, kv_width), value_proj], axis=1)
    for axis_name in SUB_AXES[::-1]:
        joined = lax.all_gather(joined, axis_name, axis=0, tiled=True)
    keys_all = joined[:, :kv_width].reshape(total_tokens, kv_heads, HEAD_DIM).transpose(1, 0, 2)
    values_all = joined[:, kv_width:].reshape(total_tokens, kv_heads, HEAD_DIM).transpose(1, 0, 2)
    last_query = first_row + tokens - 1
    lowest_seg = own_segs[0]
    chunk_ends = segment_ids[KEY_CHUNK - 1 :: KEY_CHUNK]
    first_chunk = jnp.sum((chunk_ends < lowest_seg).astype(jnp.int32))
    last_chunk = last_query // KEY_CHUNK

    def visit_chunk(chunk, carried):
        running_max, weight_sum, accumulated = carried
        key_start = chunk * KEY_CHUNK
        key_rows = lax.dynamic_slice_in_dim(keys_all, key_start, KEY_CHUNK, axis=1)
        value_rows = lax.dynamic_slice_in_dim(values_all, key_start, KEY_CHUNK, axis=1)
        key_segs = lax.dynamic_slice_in_dim(segment_ids, key_start, KEY_CHUNK)
        scores = (
            jnp.einsum("kgtd,ksd->kgts", queries, key_rows, preferred_element_type=jnp.float32)
            * SCORE_SCALE
        )
        key_index = key_start + jnp.arange(KEY_CHUNK, dtype=jnp.int32)
        allowed = (own_segs[:, None] == key_segs[None, :]) & (
            query_index[:, None] >= key_index[None, :]
        )
        masked = jnp.where(allowed, scores, -1e30)
        new_max = jnp.maximum(running_max, jnp.max(masked, axis=-1))
        weights = jnp.where(allowed, jnp.exp(masked - new_max[..., None]), 0.0)
        factor = jnp.exp(running_max - new_max)
        weight_sum = weight_sum * factor + jnp.sum(weights, axis=-1)
        accumulated = accumulated * factor[..., None] + jnp.einsum(
            "kgts,ksd->kgtd",
            weights.astype(jnp.bfloat16),
            value_rows,
            preferred_element_type=jnp.float32,
        )
        return (new_max, weight_sum, accumulated)

    start_state = (
        jnp.full((kv_heads, group_size, tokens), -1e30, jnp.float32),
        jnp.zeros((kv_heads, group_size, tokens), jnp.float32),
        jnp.zeros((kv_heads, group_size, tokens, HEAD_DIM), jnp.float32),
    )
    running_max, weight_sum, accumulated = lax.fori_loop(
        first_chunk, last_chunk + 1, visit_chunk, start_state
    )
    attended = (
        (accumulated / weight_sum[..., None])
        .transpose(2, 0, 1, 3)
        .reshape(tokens, query_heads * HEAD_DIM)
    )
    attended = attended.astype(jnp.bfloat16)
    partial_out = jnp.dot(attended, w_out, preferred_element_type=jnp.float32)
    attn_mixed = tp_sum(partial_out.astype(jnp.bfloat16))
    residual = (hidden.astype(jnp.float32) + attn_mixed).astype(jnp.bfloat16)
    normed_moe = normalize(residual, norm_moe).astype(jnp.bfloat16)
    route_count = routes.shape[1]
    slots_dev = w_gate.shape[0]
    seq_count = lax.axis_size(SUB_AXES)
    slot_total = slots_dev * seq_count
    copies = slot_total // EXPERTS
    block_rows = tokens // copies
    capacity = 2 * block_rows * route_count // EXPERTS
    copy_of = (jnp.arange(tokens, dtype=jnp.int32) // block_rows)[:, None]
    slot_of = routes + EXPERTS * copy_of
    flat_expert = routes.reshape(copies, block_rows * route_count)
    onehot = (
        flat_expert[:, :, None] == jnp.arange(EXPERTS, dtype=jnp.int32)[None, None, :]
    ).astype(jnp.int32)
    before = jnp.cumsum(onehot, axis=1) - onehot
    slot_rank = jnp.sum(before * onehot, axis=2).reshape(tokens, route_count)
    target = slot_of * capacity + slot_rank
    token_ids = jnp.broadcast_to(
        jnp.arange(tokens, dtype=jnp.int32)[:, None], (tokens, route_count)
    )
    source = (
        jnp.full((slot_total * capacity,), tokens, jnp.int32)
        .at[target.reshape(-1)]
        .set(token_ids.reshape(-1))
    )
    half = capacity // 2
    core = lax.axis_index("tc")
    swap = [(0, 1), (1, 0)]
    own_source = lax.dynamic_slice_in_dim(
        source.reshape(seq_count, slots_dev, capacity), core * half, half, axis=2
    )
    padded_rows = jnp.concatenate([normed_moe, jnp.zeros((1, normed_moe.shape[1]), jnp.bfloat16)])
    outbound = padded_rows[own_source]
    arrived_own = lax.all_to_all(outbound, SUB_AXES, split_axis=0, concat_axis=0, tiled=True)
    arrived_other = lax.ppermute(arrived_own, "tc", swap)
    arrived = jnp.concatenate([arrived_own, arrived_other], axis=2)
    gate_val = jnp.einsum("jsrd,sdf->jsrf", arrived, w_gate, preferred_element_type=jnp.float32)
    up_val = jnp.einsum("jsrd,sdf->jsrf", arrived, w_up, preferred_element_type=jnp.float32)
    activated = (jax.nn.silu(gate_val) * up_val).astype(jnp.bfloat16)
    group_part = jnp.einsum("jsrf,sfd->jsrd", activated, w_down, preferred_element_type=jnp.float32)
    result = group_part.astype(jnp.bfloat16)
    sibling_part = lax.ppermute(result[:, :, half:], "tc", swap)
    pair_sum = (result[:, :, :half].astype(jnp.float32) + sibling_part.astype(jnp.float32)).astype(
        jnp.bfloat16
    )
    returned = lax.all_to_all(pair_sum, SUB_AXES, split_axis=0, concat_axis=0, tiled=True).reshape(
        slot_total * half, model_width
    )
    returned = jnp.concatenate([returned, jnp.zeros((1, model_width), jnp.bfloat16)])
    own_route = (slot_rank // half) == core
    local_target = jnp.where(own_route, slot_of * half + slot_rank - core * half, slot_total * half)
    picked = returned[local_target]
    combined = jnp.einsum(
        "tk,tkd->td",
        gates,
        picked,
        preferred_element_type=jnp.float32,
        precision=lax.Precision.HIGHEST,
    )
    expert_sum = tp_sum(combined.astype(jnp.bfloat16))
    hidden_out = (residual.astype(jnp.float32) + expert_sum).astype(jnp.bfloat16)
    return (hidden_out, kv_cache)


def solution(mesh):
    seq_size, tp_size = mesh.devices.shape
    side = round(seq_size ** (1 / 3))
    sub_mesh = Mesh(
        mesh.devices.reshape(side, side, seq_size // side // side, tp_size // 2, 2), SUB_AXES + TP_AXES
    )
    return jax.shard_map(
        per_device,
        mesh=sub_mesh,
        in_specs=(
            P(SUB_AXES, None),
            P(),
            P(SUB_AXES, None),
            P(SUB_AXES, None),
            P(),
            P(),
            P(None, TP_AXES),
            P(None, TP_AXES),
            P(None, TP_AXES),
            P(TP_AXES, None),
            P(SUB_AXES, None, TP_AXES),
            P(SUB_AXES, None, TP_AXES),
            P(SUB_AXES, TP_AXES, None),
        ),
        out_specs=(P(SUB_AXES, None), P(SUB_AXES, None, TP_AXES)),
        check_vma=False,
    )
```

```python
import jax
import jax.numpy as jnp
from jax import lax
from jax.experimental import pallas as pl
from jax.experimental.pallas import tpu as pltpu
from jax.sharding import Mesh
from jax.sharding import PartitionSpec as P

HEAD_DIM = 64
EXPERTS = 32
SEG_VALUES = 8
KEY_CHUNK = 1024

EPS = 1e-06
SCORE_SCALE = 0.015625
SUB_AXES = ("sy", "sz", "sx")
TP_AXES = ("tz", "tc")


def normalize(values, gain):
    widened = values.astype(jnp.float32)
    return (
        widened
        * lax.rsqrt(jnp.mean(widened * widened, axis=-1, keepdims=True) + EPS)
        * gain.astype(jnp.float32)
    )


def rotary(tensor, positions):
    half_dim = tensor.shape[-1] // 2
    frequencies = 10000.0 ** (-jnp.arange(half_dim, dtype=jnp.float32) * 2.0 / tensor.shape[-1])
    angles = positions.astype(jnp.float32)[:, None] * frequencies[None, :]
    cosine = jnp.cos(angles)[:, None, :]
    sine_part = jnp.sin(angles)[:, None, :]
    lower_half = tensor[..., :half_dim]
    upper_half = tensor[..., half_dim:]
    return jnp.concatenate(
        [
            lower_half * cosine - upper_half * sine_part,
            upper_half * cosine + lower_half * sine_part,
        ],
        axis=-1,
    )


def attention_kernel(bounds_ref, q_ref, k_ref, v_ref, kseg_ref, qseg_ref, qidx_ref, o_ref, m_sc, l_sc, acc_sc):
    step = pl.program_id(0)
    kv_heads, group_size = q_ref.shape[0], q_ref.shape[1]

    @pl.when(step == 0)
    def _():
        m_sc[...] = jnp.full(m_sc.shape, -1e30, jnp.float32)
        l_sc[...] = jnp.zeros(l_sc.shape, jnp.float32)
        acc_sc[...] = jnp.zeros(acc_sc.shape, jnp.float32)

    chunk = bounds_ref[0] + step

    @pl.when(chunk <= bounds_ref[1])
    def _():
        key_index = chunk * KEY_CHUNK + lax.broadcasted_iota(jnp.int32, (1, KEY_CHUNK), 1)
        allowed = (qseg_ref[...] == kseg_ref[0]) & (qidx_ref[...] >= key_index)
        for head in range(kv_heads):
            key_rows = k_ref[head]
            value_rows = v_ref[head]
            for member in range(group_size):
                slot = head * group_size + member
                scores = (
                    lax.dot_general(
                        q_ref[head, member],
                        key_rows,
                        (((1,), (1,)), ((), ())),
                        preferred_element_type=jnp.float32,
                    )
                    * SCORE_SCALE
                )
                masked = jnp.where(allowed, scores, -1e30)
                running_max = m_sc[slot]
                new_max = jnp.maximum(running_max, jnp.max(masked, axis=-1, keepdims=True))
                weights = jnp.where(allowed, jnp.exp(masked - new_max), 0.0)
                factor = jnp.exp(running_max - new_max)
                l_sc[slot] = l_sc[slot] * factor + jnp.sum(weights, axis=-1, keepdims=True)
                acc_sc[slot] = acc_sc[slot] * factor + jnp.dot(
                    weights.astype(jnp.bfloat16), value_rows, preferred_element_type=jnp.float32
                )
                m_sc[slot] = new_max

    @pl.when(step == pl.num_programs(0) - 1)
    def _():
        o_ref[...] = acc_sc[...] / l_sc[...]


def chunk_attention(queries, keys_all, values_all, segment_ids, own_segs, query_index, first_chunk, last_chunk):
    kv_heads, group_size, tokens, head_dim = queries.shape
    total = keys_all.shape[1]
    chunks = total // KEY_CHUNK
    bounds = jnp.stack([first_chunk, last_chunk]).astype(jnp.int32)

    def chunk_map(step, bounds_ref):
        return (0, jnp.minimum(bounds_ref[0] + step, bounds_ref[1]), 0)

    def seg_map(step, bounds_ref):
        return (jnp.minimum(bounds_ref[0] + step, bounds_ref[1]), 0, 0)

    def whole(step, bounds_ref):
        return (0, 0, 0, 0)

    def whole2(step, bounds_ref):
        return (0, 0)

    def whole3(step, bounds_ref):
        return (0, 0, 0)

    spec = pltpu.PrefetchScalarGridSpec(
        num_scalar_prefetch=1,
        grid=(chunks,),
        in_specs=[
            pl.BlockSpec((kv_heads, group_size, tokens, head_dim), whole),
            pl.BlockSpec((kv_heads, KEY_CHUNK, head_dim), chunk_map),
            pl.BlockSpec((kv_heads, KEY_CHUNK, head_dim), chunk_map),
            pl.BlockSpec((1, 1, KEY_CHUNK), seg_map),
            pl.BlockSpec((tokens, 1), whole2),
            pl.BlockSpec((tokens, 1), whole2),
        ],
        out_specs=pl.BlockSpec((kv_heads * group_size, tokens, head_dim), whole3),
        scratch_shapes=[
            pltpu.VMEM((kv_heads * group_size, tokens, 1), jnp.float32),
            pltpu.VMEM((kv_heads * group_size, tokens, 1), jnp.float32),
            pltpu.VMEM((kv_heads * group_size, tokens, head_dim), jnp.float32),
        ],
    )
    out = pl.pallas_call(
        attention_kernel,
        grid_spec=spec,
        out_shape=jax.ShapeDtypeStruct((kv_heads * group_size, tokens, head_dim), jnp.float32),
        compiler_params=pltpu.CompilerParams(dimension_semantics=("arbitrary",)),
    )(
        bounds,
        queries,
        keys_all,
        values_all,
        segment_ids.reshape(chunks, 1, KEY_CHUNK),
        own_segs.reshape(tokens, 1),
        query_index.reshape(tokens, 1),
    )
    return out.reshape(kv_heads, group_size, tokens, head_dim)


def tp_sum(partial):
    swap = [(0, 1), (1, 0)]
    pair = partial.astype(jnp.float32) + lax.ppermute(partial, "tc", swap).astype(jnp.float32)
    pair = pair.astype(jnp.bfloat16)
    return pair.astype(jnp.float32) + lax.ppermute(pair, "tz", swap).astype(jnp.float32)


def per_device(
    hidden,
    segment_ids,
    routes,
    gates,
    norm_attn,
    norm_moe,
    w_query,
    w_key,
    w_value,
    w_out,
    w_gate,
    w_up,
    w_down,
):
    tokens = hidden.shape[0]
    model_width = hidden.shape[1]
    total_tokens = segment_ids.shape[0]
    first_row = lax.axis_index(SUB_AXES) * tokens
    own_segs = lax.dynamic_slice_in_dim(segment_ids, first_row, tokens)
    seg_starts = jnp.sum(
        (segment_ids[None, :] < jnp.arange(SEG_VALUES, dtype=jnp.int32)[:, None]).astype(jnp.int32),
        axis=1,
    )
    query_index = first_row + jnp.arange(tokens, dtype=jnp.int32)
    positions = query_index - seg_starts[own_segs]
    normed = normalize(hidden, norm_attn).astype(jnp.bfloat16)
    query_heads = w_query.shape[1] // HEAD_DIM
    kv_heads = w_key.shape[1] // HEAD_DIM
    group_size = query_heads // kv_heads
    queries = jnp.dot(normed, w_query, preferred_element_type=jnp.float32).reshape(
        tokens, query_heads, HEAD_DIM
    )
    queries = (
        rotary(queries, positions)
        .astype(jnp.bfloat16)
        .reshape(tokens, kv_heads, group_size, HEAD_DIM)
        .transpose(1, 2, 0, 3)
    )
    key_raw = jnp.dot(normed, w_key, preferred_element_type=jnp.float32).reshape(
        tokens, kv_heads, HEAD_DIM
    )
    value_proj = jnp.dot(normed, w_value, preferred_element_type=jnp.float32).astype(jnp.bfloat16)
    kv_cache = jnp.stack(
        [key_raw.reshape(tokens, kv_heads * HEAD_DIM).astype(jnp.bfloat16), value_proj], axis=1
    )
    key_rot = rotary(key_raw, positions).astype(jnp.bfloat16)
    kv_width = kv_heads * HEAD_DIM
    joined = jnp.concatenate([key_rot.reshape(tokens, kv_width), value_proj], axis=1)
    for axis_name in SUB_AXES[::-1]:
        joined = lax.all_gather(joined, axis_name, axis=0, tiled=True)
    keys_all = joined[:, :kv_width].reshape(total_tokens, kv_heads, HEAD_DIM).transpose(1, 0, 2)
    values_all = joined[:, kv_width:].reshape(total_tokens, kv_heads, HEAD_DIM).transpose(1, 0, 2)
    last_query = first_row + tokens - 1
    lowest_seg = own_segs[0]
    chunk_ends = segment_ids[KEY_CHUNK - 1 :: KEY_CHUNK]
    first_chunk = jnp.sum((chunk_ends < lowest_seg).astype(jnp.int32))
    last_chunk = last_query // KEY_CHUNK

    attended = chunk_attention(
        queries, keys_all, values_all, segment_ids, own_segs, query_index, first_chunk, last_chunk
    )
    attended = (
        attended.transpose(2, 0, 1, 3)
        .reshape(tokens, query_heads * HEAD_DIM)
    )
    attended = attended.astype(jnp.bfloat16)
    partial_out = jnp.dot(attended, w_out, preferred_element_type=jnp.float32)
    attn_mixed = tp_sum(partial_out.astype(jnp.bfloat16))
    residual = (hidden.astype(jnp.float32) + attn_mixed).astype(jnp.bfloat16)
    normed_moe = normalize(residual, norm_moe).astype(jnp.bfloat16)
    route_count = routes.shape[1]
    slots_dev = w_gate.shape[0]
    seq_count = lax.axis_size(SUB_AXES)
    slot_total = slots_dev * seq_count
    copies = slot_total // EXPERTS
    block_rows = tokens // copies
    capacity = 2 * block_rows * route_count // EXPERTS
    copy_of = (jnp.arange(tokens, dtype=jnp.int32) // block_rows)[:, None]
    slot_of = routes + EXPERTS * copy_of
    flat_expert = routes.reshape(copies, block_rows * route_count)
    onehot = (
        flat_expert[:, :, None] == jnp.arange(EXPERTS, dtype=jnp.int32)[None, None, :]
    ).astype(jnp.int32)
    before = jnp.cumsum(onehot, axis=1) - onehot
    slot_rank = jnp.sum(before * onehot, axis=2).reshape(tokens, route_count)
    target = slot_of * capacity + slot_rank
    token_ids = jnp.broadcast_to(
        jnp.arange(tokens, dtype=jnp.int32)[:, None], (tokens, route_count)
    )
    source = (
        jnp.full((slot_total * capacity,), tokens, jnp.int32)
        .at[target.reshape(-1)]
        .set(token_ids.reshape(-1))
    )
    half = capacity // 2
    core = lax.axis_index("tc")
    swap = [(0, 1), (1, 0)]
    own_source = lax.dynamic_slice_in_dim(
        source.reshape(seq_count, slots_dev, capacity), core * half, half, axis=2
    )
    padded_rows = jnp.concatenate([normed_moe, jnp.zeros((1, normed_moe.shape[1]), jnp.bfloat16)])
    outbound = padded_rows[own_source]
    arrived_own = lax.all_to_all(outbound, SUB_AXES, split_axis=0, concat_axis=0, tiled=True)
    arrived_other = lax.ppermute(arrived_own, "tc", swap)
    arrived = jnp.concatenate([arrived_own, arrived_other], axis=2)
    gate_val = jnp.einsum("jsrd,sdf->jsrf", arrived, w_gate, preferred_element_type=jnp.float32)
    up_val = jnp.einsum("jsrd,sdf->jsrf", arrived, w_up, preferred_element_type=jnp.float32)
    activated = (jax.nn.silu(gate_val) * up_val).astype(jnp.bfloat16)
    group_part = jnp.einsum("jsrf,sfd->jsrd", activated, w_down, preferred_element_type=jnp.float32)
    result = group_part.astype(jnp.bfloat16)
    sibling_part = lax.ppermute(result[:, :, half:], "tc", swap)
    pair_sum = (result[:, :, :half].astype(jnp.float32) + sibling_part.astype(jnp.float32)).astype(
        jnp.bfloat16
    )
    returned = lax.all_to_all(pair_sum, SUB_AXES, split_axis=0, concat_axis=0, tiled=True).reshape(
        slot_total * half, model_width
    )
    returned = jnp.concatenate([returned, jnp.zeros((1, model_width), jnp.bfloat16)])
    own_route = (slot_rank // half) == core
    local_target = jnp.where(own_route, slot_of * half + slot_rank - core * half, slot_total * half)
    picked = returned[local_target]
    combined = jnp.einsum(
        "tk,tkd->td",
        gates,
        picked,
        preferred_element_type=jnp.float32,
        precision=lax.Precision.HIGHEST,
    )
    expert_sum = tp_sum(combined.astype(jnp.bfloat16))
    hidden_out = (residual.astype(jnp.float32) + expert_sum).astype(jnp.bfloat16)
    return (hidden_out, kv_cache)


def solution(mesh):
    seq_size, tp_size = mesh.devices.shape
    side = round(seq_size ** (1 / 3))
    sub_mesh = Mesh(
        mesh.devices.reshape(side, side, seq_size // side // side, tp_size // 2, 2), SUB_AXES + TP_AXES
    )
    return jax.shard_map(
        per_device,
        mesh=sub_mesh,
        in_specs=(
            P(SUB_AXES, None),
            P(),
            P(SUB_AXES, None),
            P(SUB_AXES, None),
            P(),
            P(),
            P(None, TP_AXES),
            P(None, TP_AXES),
            P(None, TP_AXES),
            P(TP_AXES, None),
            P(SUB_AXES, None, TP_AXES),
            P(SUB_AXES, None, TP_AXES),
            P(SUB_AXES, TP_AXES, None),
        ),
        out_specs=(P(SUB_AXES, None), P(SUB_AXES, None, TP_AXES)),
        check_vma=False,
    )
```

```python
import jax
import jax.numpy as jnp
from jax import lax
from jax.experimental import pallas as pl
from jax.experimental.pallas import tpu as pltpu
from jax.sharding import Mesh
from jax.sharding import PartitionSpec as P

HEAD_DIM = 64
EXPERTS = 32
SEG_VALUES = 8
KEY_CHUNK = 1024

EPS = 1e-06
SCORE_SCALE = 0.015625
SUB_AXES = ("sy", "sz", "sx")
TP_AXES = ("tz", "tc")


def normalize(values, gain):
    widened = values.astype(jnp.float32)
    return (
        widened
        * lax.rsqrt(jnp.mean(widened * widened, axis=-1, keepdims=True) + EPS)
        * gain.astype(jnp.float32)
    )


def rotary(tensor, positions):
    half_dim = tensor.shape[-1] // 2
    frequencies = 10000.0 ** (-jnp.arange(half_dim, dtype=jnp.float32) * 2.0 / tensor.shape[-1])
    angles = positions.astype(jnp.float32)[:, None] * frequencies[None, :]
    cosine = jnp.cos(angles)[:, None, :]
    sine_part = jnp.sin(angles)[:, None, :]
    lower_half = tensor[..., :half_dim]
    upper_half = tensor[..., half_dim:]
    return jnp.concatenate(
        [
            lower_half * cosine - upper_half * sine_part,
            upper_half * cosine + lower_half * sine_part,
        ],
        axis=-1,
    )


def attention_kernel(bounds_ref, q_ref, k_ref, v_ref, kseg_ref, qseg_ref, qidx_ref, o_ref, m_sc, l_sc, acc_sc):
    step = pl.program_id(0)
    kv_heads, group_size = q_ref.shape[0], q_ref.shape[1]

    @pl.when(step == 0)
    def _():
        m_sc[...] = jnp.full(m_sc.shape, -1e30, jnp.float32)
        l_sc[...] = jnp.zeros(l_sc.shape, jnp.float32)
        acc_sc[...] = jnp.zeros(acc_sc.shape, jnp.float32)

    chunk = bounds_ref[0] + step

    @pl.when(chunk <= bounds_ref[1])
    def _():
        key_index = chunk * KEY_CHUNK + lax.broadcasted_iota(jnp.int32, (1, KEY_CHUNK), 1)
        allowed = (qseg_ref[...] == kseg_ref[0]) & (qidx_ref[...] >= key_index)
        key_rows = k_ref[...]
        value_rows = v_ref[...]
        for head in range(kv_heads):
            for member in range(group_size):
                slot = head * group_size + member
                scores = (
                    lax.dot_general(
                        q_ref[head, member],
                        key_rows,
                        (((1,), (1,)), ((), ())),
                        preferred_element_type=jnp.float32,
                    )
                    * SCORE_SCALE
                )
                masked = jnp.where(allowed, scores, -1e30)
                running_max = m_sc[slot]
                new_max = jnp.maximum(running_max, jnp.max(masked, axis=-1, keepdims=True))
                weights = jnp.where(allowed, jnp.exp(masked - new_max), 0.0)
                factor = jnp.exp(running_max - new_max)
                l_sc[slot] = l_sc[slot] * factor + jnp.sum(weights, axis=-1, keepdims=True)
                acc_sc[slot] = acc_sc[slot] * factor + jnp.dot(
                    weights.astype(jnp.bfloat16), value_rows, preferred_element_type=jnp.float32
                )
                m_sc[slot] = new_max

    @pl.when(step == pl.num_programs(0) - 1)
    def _():
        o_ref[...] = acc_sc[...] / l_sc[...]


def chunk_attention(queries, joined, segment_ids, own_segs, query_index, first_chunk, last_chunk):
    kv_heads, group_size, tokens, head_dim = queries.shape
    total, both_width = joined.shape
    kv_width = both_width // 2
    chunks = total // KEY_CHUNK
    head_mask = jnp.eye(kv_heads, dtype=jnp.bool_)[:, None, None, :, None]
    padded_queries = jnp.where(head_mask, queries[:, :, :, None, :], jnp.zeros((), queries.dtype)).reshape(
        kv_heads, group_size, tokens, kv_width
    )
    bounds = jnp.stack([first_chunk, last_chunk]).astype(jnp.int32)

    def key_map(step, bounds_ref):
        return (jnp.minimum(bounds_ref[0] + step, bounds_ref[1]), 0)

    def value_map(step, bounds_ref):
        return (jnp.minimum(bounds_ref[0] + step, bounds_ref[1]), 1)

    def seg_map(step, bounds_ref):
        return (jnp.minimum(bounds_ref[0] + step, bounds_ref[1]), 0, 0)

    def whole(step, bounds_ref):
        return (0, 0, 0, 0)

    def whole2(step, bounds_ref):
        return (0, 0)

    def whole3(step, bounds_ref):
        return (0, 0, 0)

    spec = pltpu.PrefetchScalarGridSpec(
        num_scalar_prefetch=1,
        grid=(chunks,),
        in_specs=[
            pl.BlockSpec((kv_heads, group_size, tokens, kv_width), whole),
            pl.BlockSpec((KEY_CHUNK, kv_width), key_map),
            pl.BlockSpec((KEY_CHUNK, kv_width), value_map),
            pl.BlockSpec((1, 1, KEY_CHUNK), seg_map),
            pl.BlockSpec((tokens, 1), whole2),
            pl.BlockSpec((tokens, 1), whole2),
        ],
        out_specs=pl.BlockSpec((kv_heads * group_size, tokens, kv_width), whole3),
        scratch_shapes=[
            pltpu.VMEM((kv_heads * group_size, tokens, 1), jnp.float32),
            pltpu.VMEM((kv_heads * group_size, tokens, 1), jnp.float32),
            pltpu.VMEM((kv_heads * group_size, tokens, kv_width), jnp.float32),
        ],
    )
    out = pl.pallas_call(
        attention_kernel,
        grid_spec=spec,
        out_shape=jax.ShapeDtypeStruct((kv_heads * group_size, tokens, kv_width), jnp.float32),
        compiler_params=pltpu.CompilerParams(dimension_semantics=("arbitrary",)),
    )(
        bounds,
        padded_queries,
        joined,
        joined,
        segment_ids.reshape(chunks, 1, KEY_CHUNK),
        own_segs.reshape(tokens, 1),
        query_index.reshape(tokens, 1),
    )
    out = out.reshape(kv_heads, group_size, tokens, kv_heads, head_dim)
    return jnp.stack([out[head, :, :, head] for head in range(kv_heads)])


def tp_sum(partial):
    swap = [(0, 1), (1, 0)]
    pair = partial.astype(jnp.float32) + lax.ppermute(partial, "tc", swap).astype(jnp.float32)
    pair = pair.astype(jnp.bfloat16)
    return pair.astype(jnp.float32) + lax.ppermute(pair, "tz", swap).astype(jnp.float32)


def per_device(
    hidden,
    segment_ids,
    routes,
    gates,
    norm_attn,
    norm_moe,
    w_query,
    w_key,
    w_value,
    w_out,
    w_gate,
    w_up,
    w_down,
):
    tokens = hidden.shape[0]
    model_width = hidden.shape[1]
    total_tokens = segment_ids.shape[0]
    first_row = lax.axis_index(SUB_AXES) * tokens
    own_segs = lax.dynamic_slice_in_dim(segment_ids, first_row, tokens)
    seg_starts = jnp.sum(
        (segment_ids[None, :] < jnp.arange(SEG_VALUES, dtype=jnp.int32)[:, None]).astype(jnp.int32),
        axis=1,
    )
    query_index = first_row + jnp.arange(tokens, dtype=jnp.int32)
    positions = query_index - seg_starts[own_segs]
    normed = normalize(hidden, norm_attn).astype(jnp.bfloat16)
    query_heads = w_query.shape[1] // HEAD_DIM
    kv_heads = w_key.shape[1] // HEAD_DIM
    group_size = query_heads // kv_heads
    queries = jnp.dot(normed, w_query, preferred_element_type=jnp.float32).reshape(
        tokens, query_heads, HEAD_DIM
    )
    queries = (
        rotary(queries, positions)
        .astype(jnp.bfloat16)
        .reshape(tokens, kv_heads, group_size, HEAD_DIM)
        .transpose(1, 2, 0, 3)
    )
    key_raw = jnp.dot(normed, w_key, preferred_element_type=jnp.float32).reshape(
        tokens, kv_heads, HEAD_DIM
    )
    value_proj = jnp.dot(normed, w_value, preferred_element_type=jnp.float32).astype(jnp.bfloat16)
    kv_cache = jnp.stack(
        [key_raw.reshape(tokens, kv_heads * HEAD_DIM).astype(jnp.bfloat16), value_proj], axis=1
    )
    key_rot = rotary(key_raw, positions).astype(jnp.bfloat16)
    kv_width = kv_heads * HEAD_DIM
    joined = jnp.concatenate([key_rot.reshape(tokens, kv_width), value_proj], axis=1)
    for axis_name in SUB_AXES[::-1]:
        joined = lax.all_gather(joined, axis_name, axis=0, tiled=True)
    last_query = first_row + tokens - 1
    lowest_seg = own_segs[0]
    chunk_ends = segment_ids[KEY_CHUNK - 1 :: KEY_CHUNK]
    first_chunk = jnp.sum((chunk_ends < lowest_seg).astype(jnp.int32))
    last_chunk = last_query // KEY_CHUNK

    attended = chunk_attention(
        queries, joined, segment_ids, own_segs, query_index, first_chunk, last_chunk
    )
    attended = (
        attended.transpose(2, 0, 1, 3)
        .reshape(tokens, query_heads * HEAD_DIM)
    )
    attended = attended.astype(jnp.bfloat16)
    partial_out = jnp.dot(attended, w_out, preferred_element_type=jnp.float32)
    attn_mixed = tp_sum(partial_out.astype(jnp.bfloat16))
    residual = (hidden.astype(jnp.float32) + attn_mixed).astype(jnp.bfloat16)
    normed_moe = normalize(residual, norm_moe).astype(jnp.bfloat16)
    route_count = routes.shape[1]
    slots_dev = w_gate.shape[0]
    seq_count = lax.axis_size(SUB_AXES)
    slot_total = slots_dev * seq_count
    copies = slot_total // EXPERTS
    block_rows = tokens // copies
    capacity = 2 * block_rows * route_count // EXPERTS
    copy_of = (jnp.arange(tokens, dtype=jnp.int32) // block_rows)[:, None]
    slot_of = routes + EXPERTS * copy_of
    flat_expert = routes.reshape(copies, block_rows * route_count)
    onehot = (
        flat_expert[:, :, None] == jnp.arange(EXPERTS, dtype=jnp.int32)[None, None, :]
    ).astype(jnp.int32)
    before = jnp.cumsum(onehot, axis=1) - onehot
    slot_rank = jnp.sum(before * onehot, axis=2).reshape(tokens, route_count)
    target = slot_of * capacity + slot_rank
    token_ids = jnp.broadcast_to(
        jnp.arange(tokens, dtype=jnp.int32)[:, None], (tokens, route_count)
    )
    source = (
        jnp.full((slot_total * capacity,), tokens, jnp.int32)
        .at[target.reshape(-1)]
        .set(token_ids.reshape(-1))
    )
    half = capacity // 2
    core = lax.axis_index("tc")
    swap = [(0, 1), (1, 0)]
    own_source = lax.dynamic_slice_in_dim(
        source.reshape(seq_count, slots_dev, capacity), core * half, half, axis=2
    )
    padded_rows = jnp.concatenate([normed_moe, jnp.zeros((1, normed_moe.shape[1]), jnp.bfloat16)])
    outbound = padded_rows[own_source]
    arrived_own = lax.all_to_all(outbound, SUB_AXES, split_axis=0, concat_axis=0, tiled=True)
    arrived_other = lax.ppermute(arrived_own, "tc", swap)
    arrived = jnp.concatenate([arrived_own, arrived_other], axis=2)
    gate_val = jnp.einsum("jsrd,sdf->jsrf", arrived, w_gate, preferred_element_type=jnp.float32)
    up_val = jnp.einsum("jsrd,sdf->jsrf", arrived, w_up, preferred_element_type=jnp.float32)
    activated = (jax.nn.silu(gate_val) * up_val).astype(jnp.bfloat16)
    group_part = jnp.einsum("jsrf,sfd->jsrd", activated, w_down, preferred_element_type=jnp.float32)
    result = group_part.astype(jnp.bfloat16)
    sibling_part = lax.ppermute(result[:, :, half:], "tc", swap)
    pair_sum = (result[:, :, :half].astype(jnp.float32) + sibling_part.astype(jnp.float32)).astype(
        jnp.bfloat16
    )
    returned = lax.all_to_all(pair_sum, SUB_AXES, split_axis=0, concat_axis=0, tiled=True).reshape(
        slot_total * half, model_width
    )
    own_route = (slot_rank // half) == core
    local_target = jnp.where(own_route, slot_of * half + slot_rank - core * half, 0)
    own_gates = jnp.where(own_route, gates, 0.0)
    picked = returned[local_target]
    combined = jnp.einsum(
        "tk,tkd->td",
        own_gates,
        picked,
        preferred_element_type=jnp.float32,
        precision=lax.Precision.HIGHEST,
    )
    expert_sum = tp_sum(combined.astype(jnp.bfloat16))
    hidden_out = (residual.astype(jnp.float32) + expert_sum).astype(jnp.bfloat16)
    return (hidden_out, kv_cache)


def solution(mesh):
    seq_size, tp_size = mesh.devices.shape
    side = round(seq_size ** (1 / 3))
    sub_mesh = Mesh(
        mesh.devices.reshape(side, side, seq_size // side // side, tp_size // 2, 2), SUB_AXES + TP_AXES
    )
    return jax.shard_map(
        per_device,
        mesh=sub_mesh,
        in_specs=(
            P(SUB_AXES, None),
            P(),
            P(SUB_AXES, None),
            P(SUB_AXES, None),
            P(),
            P(),
            P(None, TP_AXES),
            P(None, TP_AXES),
            P(None, TP_AXES),
            P(TP_AXES, None),
            P(SUB_AXES, None, TP_AXES),
            P(SUB_AXES, None, TP_AXES),
            P(SUB_AXES, TP_AXES, None),
        ),
        out_specs=(P(SUB_AXES, None), P(SUB_AXES, None, TP_AXES)),
        check_vma=False,
    )
```

```python
import jax
import jax.numpy as jnp
from jax import lax
from jax.experimental import pallas as pl
from jax.experimental.pallas import tpu as pltpu
from jax.sharding import Mesh
from jax.sharding import PartitionSpec as P

HEAD_DIM = 64
EXPERTS = 32
SEG_VALUES = 8
KEY_CHUNK = 1024

EPS = 1e-06
SCORE_SCALE = 0.015625
SUB_AXES = ("sy", "sz", "sx")
TP_AXES = ("tz", "tc")


def normalize(values, gain):
    widened = values.astype(jnp.float32)
    return (
        widened
        * lax.rsqrt(jnp.mean(widened * widened, axis=-1, keepdims=True) + EPS)
        * gain.astype(jnp.float32)
    )


def rotary(tensor, positions):
    half_dim = tensor.shape[-1] // 2
    frequencies = 10000.0 ** (-jnp.arange(half_dim, dtype=jnp.float32) * 2.0 / tensor.shape[-1])
    angles = positions.astype(jnp.float32)[:, None] * frequencies[None, :]
    cosine = jnp.cos(angles)[:, None, :]
    sine_part = jnp.sin(angles)[:, None, :]
    lower_half = tensor[..., :half_dim]
    upper_half = tensor[..., half_dim:]
    return jnp.concatenate(
        [
            lower_half * cosine - upper_half * sine_part,
            upper_half * cosine + lower_half * sine_part,
        ],
        axis=-1,
    )


def attention_kernel(bounds_ref, q_ref, k_ref, v_ref, kseg_ref, qseg_ref, qidx_ref, o_ref, m_sc, l_sc, acc_sc):
    step = pl.program_id(0)
    kv_heads, group_size = q_ref.shape[0], q_ref.shape[1]

    @pl.when(step == 0)
    def _():
        m_sc[...] = jnp.full(m_sc.shape, -1e30, jnp.float32)
        l_sc[...] = jnp.zeros(l_sc.shape, jnp.float32)
        acc_sc[...] = jnp.zeros(acc_sc.shape, jnp.float32)

    chunk = bounds_ref[0] + step

    @pl.when(chunk <= bounds_ref[1])
    def _():
        key_index = chunk * KEY_CHUNK + lax.broadcasted_iota(jnp.int32, (1, KEY_CHUNK), 1)
        allowed = (qseg_ref[...] == kseg_ref[0]) & (qidx_ref[...] >= key_index)
        key_rows = k_ref[...]
        value_rows = v_ref[...]
        for head in range(kv_heads):
            for member in range(group_size):
                slot = head * group_size + member
                scores = (
                    lax.dot_general(
                        q_ref[head, member],
                        key_rows,
                        (((1,), (1,)), ((), ())),
                        preferred_element_type=jnp.float32,
                    )
                    * SCORE_SCALE
                )
                masked = jnp.where(allowed, scores, -1e30)
                running_max = m_sc[slot]
                new_max = jnp.maximum(running_max, jnp.max(masked, axis=-1, keepdims=True))
                weights = jnp.where(allowed, jnp.exp(masked - new_max), 0.0)
                factor = jnp.exp(running_max - new_max)
                l_sc[slot] = l_sc[slot] * factor + jnp.sum(weights, axis=-1, keepdims=True)
                acc_sc[slot] = acc_sc[slot] * factor + jnp.dot(
                    weights.astype(jnp.bfloat16), value_rows, preferred_element_type=jnp.float32
                )
                m_sc[slot] = new_max

    @pl.when(step == pl.num_programs(0) - 1)
    def _():
        o_ref[...] = acc_sc[...] / l_sc[...]


def chunk_attention(queries, joined, segment_ids, own_segs, query_index, first_chunk, last_chunk):
    kv_heads, group_size, tokens, head_dim = queries.shape
    total, both_width = joined.shape
    kv_width = both_width // 2
    chunks = total // KEY_CHUNK
    head_mask = jnp.eye(kv_heads, dtype=jnp.bool_)[:, None, None, :, None]
    padded_queries = jnp.where(head_mask, queries[:, :, :, None, :], jnp.zeros((), queries.dtype)).reshape(
        kv_heads, group_size, tokens, kv_width
    )
    bounds = jnp.stack([first_chunk, last_chunk]).astype(jnp.int32)

    def key_map(step, bounds_ref):
        return (jnp.minimum(bounds_ref[0] + step, bounds_ref[1]), 0)

    def value_map(step, bounds_ref):
        return (jnp.minimum(bounds_ref[0] + step, bounds_ref[1]), 1)

    def seg_map(step, bounds_ref):
        return (jnp.minimum(bounds_ref[0] + step, bounds_ref[1]), 0, 0)

    def whole(step, bounds_ref):
        return (0, 0, 0, 0)

    def whole2(step, bounds_ref):
        return (0, 0)

    def whole3(step, bounds_ref):
        return (0, 0, 0)

    spec = pltpu.PrefetchScalarGridSpec(
        num_scalar_prefetch=1,
        grid=(chunks,),
        in_specs=[
            pl.BlockSpec((kv_heads, group_size, tokens, kv_width), whole),
            pl.BlockSpec((KEY_CHUNK, kv_width), key_map),
            pl.BlockSpec((KEY_CHUNK, kv_width), value_map),
            pl.BlockSpec((1, 1, KEY_CHUNK), seg_map),
            pl.BlockSpec((tokens, 1), whole2),
            pl.BlockSpec((tokens, 1), whole2),
        ],
        out_specs=pl.BlockSpec((kv_heads * group_size, tokens, kv_width), whole3),
        scratch_shapes=[
            pltpu.VMEM((kv_heads * group_size, tokens, 1), jnp.float32),
            pltpu.VMEM((kv_heads * group_size, tokens, 1), jnp.float32),
            pltpu.VMEM((kv_heads * group_size, tokens, kv_width), jnp.float32),
        ],
    )
    out = pl.pallas_call(
        attention_kernel,
        grid_spec=spec,
        out_shape=jax.ShapeDtypeStruct((kv_heads * group_size, tokens, kv_width), jnp.float32),
        compiler_params=pltpu.CompilerParams(dimension_semantics=("arbitrary",)),
    )(
        bounds,
        padded_queries,
        joined,
        joined,
        segment_ids.reshape(chunks, 1, KEY_CHUNK),
        own_segs.reshape(tokens, 1),
        query_index.reshape(tokens, 1),
    )
    out = out.reshape(kv_heads, group_size, tokens, kv_heads, head_dim)
    return jnp.stack([out[head, :, :, head] for head in range(kv_heads)])


def seq_all_to_all(blocks):
    grid = blocks.reshape((4, 4, 4) + blocks.shape[1:])
    for position, axis_name in ((2, "sx"), (1, "sz"), (0, "sy")):
        grid = lax.all_to_all(grid, axis_name, split_axis=position, concat_axis=position, tiled=True)
    return grid.reshape(blocks.shape)


def tp_sum(partial):
    swap = [(0, 1), (1, 0)]
    pair = partial.astype(jnp.float32) + lax.ppermute(partial, "tc", swap).astype(jnp.float32)
    pair = pair.astype(jnp.bfloat16)
    return pair.astype(jnp.float32) + lax.ppermute(pair, "tz", swap).astype(jnp.float32)


def per_device(
    hidden,
    segment_ids,
    routes,
    gates,
    norm_attn,
    norm_moe,
    w_query,
    w_key,
    w_value,
    w_out,
    w_gate,
    w_up,
    w_down,
):
    tokens = hidden.shape[0]
    model_width = hidden.shape[1]
    total_tokens = segment_ids.shape[0]
    first_row = lax.axis_index(SUB_AXES) * tokens
    own_segs = lax.dynamic_slice_in_dim(segment_ids, first_row, tokens)
    seg_starts = jnp.sum(
        (segment_ids[None, :] < jnp.arange(SEG_VALUES, dtype=jnp.int32)[:, None]).astype(jnp.int32),
        axis=1,
    )
    query_index = first_row + jnp.arange(tokens, dtype=jnp.int32)
    positions = query_index - seg_starts[own_segs]
    normed = normalize(hidden, norm_attn).astype(jnp.bfloat16)
    query_heads = w_query.shape[1] // HEAD_DIM
    kv_heads = w_key.shape[1] // HEAD_DIM
    group_size = query_heads // kv_heads
    queries = jnp.dot(normed, w_query, preferred_element_type=jnp.float32).reshape(
        tokens, query_heads, HEAD_DIM
    )
    queries = (
        rotary(queries, positions)
        .astype(jnp.bfloat16)
        .reshape(tokens, kv_heads, group_size, HEAD_DIM)
        .transpose(1, 2, 0, 3)
    )
    key_raw = jnp.dot(normed, w_key, preferred_element_type=jnp.float32).reshape(
        tokens, kv_heads, HEAD_DIM
    )
    value_proj = jnp.dot(normed, w_value, preferred_element_type=jnp.float32).astype(jnp.bfloat16)
    kv_cache = jnp.stack(
        [key_raw.reshape(tokens, kv_heads * HEAD_DIM).astype(jnp.bfloat16), value_proj], axis=1
    )
    key_rot = rotary(key_raw, positions).astype(jnp.bfloat16)
    kv_width = kv_heads * HEAD_DIM
    joined = jnp.concatenate([key_rot.reshape(tokens, kv_width), value_proj], axis=1)
    for axis_name in SUB_AXES[::-1]:
        joined = lax.all_gather(joined, axis_name, axis=0, tiled=True)
    last_query = first_row + tokens - 1
    lowest_seg = own_segs[0]
    chunk_ends = segment_ids[KEY_CHUNK - 1 :: KEY_CHUNK]
    first_chunk = jnp.sum((chunk_ends < lowest_seg).astype(jnp.int32))
    last_chunk = last_query // KEY_CHUNK

    attended = chunk_attention(
        queries, joined, segment_ids, own_segs, query_index, first_chunk, last_chunk
    )
    attended = (
        attended.transpose(2, 0, 1, 3)
        .reshape(tokens, query_heads * HEAD_DIM)
    )
    attended = attended.astype(jnp.bfloat16)
    partial_out = jnp.dot(attended, w_out, preferred_element_type=jnp.float32)
    attn_mixed = tp_sum(partial_out.astype(jnp.bfloat16))
    residual = (hidden.astype(jnp.float32) + attn_mixed).astype(jnp.bfloat16)
    normed_moe = normalize(residual, norm_moe).astype(jnp.bfloat16)
    route_count = routes.shape[1]
    slots_dev = w_gate.shape[0]
    seq_count = lax.axis_size(SUB_AXES)
    slot_total = slots_dev * seq_count
    copies = slot_total // EXPERTS
    block_rows = tokens // copies
    capacity = 2 * block_rows * route_count // EXPERTS
    copy_of = (jnp.arange(tokens, dtype=jnp.int32) // block_rows)[:, None]
    slot_of = routes + EXPERTS * copy_of
    flat_expert = routes.reshape(copies, block_rows * route_count)
    onehot = (
        flat_expert[:, :, None] == jnp.arange(EXPERTS, dtype=jnp.int32)[None, None, :]
    ).astype(jnp.int32)
    before = jnp.cumsum(onehot, axis=1) - onehot
    slot_rank = jnp.sum(before * onehot, axis=2).reshape(tokens, route_count)
    target = slot_of * capacity + slot_rank
    token_ids = jnp.broadcast_to(
        jnp.arange(tokens, dtype=jnp.int32)[:, None], (tokens, route_count)
    )
    source = (
        jnp.full((slot_total * capacity,), tokens, jnp.int32)
        .at[target.reshape(-1)]
        .set(token_ids.reshape(-1))
    )
    half = capacity // 2
    core = lax.axis_index("tc")
    swap = [(0, 1), (1, 0)]
    own_source = lax.dynamic_slice_in_dim(
        source.reshape(seq_count, slots_dev, capacity), core * half, half, axis=2
    )
    padded_rows = jnp.concatenate([normed_moe, jnp.zeros((1, normed_moe.shape[1]), jnp.bfloat16)])
    outbound = padded_rows[own_source]
    arrived_own = seq_all_to_all(outbound)
    arrived_other = lax.ppermute(arrived_own, "tc", swap)
    arrived = jnp.concatenate([arrived_own, arrived_other], axis=2)
    gate_val = jnp.einsum("jsrd,sdf->jsrf", arrived, w_gate, preferred_element_type=jnp.float32)
    up_val = jnp.einsum("jsrd,sdf->jsrf", arrived, w_up, preferred_element_type=jnp.float32)
    activated = (jax.nn.silu(gate_val) * up_val).astype(jnp.bfloat16)
    group_part = jnp.einsum("jsrf,sfd->jsrd", activated, w_down, preferred_element_type=jnp.float32)
    result = group_part.astype(jnp.bfloat16)
    sibling_part = lax.ppermute(result[:, :, half:], "tc", swap)
    pair_sum = (result[:, :, :half].astype(jnp.float32) + sibling_part.astype(jnp.float32)).astype(
        jnp.bfloat16
    )
    returned = seq_all_to_all(pair_sum).reshape(
        slot_total * half, model_width
    )
    own_route = (slot_rank // half) == core
    local_target = jnp.where(own_route, slot_of * half + slot_rank - core * half, 0)
    own_gates = jnp.where(own_route, gates, 0.0)
    picked = returned[local_target]
    combined = jnp.einsum(
        "tk,tkd->td",
        own_gates,
        picked,
        preferred_element_type=jnp.float32,
        precision=lax.Precision.HIGHEST,
    )
    expert_sum = tp_sum(combined.astype(jnp.bfloat16))
    hidden_out = (residual.astype(jnp.float32) + expert_sum).astype(jnp.bfloat16)
    return (hidden_out, kv_cache)


def solution(mesh):
    seq_size, tp_size = mesh.devices.shape
    side = round(seq_size ** (1 / 3))
    sub_mesh = Mesh(
        mesh.devices.reshape(side, side, seq_size // side // side, tp_size // 2, 2), SUB_AXES + TP_AXES
    )
    return jax.shard_map(
        per_device,
        mesh=sub_mesh,
        in_specs=(
            P(SUB_AXES, None),
            P(),
            P(SUB_AXES, None),
            P(SUB_AXES, None),
            P(),
            P(),
            P(None, TP_AXES),
            P(None, TP_AXES),
            P(None, TP_AXES),
            P(TP_AXES, None),
            P(SUB_AXES, None, TP_AXES),
            P(SUB_AXES, None, TP_AXES),
            P(SUB_AXES, TP_AXES, None),
        ),
        out_specs=(P(SUB_AXES, None), P(SUB_AXES, None, TP_AXES)),
        check_vma=False,
    )
```

```python
import jax
import jax.numpy as jnp
from jax import lax
from jax.experimental import pallas as pl
from jax.experimental.pallas import tpu as pltpu
from jax.sharding import Mesh
from jax.sharding import PartitionSpec as P

HEAD_DIM = 64
EXPERTS = 32
SEG_VALUES = 8
KEY_CHUNK = 1024

EPS = 1e-06
SCORE_SCALE = 0.015625
SUB_AXES = ("sy", "sz", "sx")
TP_AXES = ("tz", "tc")


def normalize(values, gain):
    widened = values.astype(jnp.float32)
    return (
        widened
        * lax.rsqrt(jnp.mean(widened * widened, axis=-1, keepdims=True) + EPS)
        * gain.astype(jnp.float32)
    )


def rotary(tensor, positions):
    half_dim = tensor.shape[-1] // 2
    frequencies = 10000.0 ** (-jnp.arange(half_dim, dtype=jnp.float32) * 2.0 / tensor.shape[-1])
    angles = positions.astype(jnp.float32)[:, None] * frequencies[None, :]
    cosine = jnp.cos(angles)[:, None, :]
    sine_part = jnp.sin(angles)[:, None, :]
    lower_half = tensor[..., :half_dim]
    upper_half = tensor[..., half_dim:]
    return jnp.concatenate(
        [
            lower_half * cosine - upper_half * sine_part,
            upper_half * cosine + lower_half * sine_part,
        ],
        axis=-1,
    )


def attention_kernel(bounds_ref, q_ref, k_ref, v_ref, kseg_ref, qseg_ref, qidx_ref, o_ref, m_sc, l_sc, acc_sc):
    step = pl.program_id(0)
    kv_heads, group_size = q_ref.shape[0], q_ref.shape[1]

    @pl.when(step == 0)
    def _():
        m_sc[...] = jnp.full(m_sc.shape, -1e30, jnp.float32)
        l_sc[...] = jnp.zeros(l_sc.shape, jnp.float32)
        acc_sc[...] = jnp.zeros(acc_sc.shape, jnp.float32)

    chunk = bounds_ref[0] + step

    @pl.when(chunk <= bounds_ref[1])
    def _():
        key_index = chunk * KEY_CHUNK + lax.broadcasted_iota(jnp.int32, (1, KEY_CHUNK), 1)
        allowed = (qseg_ref[...] == kseg_ref[0]) & (qidx_ref[...] >= key_index)
        key_rows = k_ref[...]
        value_rows = v_ref[...]
        for head in range(kv_heads):
            for member in range(group_size):
                slot = head * group_size + member
                scores = (
                    lax.dot_general(
                        q_ref[head, member],
                        key_rows,
                        (((1,), (1,)), ((), ())),
                        preferred_element_type=jnp.float32,
                    )
                    * SCORE_SCALE
                )
                masked = jnp.where(allowed, scores, -1e30)
                running_max = m_sc[slot]
                new_max = jnp.maximum(running_max, jnp.max(masked, axis=-1, keepdims=True))
                weights = jnp.where(allowed, jnp.exp(masked - new_max), 0.0)
                factor = jnp.exp(running_max - new_max)
                l_sc[slot] = l_sc[slot] * factor + jnp.sum(weights, axis=-1, keepdims=True)
                acc_sc[slot] = acc_sc[slot] * factor + jnp.dot(
                    weights.astype(jnp.bfloat16), value_rows, preferred_element_type=jnp.float32
                )
                m_sc[slot] = new_max

    @pl.when(step == pl.num_programs(0) - 1)
    def _():
        o_ref[...] = acc_sc[...] / l_sc[...]


def chunk_attention(queries, joined, segment_ids, own_segs, query_index, first_chunk, last_chunk):
    kv_heads, group_size, tokens, head_dim = queries.shape
    total, both_width = joined.shape
    kv_width = both_width // 2
    chunks = total // KEY_CHUNK
    head_mask = jnp.eye(kv_heads, dtype=jnp.bool_)[:, None, None, :, None]
    padded_queries = jnp.where(head_mask, queries[:, :, :, None, :], jnp.zeros((), queries.dtype)).reshape(
        kv_heads, group_size, tokens, kv_width
    )
    bounds = jnp.stack([first_chunk, last_chunk]).astype(jnp.int32)

    def key_map(step, bounds_ref):
        return (jnp.minimum(bounds_ref[0] + step, bounds_ref[1]), 0)

    def value_map(step, bounds_ref):
        return (jnp.minimum(bounds_ref[0] + step, bounds_ref[1]), 1)

    def seg_map(step, bounds_ref):
        return (jnp.minimum(bounds_ref[0] + step, bounds_ref[1]), 0, 0)

    def whole(step, bounds_ref):
        return (0, 0, 0, 0)

    def whole2(step, bounds_ref):
        return (0, 0)

    def whole3(step, bounds_ref):
        return (0, 0, 0)

    spec = pltpu.PrefetchScalarGridSpec(
        num_scalar_prefetch=1,
        grid=(chunks,),
        in_specs=[
            pl.BlockSpec((kv_heads, group_size, tokens, kv_width), whole),
            pl.BlockSpec((KEY_CHUNK, kv_width), key_map),
            pl.BlockSpec((KEY_CHUNK, kv_width), value_map),
            pl.BlockSpec((1, 1, KEY_CHUNK), seg_map),
            pl.BlockSpec((tokens, 1), whole2),
            pl.BlockSpec((tokens, 1), whole2),
        ],
        out_specs=pl.BlockSpec((kv_heads * group_size, tokens, kv_width), whole3),
        scratch_shapes=[
            pltpu.VMEM((kv_heads * group_size, tokens, 1), jnp.float32),
            pltpu.VMEM((kv_heads * group_size, tokens, 1), jnp.float32),
            pltpu.VMEM((kv_heads * group_size, tokens, kv_width), jnp.float32),
        ],
    )
    out = pl.pallas_call(
        attention_kernel,
        grid_spec=spec,
        out_shape=jax.ShapeDtypeStruct((kv_heads * group_size, tokens, kv_width), jnp.float32),
        compiler_params=pltpu.CompilerParams(dimension_semantics=("arbitrary",)),
    )(
        bounds,
        padded_queries,
        joined,
        joined,
        segment_ids.reshape(chunks, 1, KEY_CHUNK),
        own_segs.reshape(tokens, 1),
        query_index.reshape(tokens, 1),
    )
    out = out.reshape(kv_heads, group_size, tokens, kv_heads, head_dim)
    return jnp.stack([out[head, :, :, head] for head in range(kv_heads)])


def tp_sum(partial):
    swap = [(0, 1), (1, 0)]
    pair = partial.astype(jnp.float32) + lax.ppermute(partial, "tc", swap).astype(jnp.float32)
    pair = pair.astype(jnp.bfloat16)
    return pair.astype(jnp.float32) + lax.ppermute(pair, "tz", swap).astype(jnp.float32)


def per_device(
    hidden,
    segment_ids,
    routes,
    gates,
    norm_attn,
    norm_moe,
    w_query,
    w_key,
    w_value,
    w_out,
    w_gate,
    w_up,
    w_down,
):
    tokens = hidden.shape[0]
    model_width = hidden.shape[1]
    total_tokens = segment_ids.shape[0]
    first_row = lax.axis_index(SUB_AXES) * tokens
    own_segs = lax.dynamic_slice_in_dim(segment_ids, first_row, tokens)
    seg_starts = jnp.sum(
        (segment_ids[None, :] < jnp.arange(SEG_VALUES, dtype=jnp.int32)[:, None]).astype(jnp.int32),
        axis=1,
    )
    query_index = first_row + jnp.arange(tokens, dtype=jnp.int32)
    positions = query_index - seg_starts[own_segs]
    normed = normalize(hidden, norm_attn).astype(jnp.bfloat16)
    query_heads = w_query.shape[1] // HEAD_DIM
    kv_heads = w_key.shape[1] // HEAD_DIM
    group_size = query_heads // kv_heads
    queries = jnp.dot(normed, w_query, preferred_element_type=jnp.float32).reshape(
        tokens, query_heads, HEAD_DIM
    )
    queries = (
        rotary(queries, positions)
        .astype(jnp.bfloat16)
        .reshape(tokens, kv_heads, group_size, HEAD_DIM)
        .transpose(1, 2, 0, 3)
    )
    key_raw = jnp.dot(normed, w_key, preferred_element_type=jnp.float32).reshape(
        tokens, kv_heads, HEAD_DIM
    )
    value_proj = jnp.dot(normed, w_value, preferred_element_type=jnp.float32).astype(jnp.bfloat16)
    kv_cache = jnp.stack(
        [key_raw.reshape(tokens, kv_heads * HEAD_DIM).astype(jnp.bfloat16), value_proj], axis=1
    )
    key_rot = rotary(key_raw, positions).astype(jnp.bfloat16)
    kv_width = kv_heads * HEAD_DIM
    joined = jnp.concatenate([key_rot.reshape(tokens, kv_width), value_proj], axis=1)
    for axis_name in SUB_AXES[::-1]:
        joined = lax.all_gather(joined, axis_name, axis=0, tiled=True)
    last_query = first_row + tokens - 1
    lowest_seg = own_segs[0]
    chunk_ends = segment_ids[KEY_CHUNK - 1 :: KEY_CHUNK]
    first_chunk = jnp.sum((chunk_ends < lowest_seg).astype(jnp.int32))
    last_chunk = last_query // KEY_CHUNK

    attended = chunk_attention(
        queries, joined, segment_ids, own_segs, query_index, first_chunk, last_chunk
    )
    attended = (
        attended.transpose(2, 0, 1, 3)
        .reshape(tokens, query_heads * HEAD_DIM)
    )
    attended = attended.astype(jnp.bfloat16)
    partial_out = jnp.dot(attended, w_out, preferred_element_type=jnp.float32)
    attn_mixed = tp_sum(partial_out.astype(jnp.bfloat16))
    residual = (hidden.astype(jnp.float32) + attn_mixed).astype(jnp.bfloat16)
    normed_moe = normalize(residual, norm_moe).astype(jnp.bfloat16)
    route_count = routes.shape[1]
    slots_dev = w_gate.shape[0]
    seq_count = lax.axis_size(SUB_AXES)
    slot_total = slots_dev * seq_count
    copies = slot_total // EXPERTS
    block_rows = tokens // copies
    capacity = 2 * block_rows * route_count // EXPERTS
    copy_of = (jnp.arange(tokens, dtype=jnp.int32) // block_rows)[:, None]
    slot_of = routes + EXPERTS * copy_of
    flat_expert = routes.reshape(copies, block_rows * route_count)
    onehot = (
        flat_expert[:, :, None] == jnp.arange(EXPERTS, dtype=jnp.int32)[None, None, :]
    ).astype(jnp.int32)
    before = jnp.cumsum(onehot, axis=1) - onehot
    slot_rank = jnp.sum(before * onehot, axis=2).reshape(tokens, route_count)
    target = slot_of * capacity + slot_rank
    half = capacity // 2
    core = lax.axis_index("tc")
    swap = [(0, 1), (1, 0)]
    own_route = (slot_rank // half) == core
    local_target = jnp.where(own_route, slot_of * half + slot_rank - core * half, -1)
    row_ids = jnp.arange(slot_total * half, dtype=jnp.int32)
    picks = local_target[None, :, :] == row_ids[:, None, None]
    dispatch = jnp.any(picks, axis=2).astype(jnp.bfloat16)
    outbound = jnp.dot(dispatch, normed_moe, preferred_element_type=jnp.float32).astype(jnp.bfloat16)
    outbound = outbound.reshape(seq_count, slots_dev, half, model_width)
    arrived_own = lax.all_to_all(outbound, SUB_AXES, split_axis=0, concat_axis=0, tiled=True)
    arrived_other = lax.ppermute(arrived_own, "tc", swap)
    arrived = jnp.concatenate([arrived_own, arrived_other], axis=2)
    gate_val = jnp.einsum("jsrd,sdf->jsrf", arrived, w_gate, preferred_element_type=jnp.float32)
    up_val = jnp.einsum("jsrd,sdf->jsrf", arrived, w_up, preferred_element_type=jnp.float32)
    activated = (jax.nn.silu(gate_val) * up_val).astype(jnp.bfloat16)
    group_part = jnp.einsum("jsrf,sfd->jsrd", activated, w_down, preferred_element_type=jnp.float32)
    result = group_part.astype(jnp.bfloat16)
    sibling_part = lax.ppermute(result[:, :, half:], "tc", swap)
    pair_sum = (result[:, :, :half].astype(jnp.float32) + sibling_part.astype(jnp.float32)).astype(
        jnp.bfloat16
    )
    returned = lax.all_to_all(pair_sum, SUB_AXES, split_axis=0, concat_axis=0, tiled=True).reshape(
        slot_total * half, model_width
    )
    weighting = jnp.sum(
        jnp.where(local_target[:, :, None] == row_ids[None, None, :], gates[:, :, None], 0.0), axis=1
    )
    combined = jnp.dot(
        weighting, returned, preferred_element_type=jnp.float32, precision=lax.Precision.HIGHEST
    )
    expert_sum = tp_sum(combined.astype(jnp.bfloat16))
    hidden_out = (residual.astype(jnp.float32) + expert_sum).astype(jnp.bfloat16)
    return (hidden_out, kv_cache)


def solution(mesh):
    seq_size, tp_size = mesh.devices.shape
    side = round(seq_size ** (1 / 3))
    sub_mesh = Mesh(
        mesh.devices.reshape(side, side, seq_size // side // side, tp_size // 2, 2), SUB_AXES + TP_AXES
    )
    return jax.shard_map(
        per_device,
        mesh=sub_mesh,
        in_specs=(
            P(SUB_AXES, None),
            P(),
            P(SUB_AXES, None),
            P(SUB_AXES, None),
            P(),
            P(),
            P(None, TP_AXES),
            P(None, TP_AXES),
            P(None, TP_AXES),
            P(TP_AXES, None),
            P(SUB_AXES, None, TP_AXES),
            P(SUB_AXES, None, TP_AXES),
            P(SUB_AXES, TP_AXES, None),
        ),
        out_specs=(P(SUB_AXES, None), P(SUB_AXES, None, TP_AXES)),
        check_vma=False,
    )
```

```python
import jax
import jax.numpy as jnp
from jax import lax
from jax.experimental import pallas as pl
from jax.experimental.pallas import tpu as pltpu
from jax.sharding import Mesh
from jax.sharding import PartitionSpec as P

HEAD_DIM = 64
EXPERTS = 32
SEG_VALUES = 8
KEY_CHUNK = 1024

EPS = 1e-06
SCORE_SCALE = 0.015625
SUB_AXES = ("sy", "sz", "sx")
TP_AXES = ("tz", "tc")


def normalize(values, gain):
    widened = values.astype(jnp.float32)
    return (
        widened
        * lax.rsqrt(jnp.mean(widened * widened, axis=-1, keepdims=True) + EPS)
        * gain.astype(jnp.float32)
    )


def rotary(tensor, positions):
    half_dim = tensor.shape[-1] // 2
    frequencies = 10000.0 ** (-jnp.arange(half_dim, dtype=jnp.float32) * 2.0 / tensor.shape[-1])
    angles = positions.astype(jnp.float32)[:, None] * frequencies[None, :]
    cosine = jnp.cos(angles)[:, None, :]
    sine_part = jnp.sin(angles)[:, None, :]
    lower_half = tensor[..., :half_dim]
    upper_half = tensor[..., half_dim:]
    return jnp.concatenate(
        [
            lower_half * cosine - upper_half * sine_part,
            upper_half * cosine + lower_half * sine_part,
        ],
        axis=-1,
    )


def attention_kernel(bounds_ref, q_ref, k_ref, v_ref, kseg_ref, qseg_ref, qidx_ref, o_ref, m_sc, l_sc, acc_sc):
    step = pl.program_id(0)
    kv_heads, group_size = q_ref.shape[0], q_ref.shape[1]

    @pl.when(step == 0)
    def _():
        m_sc[...] = jnp.full(m_sc.shape, -1e30, jnp.float32)
        l_sc[...] = jnp.zeros(l_sc.shape, jnp.float32)
        acc_sc[...] = jnp.zeros(acc_sc.shape, jnp.float32)

    chunk = bounds_ref[0] + step

    @pl.when(chunk <= bounds_ref[1])
    def _():
        key_index = chunk * KEY_CHUNK + lax.broadcasted_iota(jnp.int32, (1, KEY_CHUNK), 1)
        allowed = (qseg_ref[...] == kseg_ref[0]) & (qidx_ref[...] >= key_index)
        key_rows = k_ref[...]
        value_rows = v_ref[...]
        for head in range(kv_heads):
            for member in range(group_size):
                slot = head * group_size + member
                scores = (
                    lax.dot_general(
                        q_ref[head, member],
                        key_rows,
                        (((1,), (1,)), ((), ())),
                        preferred_element_type=jnp.float32,
                    )
                    * SCORE_SCALE
                )
                masked = jnp.where(allowed, scores, -1e30)
                running_max = m_sc[slot]
                new_max = jnp.maximum(running_max, jnp.max(masked, axis=-1, keepdims=True))
                weights = jnp.where(allowed, jnp.exp(masked - new_max), 0.0)
                factor = jnp.exp(running_max - new_max)
                l_sc[slot] = l_sc[slot] * factor + jnp.sum(weights, axis=-1, keepdims=True)
                acc_sc[slot] = acc_sc[slot] * factor + jnp.dot(
                    weights.astype(jnp.bfloat16), value_rows, preferred_element_type=jnp.float32
                )
                m_sc[slot] = new_max

    @pl.when(step == pl.num_programs(0) - 1)
    def _():
        o_ref[...] = acc_sc[...] / l_sc[...]


def chunk_attention(queries, joined, segment_ids, own_segs, query_index, first_chunk, last_chunk):
    kv_heads, group_size, tokens, head_dim = queries.shape
    total, both_width = joined.shape
    kv_width = both_width // 2
    chunks = total // KEY_CHUNK
    head_mask = jnp.eye(kv_heads, dtype=jnp.bool_)[:, None, None, :, None]
    padded_queries = jnp.where(head_mask, queries[:, :, :, None, :], jnp.zeros((), queries.dtype)).reshape(
        kv_heads, group_size, tokens, kv_width
    )
    bounds = jnp.stack([first_chunk, last_chunk]).astype(jnp.int32)

    def key_map(step, bounds_ref):
        return (jnp.minimum(bounds_ref[0] + step, bounds_ref[1]), 0)

    def value_map(step, bounds_ref):
        return (jnp.minimum(bounds_ref[0] + step, bounds_ref[1]), 1)

    def seg_map(step, bounds_ref):
        return (jnp.minimum(bounds_ref[0] + step, bounds_ref[1]), 0, 0)

    def whole(step, bounds_ref):
        return (0, 0, 0, 0)

    def whole2(step, bounds_ref):
        return (0, 0)

    def whole3(step, bounds_ref):
        return (0, 0, 0)

    spec = pltpu.PrefetchScalarGridSpec(
        num_scalar_prefetch=1,
        grid=(chunks,),
        in_specs=[
            pl.BlockSpec((kv_heads, group_size, tokens, kv_width), whole),
            pl.BlockSpec((KEY_CHUNK, kv_width), key_map),
            pl.BlockSpec((KEY_CHUNK, kv_width), value_map),
            pl.BlockSpec((1, 1, KEY_CHUNK), seg_map),
            pl.BlockSpec((tokens, 1), whole2),
            pl.BlockSpec((tokens, 1), whole2),
        ],
        out_specs=pl.BlockSpec((kv_heads * group_size, tokens, kv_width), whole3),
        scratch_shapes=[
            pltpu.VMEM((kv_heads * group_size, tokens, 1), jnp.float32),
            pltpu.VMEM((kv_heads * group_size, tokens, 1), jnp.float32),
            pltpu.VMEM((kv_heads * group_size, tokens, kv_width), jnp.float32),
        ],
    )
    out = pl.pallas_call(
        attention_kernel,
        grid_spec=spec,
        out_shape=jax.ShapeDtypeStruct((kv_heads * group_size, tokens, kv_width), jnp.float32),
        compiler_params=pltpu.CompilerParams(dimension_semantics=("arbitrary",)),
    )(
        bounds,
        padded_queries,
        joined,
        joined,
        segment_ids.reshape(chunks, 1, KEY_CHUNK),
        own_segs.reshape(tokens, 1),
        query_index.reshape(tokens, 1),
    )
    out = out.reshape(kv_heads, group_size, tokens, kv_heads, head_dim)
    return jnp.stack([out[head, :, :, head] for head in range(kv_heads)])


def tp_sum(partial):
    swap = [(0, 1), (1, 0)]
    pair = partial.astype(jnp.float32) + lax.ppermute(partial, "tc", swap).astype(jnp.float32)
    pair = pair.astype(jnp.bfloat16)
    return pair.astype(jnp.float32) + lax.ppermute(pair, "tz", swap).astype(jnp.float32)


def per_device(
    hidden,
    segment_ids,
    routes,
    gates,
    norm_attn,
    norm_moe,
    w_query,
    w_key,
    w_value,
    w_out,
    w_gate,
    w_up,
    w_down,
):
    tokens = hidden.shape[0]
    model_width = hidden.shape[1]
    total_tokens = segment_ids.shape[0]
    first_row = lax.axis_index(SUB_AXES) * tokens
    own_segs = lax.dynamic_slice_in_dim(segment_ids, first_row, tokens)
    seg_starts = jnp.sum(
        (segment_ids[None, :] < jnp.arange(SEG_VALUES, dtype=jnp.int32)[:, None]).astype(jnp.int32),
        axis=1,
    )
    query_index = first_row + jnp.arange(tokens, dtype=jnp.int32)
    positions = query_index - seg_starts[own_segs]
    normed = normalize(hidden, norm_attn).astype(jnp.bfloat16)
    query_heads = w_query.shape[1] // HEAD_DIM
    kv_heads = w_key.shape[1] // HEAD_DIM
    group_size = query_heads // kv_heads
    queries = jnp.dot(normed, w_query, preferred_element_type=jnp.float32).reshape(
        tokens, query_heads, HEAD_DIM
    )
    queries = (
        rotary(queries, positions)
        .astype(jnp.bfloat16)
        .reshape(tokens, kv_heads, group_size, HEAD_DIM)
        .transpose(1, 2, 0, 3)
    )
    key_raw = jnp.dot(normed, w_key, preferred_element_type=jnp.float32).reshape(
        tokens, kv_heads, HEAD_DIM
    )
    value_proj = jnp.dot(normed, w_value, preferred_element_type=jnp.float32).astype(jnp.bfloat16)
    kv_cache = jnp.stack(
        [key_raw.reshape(tokens, kv_heads * HEAD_DIM).astype(jnp.bfloat16), value_proj], axis=1
    )
    key_rot = rotary(key_raw, positions).astype(jnp.bfloat16)
    kv_width = kv_heads * HEAD_DIM
    joined = jnp.concatenate([key_rot.reshape(tokens, kv_width), value_proj], axis=1)
    for axis_name in SUB_AXES[::-1]:
        joined = lax.all_gather(joined, axis_name, axis=0, tiled=True)
    last_query = first_row + tokens - 1
    lowest_seg = own_segs[0]
    chunk_ends = segment_ids[KEY_CHUNK - 1 :: KEY_CHUNK]
    first_chunk = jnp.sum((chunk_ends < lowest_seg).astype(jnp.int32))
    last_chunk = last_query // KEY_CHUNK

    route_count = routes.shape[1]
    slots_dev = w_gate.shape[0]
    seq_count = lax.axis_size(SUB_AXES)
    slot_total = slots_dev * seq_count
    copies = slot_total // EXPERTS
    block_rows = tokens // copies
    capacity = 2 * block_rows * route_count // EXPERTS
    copy_of = (jnp.arange(tokens, dtype=jnp.int32) // block_rows)[:, None]
    slot_of = routes + EXPERTS * copy_of
    flat_expert = routes.reshape(copies, block_rows * route_count)
    onehot = (
        flat_expert[:, :, None] == jnp.arange(EXPERTS, dtype=jnp.int32)[None, None, :]
    ).astype(jnp.bfloat16)
    flat_rows = block_rows * route_count
    strictly_before = (
        jnp.arange(flat_rows, dtype=jnp.int32)[None, :] < jnp.arange(flat_rows, dtype=jnp.int32)[:, None]
    ).astype(jnp.bfloat16)
    before = jnp.einsum("ij,cje->cie", strictly_before, onehot, preferred_element_type=jnp.float32)
    slot_rank = (
        jnp.sum(before * onehot.astype(jnp.float32), axis=2).astype(jnp.int32).reshape(tokens, route_count)
    )
    half = capacity // 2
    core = lax.axis_index("tc")
    swap = [(0, 1), (1, 0)]
    own_route = (slot_rank // half) == core
    local_target = jnp.where(own_route, slot_of * half + slot_rank - core * half, -1)
    row_ids = jnp.arange(slot_total * half, dtype=jnp.int32)
    picks = local_target.T[:, None, :] == row_ids[None, :, None]
    dispatch = jnp.any(picks, axis=0).astype(jnp.bfloat16)
    joined, local_target, dispatch = lax.optimization_barrier((joined, local_target, dispatch))
    attended = chunk_attention(
        queries, joined, segment_ids, own_segs, query_index, first_chunk, last_chunk
    )
    attended = (
        attended.transpose(2, 0, 1, 3)
        .reshape(tokens, query_heads * HEAD_DIM)
    )
    attended = attended.astype(jnp.bfloat16)
    partial_out = jnp.dot(attended, w_out, preferred_element_type=jnp.float32)
    attn_mixed = tp_sum(partial_out.astype(jnp.bfloat16))
    residual = (hidden.astype(jnp.float32) + attn_mixed).astype(jnp.bfloat16)
    normed_moe = normalize(residual, norm_moe).astype(jnp.bfloat16)
    outbound = jnp.dot(dispatch, normed_moe, preferred_element_type=jnp.float32).astype(jnp.bfloat16)
    outbound = outbound.reshape(seq_count, slots_dev, half, model_width)
    arrived_own = lax.all_to_all(outbound, SUB_AXES, split_axis=0, concat_axis=0, tiled=True)
    arrived_other = lax.ppermute(arrived_own, "tc", swap)
    arrived = jnp.concatenate([arrived_own, arrived_other], axis=2)
    gate_val = jnp.einsum("jsrd,sdf->jsrf", arrived, w_gate, preferred_element_type=jnp.float32)
    up_val = jnp.einsum("jsrd,sdf->jsrf", arrived, w_up, preferred_element_type=jnp.float32)
    activated = (jax.nn.silu(gate_val) * up_val).astype(jnp.bfloat16)
    group_part = jnp.einsum("jsrf,sfd->jsrd", activated, w_down, preferred_element_type=jnp.float32)
    result = group_part.astype(jnp.bfloat16)
    sibling_part = lax.ppermute(result[:, :, half:], "tc", swap)
    pair_sum = (result[:, :, :half].astype(jnp.float32) + sibling_part.astype(jnp.float32)).astype(
        jnp.bfloat16
    )
    returned = lax.all_to_all(pair_sum, SUB_AXES, split_axis=0, concat_axis=0, tiled=True).reshape(
        slot_total * half, model_width
    )
    weighting = jnp.sum(
        jnp.where(local_target.T[:, :, None] == row_ids[None, None, :], gates.T[:, :, None], 0.0),
        axis=0,
    )
    combined = jnp.dot(
        weighting, returned, preferred_element_type=jnp.float32, precision=lax.Precision.HIGHEST
    )
    expert_sum = tp_sum(combined.astype(jnp.bfloat16))
    hidden_out = (residual.astype(jnp.float32) + expert_sum).astype(jnp.bfloat16)
    return (hidden_out, kv_cache)


def solution(mesh):
    seq_size, tp_size = mesh.devices.shape
    side = round(seq_size ** (1 / 3))
    sub_mesh = Mesh(
        mesh.devices.reshape(side, side, seq_size // side // side, tp_size // 2, 2), SUB_AXES + TP_AXES
    )
    return jax.shard_map(
        per_device,
        mesh=sub_mesh,
        in_specs=(
            P(SUB_AXES, None),
            P(),
            P(SUB_AXES, None),
            P(SUB_AXES, None),
            P(),
            P(),
            P(None, TP_AXES),
            P(None, TP_AXES),
            P(None, TP_AXES),
            P(TP_AXES, None),
            P(SUB_AXES, None, TP_AXES),
            P(SUB_AXES, None, TP_AXES),
            P(SUB_AXES, TP_AXES, None),
        ),
        out_specs=(P(SUB_AXES, None), P(SUB_AXES, None, TP_AXES)),
        check_vma=False,
    )
```

```python
import jax
import jax.numpy as jnp
from jax import lax
from jax.experimental import pallas as pl
from jax.experimental.pallas import tpu as pltpu
from jax.sharding import Mesh
from jax.sharding import PartitionSpec as P

HEAD_DIM = 64
EXPERTS = 32
SEG_VALUES = 8
KEY_CHUNK = 1024

EPS = 1e-06
SCORE_SCALE = 0.015625
SUB_AXES = ("sy", "sz", "sx")
TP_AXES = ("tz", "tc")


def normalize(values, gain):
    widened = values.astype(jnp.float32)
    return (
        widened
        * lax.rsqrt(jnp.mean(widened * widened, axis=-1, keepdims=True) + EPS)
        * gain.astype(jnp.float32)
    )


def rotary(tensor, positions):
    half_dim = tensor.shape[-1] // 2
    frequencies = 10000.0 ** (-jnp.arange(half_dim, dtype=jnp.float32) * 2.0 / tensor.shape[-1])
    angles = positions.astype(jnp.float32)[:, None] * frequencies[None, :]
    cosine = jnp.cos(angles)[:, None, :]
    sine_part = jnp.sin(angles)[:, None, :]
    lower_half = tensor[..., :half_dim]
    upper_half = tensor[..., half_dim:]
    return jnp.concatenate(
        [
            lower_half * cosine - upper_half * sine_part,
            upper_half * cosine + lower_half * sine_part,
        ],
        axis=-1,
    )


def attention_kernel(bounds_ref, q_ref, k_ref, v_ref, kseg_ref, qseg_ref, qidx_ref, o_ref, m_sc, l_sc, acc_sc):
    step = pl.program_id(0)
    kv_heads, group_size = q_ref.shape[0], q_ref.shape[1]

    @pl.when(step == 0)
    def _():
        m_sc[...] = jnp.full(m_sc.shape, -1e30, jnp.float32)
        l_sc[...] = jnp.zeros(l_sc.shape, jnp.float32)
        acc_sc[...] = jnp.zeros(acc_sc.shape, jnp.float32)

    chunk = bounds_ref[0] + step

    @pl.when(chunk <= bounds_ref[1])
    def _():
        key_index = chunk * KEY_CHUNK + lax.broadcasted_iota(jnp.int32, (1, KEY_CHUNK), 1)
        allowed = (qseg_ref[...] == kseg_ref[0]) & (qidx_ref[...] >= key_index)
        key_rows = k_ref[...]
        value_rows = v_ref[...]
        for head in range(kv_heads):
            for member in range(group_size):
                slot = head * group_size + member
                scores = (
                    lax.dot_general(
                        q_ref[head, member],
                        key_rows,
                        (((1,), (1,)), ((), ())),
                        preferred_element_type=jnp.float32,
                    )
                    * SCORE_SCALE
                )
                masked = jnp.where(allowed, scores, -1e30)
                running_max = m_sc[slot]
                new_max = jnp.maximum(running_max, jnp.max(masked, axis=-1, keepdims=True))
                weights = jnp.where(allowed, jnp.exp(masked - new_max), 0.0)
                factor = jnp.exp(running_max - new_max)
                l_sc[slot] = l_sc[slot] * factor + jnp.sum(weights, axis=-1, keepdims=True)
                acc_sc[slot] = acc_sc[slot] * factor + jnp.dot(
                    weights.astype(jnp.bfloat16), value_rows, preferred_element_type=jnp.float32
                )
                m_sc[slot] = new_max

    @pl.when(step == pl.num_programs(0) - 1)
    def _():
        o_ref[...] = acc_sc[...] / l_sc[...]


def chunk_attention(queries, joined, segment_ids, own_segs, query_index, first_chunk, last_chunk):
    kv_heads, group_size, tokens, head_dim = queries.shape
    total, both_width = joined.shape
    kv_width = both_width // 2
    chunks = total // KEY_CHUNK
    head_mask = jnp.eye(kv_heads, dtype=jnp.bool_)[:, None, None, :, None]
    padded_queries = jnp.where(head_mask, queries[:, :, :, None, :], jnp.zeros((), queries.dtype)).reshape(
        kv_heads, group_size, tokens, kv_width
    )
    bounds = jnp.stack([first_chunk, last_chunk]).astype(jnp.int32)

    def key_map(step, bounds_ref):
        return (jnp.minimum(bounds_ref[0] + step, bounds_ref[1]), 0)

    def value_map(step, bounds_ref):
        return (jnp.minimum(bounds_ref[0] + step, bounds_ref[1]), 1)

    def seg_map(step, bounds_ref):
        return (jnp.minimum(bounds_ref[0] + step, bounds_ref[1]), 0, 0)

    def whole(step, bounds_ref):
        return (0, 0, 0, 0)

    def whole2(step, bounds_ref):
        return (0, 0)

    def whole3(step, bounds_ref):
        return (0, 0, 0)

    spec = pltpu.PrefetchScalarGridSpec(
        num_scalar_prefetch=1,
        grid=(chunks,),
        in_specs=[
            pl.BlockSpec((kv_heads, group_size, tokens, kv_width), whole),
            pl.BlockSpec((KEY_CHUNK, kv_width), key_map),
            pl.BlockSpec((KEY_CHUNK, kv_width), value_map),
            pl.BlockSpec((1, 1, KEY_CHUNK), seg_map),
            pl.BlockSpec((tokens, 1), whole2),
            pl.BlockSpec((tokens, 1), whole2),
        ],
        out_specs=pl.BlockSpec((kv_heads * group_size, tokens, kv_width), whole3),
        scratch_shapes=[
            pltpu.VMEM((kv_heads * group_size, tokens, 1), jnp.float32),
            pltpu.VMEM((kv_heads * group_size, tokens, 1), jnp.float32),
            pltpu.VMEM((kv_heads * group_size, tokens, kv_width), jnp.float32),
        ],
    )
    out = pl.pallas_call(
        attention_kernel,
        grid_spec=spec,
        out_shape=jax.ShapeDtypeStruct((kv_heads * group_size, tokens, kv_width), jnp.float32),
        compiler_params=pltpu.CompilerParams(dimension_semantics=("arbitrary",)),
    )(
        bounds,
        padded_queries,
        joined,
        joined,
        segment_ids.reshape(chunks, 1, KEY_CHUNK),
        own_segs.reshape(tokens, 1),
        query_index.reshape(tokens, 1),
    )
    out = out.reshape(kv_heads, group_size, tokens, kv_heads, head_dim)
    return jnp.stack([out[head, :, :, head] for head in range(kv_heads)])


def tp_sum(partial):
    swap = [(0, 1), (1, 0)]
    pair = partial.astype(jnp.float32) + lax.ppermute(partial, "tc", swap).astype(jnp.float32)
    pair = pair.astype(jnp.bfloat16)
    return pair.astype(jnp.float32) + lax.ppermute(pair, "tz", swap).astype(jnp.float32)


def per_device(
    hidden,
    segment_ids,
    routes,
    gates,
    norm_attn,
    norm_moe,
    w_query,
    w_key,
    w_value,
    w_out,
    w_gate,
    w_up,
    w_down,
):
    tokens = hidden.shape[0]
    model_width = hidden.shape[1]
    total_tokens = segment_ids.shape[0]
    first_row = lax.axis_index(SUB_AXES) * tokens
    own_segs = lax.dynamic_slice_in_dim(segment_ids, first_row, tokens)
    seg_starts = jnp.sum(
        (segment_ids[None, :] < jnp.arange(SEG_VALUES, dtype=jnp.int32)[:, None]).astype(jnp.int32),
        axis=1,
    )
    query_index = first_row + jnp.arange(tokens, dtype=jnp.int32)
    positions = query_index - seg_starts[own_segs]
    normed = normalize(hidden, norm_attn).astype(jnp.bfloat16)
    query_heads = w_query.shape[1] // HEAD_DIM
    kv_heads = w_key.shape[1] // HEAD_DIM
    group_size = query_heads // kv_heads
    queries = jnp.dot(normed, w_query, preferred_element_type=jnp.float32).reshape(
        tokens, query_heads, HEAD_DIM
    )
    queries = (
        rotary(queries, positions)
        .astype(jnp.bfloat16)
        .reshape(tokens, kv_heads, group_size, HEAD_DIM)
        .transpose(1, 2, 0, 3)
    )
    key_raw = jnp.dot(normed, w_key, preferred_element_type=jnp.float32).reshape(
        tokens, kv_heads, HEAD_DIM
    )
    value_proj = jnp.dot(normed, w_value, preferred_element_type=jnp.float32).astype(jnp.bfloat16)
    kv_cache = jnp.stack(
        [key_raw.reshape(tokens, kv_heads * HEAD_DIM).astype(jnp.bfloat16), value_proj], axis=1
    )
    key_rot = rotary(key_raw, positions).astype(jnp.bfloat16)
    kv_width = kv_heads * HEAD_DIM
    joined = jnp.concatenate([key_rot.reshape(tokens, kv_width), value_proj], axis=1)
    for axis_name in SUB_AXES[::-1]:
        joined = lax.all_gather(joined, axis_name, axis=0, tiled=True)
    last_query = first_row + tokens - 1
    lowest_seg = own_segs[0]
    chunk_ends = segment_ids[KEY_CHUNK - 1 :: KEY_CHUNK]
    first_chunk = jnp.sum((chunk_ends < lowest_seg).astype(jnp.int32))
    last_chunk = last_query // KEY_CHUNK

    route_count = routes.shape[1]
    slots_dev = w_gate.shape[0]
    seq_count = lax.axis_size(SUB_AXES)
    slot_total = slots_dev * seq_count
    copies = slot_total // EXPERTS
    block_rows = tokens // copies
    capacity = 2 * block_rows * route_count // EXPERTS
    copy_of = (jnp.arange(tokens, dtype=jnp.int32) // block_rows)[:, None]
    slot_of = routes + EXPERTS * copy_of
    flat_expert = routes.reshape(copies, block_rows * route_count)
    onehot = (
        flat_expert[:, :, None] == jnp.arange(EXPERTS, dtype=jnp.int32)[None, None, :]
    ).astype(jnp.bfloat16)
    flat_rows = block_rows * route_count
    strictly_before = (
        jnp.arange(flat_rows, dtype=jnp.int32)[None, :] < jnp.arange(flat_rows, dtype=jnp.int32)[:, None]
    ).astype(jnp.bfloat16)
    before = jnp.einsum("ij,cje->cie", strictly_before, onehot, preferred_element_type=jnp.float32)
    slot_rank = (
        jnp.sum(before * onehot.astype(jnp.float32), axis=2).astype(jnp.int32).reshape(tokens, route_count)
    )
    half = capacity // 2
    core = lax.axis_index("tc")
    swap = [(0, 1), (1, 0)]
    own_route = (slot_rank // half) == core
    local_target = jnp.where(own_route, slot_of * half + slot_rank - core * half, -1)
    row_ids = jnp.arange(slot_total * half, dtype=jnp.int32)
    picks = local_target.T[:, None, :] == row_ids[None, :, None]
    dispatch = jnp.any(picks, axis=0).astype(jnp.bfloat16)
    joined, local_target, dispatch = lax.optimization_barrier((joined, local_target, dispatch))
    attended = chunk_attention(
        queries, joined, segment_ids, own_segs, query_index, first_chunk, last_chunk
    )
    attended = (
        attended.transpose(2, 0, 1, 3)
        .reshape(tokens, query_heads * HEAD_DIM)
    )
    attended = attended.astype(jnp.bfloat16)
    partial_out = jnp.dot(attended, w_out, preferred_element_type=jnp.float32)
    attn_mixed = tp_sum(partial_out.astype(jnp.bfloat16))
    residual = (hidden.astype(jnp.float32) + attn_mixed).astype(jnp.bfloat16)
    normed_moe = normalize(residual, norm_moe).astype(jnp.bfloat16)
    outbound = jnp.dot(dispatch, normed_moe, preferred_element_type=jnp.float32).astype(jnp.bfloat16)
    outbound = outbound.reshape(seq_count, slots_dev, half, model_width)
    arrived_own = lax.all_to_all(outbound, SUB_AXES, split_axis=0, concat_axis=0, tiled=True)
    arrived_other = lax.ppermute(arrived_own, "tc", swap)
    def expert_rows(arrived):
        gate_val = jnp.einsum("jsrd,sdf->jsrf", arrived, w_gate, preferred_element_type=jnp.float32)
        up_val = jnp.einsum("jsrd,sdf->jsrf", arrived, w_up, preferred_element_type=jnp.float32)
        activated = (jax.nn.silu(gate_val) * up_val).astype(jnp.bfloat16)
        group_part = jnp.einsum("jsrf,sfd->jsrd", activated, w_down, preferred_element_type=jnp.float32)
        return group_part.astype(jnp.bfloat16)

    sibling_part = lax.ppermute(expert_rows(arrived_other), "tc", swap)
    own_part = expert_rows(arrived_own)
    pair_sum = (own_part.astype(jnp.float32) + sibling_part.astype(jnp.float32)).astype(
        jnp.bfloat16
    )
    returned = lax.all_to_all(pair_sum, SUB_AXES, split_axis=0, concat_axis=0, tiled=True).reshape(
        slot_total * half, model_width
    )
    weighting = jnp.sum(
        jnp.where(local_target.T[:, :, None] == row_ids[None, None, :], gates.T[:, :, None], 0.0),
        axis=0,
    )
    combined = jnp.dot(
        weighting, returned, preferred_element_type=jnp.float32, precision=lax.Precision.HIGHEST
    )
    expert_sum = tp_sum(combined.astype(jnp.bfloat16))
    hidden_out = (residual.astype(jnp.float32) + expert_sum).astype(jnp.bfloat16)
    return (hidden_out, kv_cache)


def solution(mesh):
    seq_size, tp_size = mesh.devices.shape
    side = round(seq_size ** (1 / 3))
    sub_mesh = Mesh(
        mesh.devices.reshape(side, side, seq_size // side // side, tp_size // 2, 2), SUB_AXES + TP_AXES
    )
    return jax.shard_map(
        per_device,
        mesh=sub_mesh,
        in_specs=(
            P(SUB_AXES, None),
            P(),
            P(SUB_AXES, None),
            P(SUB_AXES, None),
            P(),
            P(),
            P(None, TP_AXES),
            P(None, TP_AXES),
            P(None, TP_AXES),
            P(TP_AXES, None),
            P(SUB_AXES, None, TP_AXES),
            P(SUB_AXES, None, TP_AXES),
            P(SUB_AXES, TP_AXES, None),
        ),
        out_specs=(P(SUB_AXES, None), P(SUB_AXES, None, TP_AXES)),
        check_vma=False,
    )
```

```python
import jax
import jax.numpy as jnp
from jax import lax
from jax.experimental import pallas as pl
from jax.experimental.pallas import tpu as pltpu
from jax.sharding import Mesh
from jax.sharding import PartitionSpec as P

HEAD_DIM = 64
EXPERTS = 32
SEG_VALUES = 8
KEY_CHUNK = 1024

EPS = 1e-06
SCORE_SCALE = 0.015625
SUB_AXES = ("sy", "sz", "sx")
TP_AXES = ("tz", "tc")


def normalize(values, gain):
    widened = values.astype(jnp.float32)
    return (
        widened
        * lax.rsqrt(jnp.mean(widened * widened, axis=-1, keepdims=True) + EPS)
        * gain.astype(jnp.float32)
    )


def rotary(tensor, positions):
    half_dim = tensor.shape[-1] // 2
    frequencies = 10000.0 ** (-jnp.arange(half_dim, dtype=jnp.float32) * 2.0 / tensor.shape[-1])
    angles = positions.astype(jnp.float32)[:, None] * frequencies[None, :]
    cosine = jnp.cos(angles)[:, None, :]
    sine_part = jnp.sin(angles)[:, None, :]
    lower_half = tensor[..., :half_dim]
    upper_half = tensor[..., half_dim:]
    return jnp.concatenate(
        [
            lower_half * cosine - upper_half * sine_part,
            upper_half * cosine + lower_half * sine_part,
        ],
        axis=-1,
    )


def attention_kernel(bounds_ref, q_ref, k_ref, v_ref, kseg_ref, qseg_ref, qidx_ref, o_ref, m_sc, l_sc, acc_sc):
    step = pl.program_id(0)
    kv_heads, group_size = q_ref.shape[0], q_ref.shape[1]

    @pl.when(step == 0)
    def _():
        m_sc[...] = jnp.full(m_sc.shape, -1e30, jnp.float32)
        l_sc[...] = jnp.zeros(l_sc.shape, jnp.float32)
        acc_sc[...] = jnp.zeros(acc_sc.shape, jnp.float32)

    chunk = bounds_ref[0] + step

    @pl.when(chunk <= bounds_ref[1])
    def _():
        key_index = chunk * KEY_CHUNK + lax.broadcasted_iota(jnp.int32, (1, KEY_CHUNK), 1)
        allowed = (qseg_ref[...] == kseg_ref[0]) & (qidx_ref[...] >= key_index)
        key_rows = k_ref[...]
        value_rows = v_ref[...]
        for head in range(kv_heads):
            for member in range(group_size):
                slot = head * group_size + member
                scores = (
                    lax.dot_general(
                        q_ref[head, member],
                        key_rows,
                        (((1,), (1,)), ((), ())),
                        preferred_element_type=jnp.float32,
                    )
                    * SCORE_SCALE
                )
                masked = jnp.where(allowed, scores, -1e30)
                running_max = m_sc[slot]
                new_max = jnp.maximum(running_max, jnp.max(masked, axis=-1, keepdims=True))
                weights = jnp.where(allowed, jnp.exp(masked - new_max), 0.0)
                factor = jnp.exp(running_max - new_max)
                l_sc[slot] = l_sc[slot] * factor + jnp.sum(weights, axis=-1, keepdims=True)
                acc_sc[slot] = acc_sc[slot] * factor + jnp.dot(
                    weights.astype(jnp.bfloat16), value_rows, preferred_element_type=jnp.float32
                )
                m_sc[slot] = new_max

    @pl.when(step == pl.num_programs(0) - 1)
    def _():
        o_ref[...] = acc_sc[...] / l_sc[...]


def chunk_attention(queries, joined, segment_ids, own_segs, query_index, first_chunk, last_chunk):
    kv_heads, group_size, tokens, head_dim = queries.shape
    total, both_width = joined.shape
    kv_width = both_width // 2
    chunks = total // KEY_CHUNK
    head_mask = jnp.eye(kv_heads, dtype=jnp.bool_)[:, None, None, :, None]
    padded_queries = jnp.where(head_mask, queries[:, :, :, None, :], jnp.zeros((), queries.dtype)).reshape(
        kv_heads, group_size, tokens, kv_width
    )
    bounds = jnp.stack([first_chunk, last_chunk]).astype(jnp.int32)

    def key_map(step, bounds_ref):
        return (jnp.minimum(bounds_ref[0] + step, bounds_ref[1]), 0)

    def value_map(step, bounds_ref):
        return (jnp.minimum(bounds_ref[0] + step, bounds_ref[1]), 1)

    def seg_map(step, bounds_ref):
        return (jnp.minimum(bounds_ref[0] + step, bounds_ref[1]), 0, 0)

    def whole(step, bounds_ref):
        return (0, 0, 0, 0)

    def whole2(step, bounds_ref):
        return (0, 0)

    def whole3(step, bounds_ref):
        return (0, 0, 0)

    spec = pltpu.PrefetchScalarGridSpec(
        num_scalar_prefetch=1,
        grid=(chunks,),
        in_specs=[
            pl.BlockSpec((kv_heads, group_size, tokens, kv_width), whole),
            pl.BlockSpec((KEY_CHUNK, kv_width), key_map),
            pl.BlockSpec((KEY_CHUNK, kv_width), value_map),
            pl.BlockSpec((1, 1, KEY_CHUNK), seg_map),
            pl.BlockSpec((tokens, 1), whole2),
            pl.BlockSpec((tokens, 1), whole2),
        ],
        out_specs=pl.BlockSpec((kv_heads * group_size, tokens, kv_width), whole3),
        scratch_shapes=[
            pltpu.VMEM((kv_heads * group_size, tokens, 1), jnp.float32),
            pltpu.VMEM((kv_heads * group_size, tokens, 1), jnp.float32),
            pltpu.VMEM((kv_heads * group_size, tokens, kv_width), jnp.float32),
        ],
    )
    out = pl.pallas_call(
        attention_kernel,
        grid_spec=spec,
        out_shape=jax.ShapeDtypeStruct((kv_heads * group_size, tokens, kv_width), jnp.float32),
        compiler_params=pltpu.CompilerParams(dimension_semantics=("arbitrary",)),
    )(
        bounds,
        padded_queries,
        joined,
        joined,
        segment_ids.reshape(chunks, 1, KEY_CHUNK),
        own_segs.reshape(tokens, 1),
        query_index.reshape(tokens, 1),
    )
    out = out.reshape(kv_heads, group_size, tokens, kv_heads, head_dim)
    return jnp.stack([out[head, :, :, head] for head in range(kv_heads)])


def tp_sum(partial):
    swap = [(0, 1), (1, 0)]
    core = lax.axis_index("tc")
    rows, width = partial.shape
    halves = partial.reshape(rows, 2, width // 2)
    mine = lax.dynamic_index_in_dim(halves, core, axis=1, keepdims=False)
    theirs = lax.dynamic_index_in_dim(halves, 1 - core, axis=1, keepdims=False)
    pair = mine.astype(jnp.float32) + lax.ppermute(theirs, "tc", swap).astype(jnp.float32)
    pair = pair.astype(jnp.bfloat16)
    summed = pair.astype(jnp.float32) + lax.ppermute(pair, "tz", swap).astype(jnp.float32)
    other = lax.ppermute(summed, "tc", swap)
    return jnp.where(
        core == 0,
        jnp.concatenate([summed, other], axis=1),
        jnp.concatenate([other, summed], axis=1),
    )


def per_device(
    hidden,
    segment_ids,
    routes,
    gates,
    norm_attn,
    norm_moe,
    w_query,
    w_key,
    w_value,
    w_out,
    w_gate,
    w_up,
    w_down,
):
    tokens = hidden.shape[0]
    model_width = hidden.shape[1]
    total_tokens = segment_ids.shape[0]
    first_row = lax.axis_index(SUB_AXES) * tokens
    own_segs = lax.dynamic_slice_in_dim(segment_ids, first_row, tokens)
    seg_starts = jnp.sum(
        (segment_ids[None, :] < jnp.arange(SEG_VALUES, dtype=jnp.int32)[:, None]).astype(jnp.int32),
        axis=1,
    )
    query_index = first_row + jnp.arange(tokens, dtype=jnp.int32)
    positions = query_index - seg_starts[own_segs]
    normed = normalize(hidden, norm_attn).astype(jnp.bfloat16)
    query_heads = w_query.shape[1] // HEAD_DIM
    kv_heads = w_key.shape[1] // HEAD_DIM
    group_size = query_heads // kv_heads
    queries = jnp.dot(normed, w_query, preferred_element_type=jnp.float32).reshape(
        tokens, query_heads, HEAD_DIM
    )
    queries = (
        rotary(queries, positions)
        .astype(jnp.bfloat16)
        .reshape(tokens, kv_heads, group_size, HEAD_DIM)
        .transpose(1, 2, 0, 3)
    )
    key_raw = jnp.dot(normed, w_key, preferred_element_type=jnp.float32).reshape(
        tokens, kv_heads, HEAD_DIM
    )
    value_proj = jnp.dot(normed, w_value, preferred_element_type=jnp.float32).astype(jnp.bfloat16)
    kv_cache = jnp.stack(
        [key_raw.reshape(tokens, kv_heads * HEAD_DIM).astype(jnp.bfloat16), value_proj], axis=1
    )
    key_rot = rotary(key_raw, positions).astype(jnp.bfloat16)
    kv_width = kv_heads * HEAD_DIM
    joined = jnp.concatenate([key_rot.reshape(tokens, kv_width), value_proj], axis=1)
    for axis_name in SUB_AXES[::-1]:
        joined = lax.all_gather(joined, axis_name, axis=0, tiled=True)
    last_query = first_row + tokens - 1
    lowest_seg = own_segs[0]
    chunk_ends = segment_ids[KEY_CHUNK - 1 :: KEY_CHUNK]
    first_chunk = jnp.sum((chunk_ends < lowest_seg).astype(jnp.int32))
    last_chunk = last_query // KEY_CHUNK

    route_count = routes.shape[1]
    slots_dev = w_gate.shape[0]
    seq_count = lax.axis_size(SUB_AXES)
    slot_total = slots_dev * seq_count
    copies = slot_total // EXPERTS
    block_rows = tokens // copies
    capacity = 2 * block_rows * route_count // EXPERTS
    copy_of = (jnp.arange(tokens, dtype=jnp.int32) // block_rows)[:, None]
    slot_of = routes + EXPERTS * copy_of
    flat_expert = routes.reshape(copies, block_rows * route_count)
    onehot = (
        flat_expert[:, :, None] == jnp.arange(EXPERTS, dtype=jnp.int32)[None, None, :]
    ).astype(jnp.bfloat16)
    flat_rows = block_rows * route_count
    strictly_before = (
        jnp.arange(flat_rows, dtype=jnp.int32)[None, :] < jnp.arange(flat_rows, dtype=jnp.int32)[:, None]
    ).astype(jnp.bfloat16)
    before = jnp.einsum("ij,cje->cie", strictly_before, onehot, preferred_element_type=jnp.float32)
    slot_rank = (
        jnp.sum(before * onehot.astype(jnp.float32), axis=2).astype(jnp.int32).reshape(tokens, route_count)
    )
    half = capacity // 2
    core = lax.axis_index("tc")
    swap = [(0, 1), (1, 0)]
    own_route = (slot_rank // half) == core
    local_target = jnp.where(own_route, slot_of * half + slot_rank - core * half, -1)
    row_ids = jnp.arange(slot_total * half, dtype=jnp.int32)
    picks = local_target.T[:, None, :] == row_ids[None, :, None]
    dispatch = jnp.any(picks, axis=0).astype(jnp.bfloat16)
    joined, local_target, dispatch = lax.optimization_barrier((joined, local_target, dispatch))
    attended = chunk_attention(
        queries, joined, segment_ids, own_segs, query_index, first_chunk, last_chunk
    )
    attended = (
        attended.transpose(2, 0, 1, 3)
        .reshape(tokens, query_heads * HEAD_DIM)
    )
    attended = attended.astype(jnp.bfloat16)
    partial_out = jnp.dot(attended, w_out, preferred_element_type=jnp.float32)
    attn_mixed = tp_sum(partial_out.astype(jnp.bfloat16))
    residual = (hidden.astype(jnp.float32) + attn_mixed).astype(jnp.bfloat16)
    normed_moe = normalize(residual, norm_moe).astype(jnp.bfloat16)
    outbound = jnp.dot(dispatch, normed_moe, preferred_element_type=jnp.float32).astype(jnp.bfloat16)
    outbound = outbound.reshape(seq_count, slots_dev, half, model_width)
    arrived_own = lax.all_to_all(outbound, SUB_AXES, split_axis=0, concat_axis=0, tiled=True)
    arrived_other = lax.ppermute(arrived_own, "tc", swap)
    def expert_rows(arrived):
        gate_val = jnp.einsum("jsrd,sdf->jsrf", arrived, w_gate, preferred_element_type=jnp.float32)
        up_val = jnp.einsum("jsrd,sdf->jsrf", arrived, w_up, preferred_element_type=jnp.float32)
        activated = (jax.nn.silu(gate_val) * up_val).astype(jnp.bfloat16)
        group_part = jnp.einsum("jsrf,sfd->jsrd", activated, w_down, preferred_element_type=jnp.float32)
        return group_part.astype(jnp.bfloat16)

    sibling_part = lax.ppermute(expert_rows(arrived_other), "tc", swap)
    own_part = expert_rows(arrived_own)
    pair_sum = (own_part.astype(jnp.float32) + sibling_part.astype(jnp.float32)).astype(
        jnp.bfloat16
    )
    returned = lax.all_to_all(pair_sum, SUB_AXES, split_axis=0, concat_axis=0, tiled=True).reshape(
        slot_total * half, model_width
    )
    weighting = jnp.sum(
        jnp.where(local_target.T[:, :, None] == row_ids[None, None, :], gates.T[:, :, None], 0.0),
        axis=0,
    )
    combined = jnp.dot(
        weighting, returned, preferred_element_type=jnp.float32, precision=lax.Precision.HIGHEST
    )
    expert_sum = tp_sum(combined.astype(jnp.bfloat16))
    hidden_out = (residual.astype(jnp.float32) + expert_sum).astype(jnp.bfloat16)
    return (hidden_out, kv_cache)


def solution(mesh):
    seq_size, tp_size = mesh.devices.shape
    side = round(seq_size ** (1 / 3))
    sub_mesh = Mesh(
        mesh.devices.reshape(side, side, seq_size // side // side, tp_size // 2, 2), SUB_AXES + TP_AXES
    )
    return jax.shard_map(
        per_device,
        mesh=sub_mesh,
        in_specs=(
            P(SUB_AXES, None),
            P(),
            P(SUB_AXES, None),
            P(SUB_AXES, None),
            P(),
            P(),
            P(None, TP_AXES),
            P(None, TP_AXES),
            P(None, TP_AXES),
            P(TP_AXES, None),
            P(SUB_AXES, None, TP_AXES),
            P(SUB_AXES, None, TP_AXES),
            P(SUB_AXES, TP_AXES, None),
        ),
        out_specs=(P(SUB_AXES, None), P(SUB_AXES, None, TP_AXES)),
        check_vma=False,
    )
```

```python
import jax
import jax.numpy as jnp
from jax import lax
from jax.experimental import pallas as pl
from jax.experimental.pallas import tpu as pltpu
from jax.sharding import Mesh
from jax.sharding import PartitionSpec as P

HEAD_DIM = 64
EXPERTS = 32
SEG_VALUES = 8
KEY_CHUNK = 1024

EPS = 1e-06
SCORE_SCALE = 0.015625
SUB_AXES = ("sy", "sz", "sx")
TP_AXES = ("tz", "tc")


def normalize(values, gain):
    widened = values.astype(jnp.float32)
    return (
        widened
        * lax.rsqrt(jnp.mean(widened * widened, axis=-1, keepdims=True) + EPS)
        * gain.astype(jnp.float32)
    )


def rotary(tensor, positions):
    half_dim = tensor.shape[-1] // 2
    frequencies = 10000.0 ** (-jnp.arange(half_dim, dtype=jnp.float32) * 2.0 / tensor.shape[-1])
    angles = positions.astype(jnp.float32)[:, None] * frequencies[None, :]
    cosine = jnp.cos(angles)[:, None, :]
    sine_part = jnp.sin(angles)[:, None, :]
    lower_half = tensor[..., :half_dim]
    upper_half = tensor[..., half_dim:]
    return jnp.concatenate(
        [
            lower_half * cosine - upper_half * sine_part,
            upper_half * cosine + lower_half * sine_part,
        ],
        axis=-1,
    )


def attention_kernel(bounds_ref, q_ref, k_ref, v_ref, kseg_ref, qseg_ref, qidx_ref, o_ref, m_sc, l_sc, acc_sc):
    step = pl.program_id(0)
    kv_heads, group_size = q_ref.shape[0], q_ref.shape[1]

    @pl.when(step == 0)
    def _():
        m_sc[...] = jnp.full(m_sc.shape, -1e30, jnp.float32)
        l_sc[...] = jnp.zeros(l_sc.shape, jnp.float32)
        acc_sc[...] = jnp.zeros(acc_sc.shape, jnp.float32)

    chunk = bounds_ref[0] + step

    @pl.when(chunk <= bounds_ref[1])
    def _():
        key_index = chunk * KEY_CHUNK + lax.broadcasted_iota(jnp.int32, (1, KEY_CHUNK), 1)
        allowed = (qseg_ref[...] == kseg_ref[0]) & (qidx_ref[...] >= key_index)
        key_rows = k_ref[...]
        value_rows = v_ref[...]
        for head in range(kv_heads):
            for member in range(group_size):
                slot = head * group_size + member
                scores = (
                    lax.dot_general(
                        q_ref[head, member],
                        key_rows,
                        (((1,), (1,)), ((), ())),
                        preferred_element_type=jnp.float32,
                    )
                    * SCORE_SCALE
                )
                masked = jnp.where(allowed, scores, -1e30)
                running_max = m_sc[slot]
                new_max = jnp.maximum(running_max, jnp.max(masked, axis=-1, keepdims=True))
                weights = jnp.where(allowed, jnp.exp(masked - new_max), 0.0)
                factor = jnp.exp(running_max - new_max)
                l_sc[slot] = l_sc[slot] * factor + jnp.sum(weights, axis=-1, keepdims=True)
                acc_sc[slot] = acc_sc[slot] * factor + jnp.dot(
                    weights.astype(jnp.bfloat16), value_rows, preferred_element_type=jnp.float32
                )
                m_sc[slot] = new_max

    @pl.when(step == pl.num_programs(0) - 1)
    def _():
        o_ref[...] = acc_sc[...] / l_sc[...]


def chunk_attention(queries, joined, segment_ids, own_segs, query_index, first_chunk, last_chunk):
    kv_heads, group_size, tokens, head_dim = queries.shape
    total, both_width = joined.shape
    kv_width = both_width // 2
    chunks = total // KEY_CHUNK
    head_mask = jnp.eye(kv_heads, dtype=jnp.bool_)[:, None, None, :, None]
    padded_queries = jnp.where(head_mask, queries[:, :, :, None, :], jnp.zeros((), queries.dtype)).reshape(
        kv_heads, group_size, tokens, kv_width
    )
    bounds = jnp.stack([first_chunk, last_chunk]).astype(jnp.int32)

    def key_map(step, bounds_ref):
        return (jnp.minimum(bounds_ref[0] + step, bounds_ref[1]), 0)

    def value_map(step, bounds_ref):
        return (jnp.minimum(bounds_ref[0] + step, bounds_ref[1]), 1)

    def seg_map(step, bounds_ref):
        return (jnp.minimum(bounds_ref[0] + step, bounds_ref[1]), 0, 0)

    def whole(step, bounds_ref):
        return (0, 0, 0, 0)

    def whole2(step, bounds_ref):
        return (0, 0)

    def whole3(step, bounds_ref):
        return (0, 0, 0)

    spec = pltpu.PrefetchScalarGridSpec(
        num_scalar_prefetch=1,
        grid=(chunks,),
        in_specs=[
            pl.BlockSpec((kv_heads, group_size, tokens, kv_width), whole),
            pl.BlockSpec((KEY_CHUNK, kv_width), key_map),
            pl.BlockSpec((KEY_CHUNK, kv_width), value_map),
            pl.BlockSpec((1, 1, KEY_CHUNK), seg_map),
            pl.BlockSpec((tokens, 1), whole2),
            pl.BlockSpec((tokens, 1), whole2),
        ],
        out_specs=pl.BlockSpec((kv_heads * group_size, tokens, kv_width), whole3),
        scratch_shapes=[
            pltpu.VMEM((kv_heads * group_size, tokens, 1), jnp.float32),
            pltpu.VMEM((kv_heads * group_size, tokens, 1), jnp.float32),
            pltpu.VMEM((kv_heads * group_size, tokens, kv_width), jnp.float32),
        ],
    )
    out = pl.pallas_call(
        attention_kernel,
        grid_spec=spec,
        out_shape=jax.ShapeDtypeStruct((kv_heads * group_size, tokens, kv_width), jnp.float32),
        compiler_params=pltpu.CompilerParams(dimension_semantics=("arbitrary",)),
    )(
        bounds,
        padded_queries,
        joined,
        joined,
        segment_ids.reshape(chunks, 1, KEY_CHUNK),
        own_segs.reshape(tokens, 1),
        query_index.reshape(tokens, 1),
    )
    out = out.reshape(kv_heads, group_size, tokens, kv_heads, head_dim)
    return jnp.stack([out[head, :, :, head] for head in range(kv_heads)])


def tp_sum(partial):
    swap = [(0, 1), (1, 0)]
    core = lax.axis_index("tc")
    rows, width = partial.shape
    halves = partial.reshape(rows, 2, width // 2)
    mine = lax.dynamic_index_in_dim(halves, core, axis=1, keepdims=False)
    theirs = lax.dynamic_index_in_dim(halves, 1 - core, axis=1, keepdims=False)
    pair = mine.astype(jnp.float32) + lax.ppermute(theirs, "tc", swap).astype(jnp.float32)
    pair = pair.astype(jnp.bfloat16)
    summed = pair.astype(jnp.float32) + lax.ppermute(pair, "tz", swap).astype(jnp.float32)
    other = lax.ppermute(summed, "tc", swap)
    return jnp.where(
        core == 0,
        jnp.concatenate([summed, other], axis=1),
        jnp.concatenate([other, summed], axis=1),
    )


def per_device(
    hidden,
    segment_ids,
    routes,
    gates,
    norm_attn,
    norm_moe,
    w_query,
    w_key,
    w_value,
    w_out,
    w_gate,
    w_up,
    w_down,
):
    tokens = hidden.shape[0]
    model_width = hidden.shape[1]
    total_tokens = segment_ids.shape[0]
    first_row = lax.axis_index(SUB_AXES) * tokens
    own_segs = lax.dynamic_slice_in_dim(segment_ids, first_row, tokens)
    seg_starts = jnp.sum(
        (segment_ids[None, :] < jnp.arange(SEG_VALUES, dtype=jnp.int32)[:, None]).astype(jnp.int32),
        axis=1,
    )
    query_index = first_row + jnp.arange(tokens, dtype=jnp.int32)
    positions = query_index - seg_starts[own_segs]
    normed = normalize(hidden, norm_attn).astype(jnp.bfloat16)
    query_heads = w_query.shape[1] // HEAD_DIM
    kv_heads = w_key.shape[1] // HEAD_DIM
    group_size = query_heads // kv_heads
    queries = jnp.dot(normed, w_query, preferred_element_type=jnp.float32).reshape(
        tokens, query_heads, HEAD_DIM
    )
    queries = (
        rotary(queries, positions)
        .astype(jnp.bfloat16)
        .reshape(tokens, kv_heads, group_size, HEAD_DIM)
        .transpose(1, 2, 0, 3)
    )
    key_raw = jnp.dot(normed, w_key, preferred_element_type=jnp.float32).reshape(
        tokens, kv_heads, HEAD_DIM
    )
    value_proj = jnp.dot(normed, w_value, preferred_element_type=jnp.float32).astype(jnp.bfloat16)
    kv_cache = jnp.stack(
        [key_raw.reshape(tokens, kv_heads * HEAD_DIM).astype(jnp.bfloat16), value_proj], axis=1
    )
    key_rot = rotary(key_raw, positions).astype(jnp.bfloat16)
    kv_width = kv_heads * HEAD_DIM
    joined = jnp.concatenate([key_rot.reshape(tokens, kv_width), value_proj], axis=1)
    for axis_name in ("sx", "sz"):
        coordinate = lax.axis_index(axis_name)
        shifted = [joined] + [
            lax.ppermute(joined, axis_name, [(j, (j + k) % 4) for j in range(4)]) for k in (1, 2, 3)
        ]
        order = (coordinate - jnp.arange(4, dtype=jnp.int32)) % 4
        joined = jnp.take(jnp.stack(shifted), order, axis=0).reshape(-1, joined.shape[1])
    joined = lax.all_gather(joined, "sy", axis=0, tiled=True)
    last_query = first_row + tokens - 1
    lowest_seg = own_segs[0]
    chunk_ends = segment_ids[KEY_CHUNK - 1 :: KEY_CHUNK]
    first_chunk = jnp.sum((chunk_ends < lowest_seg).astype(jnp.int32))
    last_chunk = last_query // KEY_CHUNK

    route_count = routes.shape[1]
    slots_dev = w_gate.shape[0]
    seq_count = lax.axis_size(SUB_AXES)
    slot_total = slots_dev * seq_count
    copies = slot_total // EXPERTS
    block_rows = tokens // copies
    capacity = 2 * block_rows * route_count // EXPERTS
    copy_of = (jnp.arange(tokens, dtype=jnp.int32) // block_rows)[:, None]
    slot_of = routes + EXPERTS * copy_of
    flat_expert = routes.reshape(copies, block_rows * route_count)
    onehot = (
        flat_expert[:, :, None] == jnp.arange(EXPERTS, dtype=jnp.int32)[None, None, :]
    ).astype(jnp.bfloat16)
    flat_rows = block_rows * route_count
    strictly_before = (
        jnp.arange(flat_rows, dtype=jnp.int32)[None, :] < jnp.arange(flat_rows, dtype=jnp.int32)[:, None]
    ).astype(jnp.bfloat16)
    before = jnp.einsum("ij,cje->cie", strictly_before, onehot, preferred_element_type=jnp.float32)
    slot_rank = (
        jnp.sum(before * onehot.astype(jnp.float32), axis=2).astype(jnp.int32).reshape(tokens, route_count)
    )
    half = capacity // 2
    core = lax.axis_index("tc")
    swap = [(0, 1), (1, 0)]
    own_route = (slot_rank // half) == core
    local_target = jnp.where(own_route, slot_of * half + slot_rank - core * half, -1)
    row_ids = jnp.arange(slot_total * half, dtype=jnp.int32)
    picks = local_target.T[:, None, :] == row_ids[None, :, None]
    dispatch = jnp.any(picks, axis=0).astype(jnp.bfloat16)
    joined, local_target, dispatch = lax.optimization_barrier((joined, local_target, dispatch))
    attended = chunk_attention(
        queries, joined, segment_ids, own_segs, query_index, first_chunk, last_chunk
    )
    attended = (
        attended.transpose(2, 0, 1, 3)
        .reshape(tokens, query_heads * HEAD_DIM)
    )
    attended = attended.astype(jnp.bfloat16)
    partial_out = jnp.dot(attended, w_out, preferred_element_type=jnp.float32)
    attn_mixed = tp_sum(partial_out.astype(jnp.bfloat16))
    residual = (hidden.astype(jnp.float32) + attn_mixed).astype(jnp.bfloat16)
    normed_moe = normalize(residual, norm_moe).astype(jnp.bfloat16)
    outbound = jnp.dot(dispatch, normed_moe, preferred_element_type=jnp.float32).astype(jnp.bfloat16)
    outbound = outbound.reshape(seq_count, slots_dev, half, model_width)
    arrived_own = lax.all_to_all(outbound, SUB_AXES, split_axis=0, concat_axis=0, tiled=True)
    arrived_other = lax.ppermute(arrived_own, "tc", swap)
    def expert_rows(arrived):
        gate_val = jnp.einsum("jsrd,sdf->jsrf", arrived, w_gate, preferred_element_type=jnp.float32)
        up_val = jnp.einsum("jsrd,sdf->jsrf", arrived, w_up, preferred_element_type=jnp.float32)
        activated = (jax.nn.silu(gate_val) * up_val).astype(jnp.bfloat16)
        group_part = jnp.einsum("jsrf,sfd->jsrd", activated, w_down, preferred_element_type=jnp.float32)
        return group_part.astype(jnp.bfloat16)

    sibling_part = lax.ppermute(expert_rows(arrived_other), "tc", swap)
    own_part = expert_rows(arrived_own)
    pair_sum = (own_part.astype(jnp.float32) + sibling_part.astype(jnp.float32)).astype(
        jnp.bfloat16
    )
    returned = lax.all_to_all(pair_sum, SUB_AXES, split_axis=0, concat_axis=0, tiled=True).reshape(
        slot_total * half, model_width
    )
    weighting = jnp.sum(
        jnp.where(local_target.T[:, :, None] == row_ids[None, None, :], gates.T[:, :, None], 0.0),
        axis=0,
    )
    combined = jnp.dot(
        weighting, returned, preferred_element_type=jnp.float32, precision=lax.Precision.HIGHEST
    )
    expert_sum = tp_sum(combined.astype(jnp.bfloat16))
    hidden_out = (residual.astype(jnp.float32) + expert_sum).astype(jnp.bfloat16)
    return (hidden_out, kv_cache)


def solution(mesh):
    seq_size, tp_size = mesh.devices.shape
    side = round(seq_size ** (1 / 3))
    sub_mesh = Mesh(
        mesh.devices.reshape(side, side, seq_size // side // side, tp_size // 2, 2), SUB_AXES + TP_AXES
    )
    return jax.shard_map(
        per_device,
        mesh=sub_mesh,
        in_specs=(
            P(SUB_AXES, None),
            P(),
            P(SUB_AXES, None),
            P(SUB_AXES, None),
            P(),
            P(),
            P(None, TP_AXES),
            P(None, TP_AXES),
            P(None, TP_AXES),
            P(TP_AXES, None),
            P(SUB_AXES, None, TP_AXES),
            P(SUB_AXES, None, TP_AXES),
            P(SUB_AXES, TP_AXES, None),
        ),
        out_specs=(P(SUB_AXES, None), P(SUB_AXES, None, TP_AXES)),
        check_vma=False,
    )
```

```python
import jax
import jax.numpy as jnp
from jax import lax
from jax.experimental import pallas as pl
from jax.experimental.pallas import tpu as pltpu
from jax.sharding import Mesh
from jax.sharding import PartitionSpec as P

HEAD_DIM = 64
EXPERTS = 32
SEG_VALUES = 8
KEY_CHUNK = 1024

EPS = 1e-06
SCORE_SCALE = 0.015625
SUB_AXES = ("sy", "sz", "sx")
TP_AXES = ("tz", "tc")


def normalize(values, gain):
    widened = values.astype(jnp.float32)
    return (
        widened
        * lax.rsqrt(jnp.mean(widened * widened, axis=-1, keepdims=True) + EPS)
        * gain.astype(jnp.float32)
    )


def rotary(tensor, positions):
    half_dim = tensor.shape[-1] // 2
    frequencies = 10000.0 ** (-jnp.arange(half_dim, dtype=jnp.float32) * 2.0 / tensor.shape[-1])
    angles = positions.astype(jnp.float32)[:, None] * frequencies[None, :]
    cosine = jnp.cos(angles)[:, None, :]
    sine_part = jnp.sin(angles)[:, None, :]
    lower_half = tensor[..., :half_dim]
    upper_half = tensor[..., half_dim:]
    return jnp.concatenate(
        [
            lower_half * cosine - upper_half * sine_part,
            upper_half * cosine + lower_half * sine_part,
        ],
        axis=-1,
    )


def attention_kernel(bounds_ref, q_ref, k_ref, v_ref, kseg_ref, qseg_ref, qidx_ref, o_ref, m_sc, l_sc, acc_sc):
    step = pl.program_id(0)

    @pl.when(step == 0)
    def _():
        m_sc[...] = jnp.full(m_sc.shape, -1e30, jnp.float32)
        l_sc[...] = jnp.zeros(l_sc.shape, jnp.float32)
        acc_sc[...] = jnp.zeros(acc_sc.shape, jnp.float32)

    chunk = bounds_ref[0] + step

    @pl.when(chunk <= bounds_ref[1])
    def _():
        key_index = chunk * KEY_CHUNK + lax.broadcasted_iota(jnp.int32, (1, KEY_CHUNK), 1)
        allowed = (qseg_ref[...] == kseg_ref[0]) & (qidx_ref[...] >= key_index)
        key_rows = k_ref[...]
        value_rows = v_ref[...]

        def one_slot(slot, carry):
            scores = (
                lax.dot_general(
                    q_ref[slot],
                    key_rows,
                    (((1,), (1,)), ((), ())),
                    preferred_element_type=jnp.float32,
                )
                * SCORE_SCALE
            )
            masked = jnp.where(allowed, scores, -1e30)
            running_max = m_sc[slot]
            new_max = jnp.maximum(running_max, jnp.max(masked, axis=-1, keepdims=True))
            weights = jnp.where(allowed, jnp.exp(masked - new_max), 0.0)
            factor = jnp.exp(running_max - new_max)
            l_sc[slot] = l_sc[slot] * factor + jnp.sum(weights, axis=-1, keepdims=True)
            acc_sc[slot] = acc_sc[slot] * factor + jnp.dot(
                weights.astype(jnp.bfloat16), value_rows, preferred_element_type=jnp.float32
            )
            m_sc[slot] = new_max
            return carry

        lax.fori_loop(0, q_ref.shape[0], one_slot, 0)

    @pl.when(step == pl.num_programs(0) - 1)
    def _():
        o_ref[...] = acc_sc[...] / l_sc[...]


def chunk_attention(queries, joined, segment_ids, own_segs, query_index, first_chunk, last_chunk):
    kv_heads, group_size, tokens, head_dim = queries.shape
    total, both_width = joined.shape
    kv_width = both_width // 2
    chunks = total // KEY_CHUNK
    head_mask = jnp.eye(kv_heads, dtype=jnp.bool_)[:, None, None, :, None]
    padded_queries = jnp.where(head_mask, queries[:, :, :, None, :], jnp.zeros((), queries.dtype)).reshape(
        kv_heads, group_size, tokens, kv_width
    )
    bounds = jnp.stack([first_chunk, last_chunk]).astype(jnp.int32)

    def key_map(step, bounds_ref):
        return (jnp.minimum(bounds_ref[0] + step, bounds_ref[1]), 0)

    def value_map(step, bounds_ref):
        return (jnp.minimum(bounds_ref[0] + step, bounds_ref[1]), 1)

    def seg_map(step, bounds_ref):
        return (jnp.minimum(bounds_ref[0] + step, bounds_ref[1]), 0, 0)

    def whole(step, bounds_ref):
        return (0, 0, 0, 0)

    def whole2(step, bounds_ref):
        return (0, 0)

    def whole3(step, bounds_ref):
        return (0, 0, 0)

    spec = pltpu.PrefetchScalarGridSpec(
        num_scalar_prefetch=1,
        grid=(chunks,),
        in_specs=[
            pl.BlockSpec((kv_heads * group_size, tokens, kv_width), whole3),
            pl.BlockSpec((KEY_CHUNK, kv_width), key_map),
            pl.BlockSpec((KEY_CHUNK, kv_width), value_map),
            pl.BlockSpec((1, 1, KEY_CHUNK), seg_map),
            pl.BlockSpec((tokens, 1), whole2),
            pl.BlockSpec((tokens, 1), whole2),
        ],
        out_specs=pl.BlockSpec((kv_heads * group_size, tokens, kv_width), whole3),
        scratch_shapes=[
            pltpu.VMEM((kv_heads * group_size, tokens, 1), jnp.float32),
            pltpu.VMEM((kv_heads * group_size, tokens, 1), jnp.float32),
            pltpu.VMEM((kv_heads * group_size, tokens, kv_width), jnp.float32),
        ],
    )
    out = pl.pallas_call(
        attention_kernel,
        grid_spec=spec,
        out_shape=jax.ShapeDtypeStruct((kv_heads * group_size, tokens, kv_width), jnp.float32),
        compiler_params=pltpu.CompilerParams(dimension_semantics=("arbitrary",)),
    )(
        bounds,
        padded_queries.reshape(kv_heads * group_size, tokens, kv_width),
        joined,
        joined,
        segment_ids.reshape(chunks, 1, KEY_CHUNK),
        own_segs.reshape(tokens, 1),
        query_index.reshape(tokens, 1),
    )
    out = out.reshape(kv_heads, group_size, tokens, kv_heads, head_dim)
    return jnp.stack([out[head, :, :, head] for head in range(kv_heads)])


def tp_sum(partial):
    swap = [(0, 1), (1, 0)]
    core = lax.axis_index("tc")
    rows, width = partial.shape
    halves = partial.reshape(rows, 2, width // 2)
    mine = lax.dynamic_index_in_dim(halves, core, axis=1, keepdims=False)
    theirs = lax.dynamic_index_in_dim(halves, 1 - core, axis=1, keepdims=False)
    pair = mine.astype(jnp.float32) + lax.ppermute(theirs, "tc", swap).astype(jnp.float32)
    pair = pair.astype(jnp.bfloat16)
    summed = pair.astype(jnp.float32) + lax.ppermute(pair, "tz", swap).astype(jnp.float32)
    other = lax.ppermute(summed, "tc", swap)
    return jnp.where(
        core == 0,
        jnp.concatenate([summed, other], axis=1),
        jnp.concatenate([other, summed], axis=1),
    )


def per_device(
    hidden,
    segment_ids,
    routes,
    gates,
    norm_attn,
    norm_moe,
    w_query,
    w_key,
    w_value,
    w_out,
    w_gate,
    w_up,
    w_down,
):
    tokens = hidden.shape[0]
    model_width = hidden.shape[1]
    total_tokens = segment_ids.shape[0]
    first_row = lax.axis_index(SUB_AXES) * tokens
    own_segs = lax.dynamic_slice_in_dim(segment_ids, first_row, tokens)
    seg_starts = jnp.sum(
        (segment_ids[None, :] < jnp.arange(SEG_VALUES, dtype=jnp.int32)[:, None]).astype(jnp.int32),
        axis=1,
    )
    query_index = first_row + jnp.arange(tokens, dtype=jnp.int32)
    positions = query_index - seg_starts[own_segs]
    normed = normalize(hidden, norm_attn).astype(jnp.bfloat16)
    query_heads = w_query.shape[1] // HEAD_DIM
    kv_heads = w_key.shape[1] // HEAD_DIM
    group_size = query_heads // kv_heads
    queries = jnp.dot(normed, w_query, preferred_element_type=jnp.float32).reshape(
        tokens, query_heads, HEAD_DIM
    )
    queries = (
        rotary(queries, positions)
        .astype(jnp.bfloat16)
        .reshape(tokens, kv_heads, group_size, HEAD_DIM)
        .transpose(1, 2, 0, 3)
    )
    key_raw = jnp.dot(normed, w_key, preferred_element_type=jnp.float32).reshape(
        tokens, kv_heads, HEAD_DIM
    )
    value_proj = jnp.dot(normed, w_value, preferred_element_type=jnp.float32).astype(jnp.bfloat16)
    kv_cache = jnp.stack(
        [key_raw.reshape(tokens, kv_heads * HEAD_DIM).astype(jnp.bfloat16), value_proj], axis=1
    )
    key_rot = rotary(key_raw, positions).astype(jnp.bfloat16)
    kv_width = kv_heads * HEAD_DIM
    joined = jnp.concatenate([key_rot.reshape(tokens, kv_width), value_proj], axis=1)
    for axis_name in SUB_AXES[::-1]:
        joined = lax.all_gather(joined, axis_name, axis=0, tiled=True)
    last_query = first_row + tokens - 1
    lowest_seg = own_segs[0]
    chunk_ends = segment_ids[KEY_CHUNK - 1 :: KEY_CHUNK]
    first_chunk = jnp.sum((chunk_ends < lowest_seg).astype(jnp.int32))
    last_chunk = last_query // KEY_CHUNK

    route_count = routes.shape[1]
    slots_dev = w_gate.shape[0]
    seq_count = lax.axis_size(SUB_AXES)
    slot_total = slots_dev * seq_count
    copies = slot_total // EXPERTS
    block_rows = tokens // copies
    capacity = 2 * block_rows * route_count // EXPERTS
    copy_of = (jnp.arange(tokens, dtype=jnp.int32) // block_rows)[:, None]
    slot_of = routes + EXPERTS * copy_of
    flat_expert = routes.reshape(copies, block_rows * route_count)
    onehot = (
        flat_expert[:, :, None] == jnp.arange(EXPERTS, dtype=jnp.int32)[None, None, :]
    ).astype(jnp.bfloat16)
    flat_rows = block_rows * route_count
    strictly_before = (
        jnp.arange(flat_rows, dtype=jnp.int32)[None, :] < jnp.arange(flat_rows, dtype=jnp.int32)[:, None]
    ).astype(jnp.bfloat16)
    before = jnp.einsum("ij,cje->cie", strictly_before, onehot, preferred_element_type=jnp.float32)
    slot_rank = (
        jnp.sum(before * onehot.astype(jnp.float32), axis=2).astype(jnp.int32).reshape(tokens, route_count)
    )
    half = capacity // 2
    core = lax.axis_index("tc")
    swap = [(0, 1), (1, 0)]
    own_route = (slot_rank // half) == core
    local_target = jnp.where(own_route, slot_of * half + slot_rank - core * half, -1)
    row_ids = jnp.arange(slot_total * half, dtype=jnp.int32)
    picks = local_target.T[:, None, :] == row_ids[None, :, None]
    dispatch = jnp.any(picks, axis=0).astype(jnp.bfloat16)
    joined, local_target, dispatch = lax.optimization_barrier((joined, local_target, dispatch))
    attended = chunk_attention(
        queries, joined, segment_ids, own_segs, query_index, first_chunk, last_chunk
    )
    attended = (
        attended.transpose(2, 0, 1, 3)
        .reshape(tokens, query_heads * HEAD_DIM)
    )
    attended = attended.astype(jnp.bfloat16)
    partial_out = jnp.dot(attended, w_out, preferred_element_type=jnp.float32)
    attn_mixed = tp_sum(partial_out.astype(jnp.bfloat16))
    residual = (hidden.astype(jnp.float32) + attn_mixed).astype(jnp.bfloat16)
    normed_moe = normalize(residual, norm_moe).astype(jnp.bfloat16)
    outbound = jnp.dot(dispatch, normed_moe, preferred_element_type=jnp.float32).astype(jnp.bfloat16)
    outbound = outbound.reshape(seq_count, slots_dev, half, model_width)
    arrived_own = lax.all_to_all(outbound, SUB_AXES, split_axis=0, concat_axis=0, tiled=True)
    arrived_other = lax.ppermute(arrived_own, "tc", swap)
    def expert_rows(arrived):
        gate_val = jnp.einsum("jsrd,sdf->jsrf", arrived, w_gate, preferred_element_type=jnp.float32)
        up_val = jnp.einsum("jsrd,sdf->jsrf", arrived, w_up, preferred_element_type=jnp.float32)
        activated = (jax.nn.silu(gate_val) * up_val).astype(jnp.bfloat16)
        group_part = jnp.einsum("jsrf,sfd->jsrd", activated, w_down, preferred_element_type=jnp.float32)
        return group_part.astype(jnp.bfloat16)

    sibling_part = lax.ppermute(expert_rows(arrived_other), "tc", swap)
    own_part = expert_rows(arrived_own)
    pair_sum = (own_part.astype(jnp.float32) + sibling_part.astype(jnp.float32)).astype(
        jnp.bfloat16
    )
    returned = lax.all_to_all(pair_sum, SUB_AXES, split_axis=0, concat_axis=0, tiled=True).reshape(
        slot_total * half, model_width
    )
    weighting = jnp.sum(
        jnp.where(local_target.T[:, :, None] == row_ids[None, None, :], gates.T[:, :, None], 0.0),
        axis=0,
    )
    combined = jnp.dot(
        weighting, returned, preferred_element_type=jnp.float32, precision=lax.Precision.HIGHEST
    )
    expert_sum = tp_sum(combined.astype(jnp.bfloat16))
    hidden_out = (residual.astype(jnp.float32) + expert_sum).astype(jnp.bfloat16)
    return (hidden_out, kv_cache)


def solution(mesh):
    seq_size, tp_size = mesh.devices.shape
    side = round(seq_size ** (1 / 3))
    sub_mesh = Mesh(
        mesh.devices.reshape(side, side, seq_size // side // side, tp_size // 2, 2), SUB_AXES + TP_AXES
    )
    return jax.shard_map(
        per_device,
        mesh=sub_mesh,
        in_specs=(
            P(SUB_AXES, None),
            P(),
            P(SUB_AXES, None),
            P(SUB_AXES, None),
            P(),
            P(),
            P(None, TP_AXES),
            P(None, TP_AXES),
            P(None, TP_AXES),
            P(TP_AXES, None),
            P(SUB_AXES, None, TP_AXES),
            P(SUB_AXES, None, TP_AXES),
            P(SUB_AXES, TP_AXES, None),
        ),
        out_specs=(P(SUB_AXES, None), P(SUB_AXES, None, TP_AXES)),
        check_vma=False,
    )
```

```python
import jax
import jax.numpy as jnp
from jax import lax
from jax.experimental import pallas as pl
from jax.experimental.pallas import tpu as pltpu
from jax.sharding import Mesh
from jax.sharding import PartitionSpec as P

HEAD_DIM = 64
EXPERTS = 32
SEG_VALUES = 8
KEY_CHUNK = 1024

EPS = 1e-06
SCORE_SCALE = 0.015625
SUB_AXES = ("sy", "sz", "sx")
TP_AXES = ("tz", "tc")


def normalize(values, gain):
    widened = values.astype(jnp.float32)
    return (
        widened
        * lax.rsqrt(jnp.mean(widened * widened, axis=-1, keepdims=True) + EPS)
        * gain.astype(jnp.float32)
    )


def rotary(tensor, positions):
    half_dim = tensor.shape[-1] // 2
    frequencies = 10000.0 ** (-jnp.arange(half_dim, dtype=jnp.float32) * 2.0 / tensor.shape[-1])
    angles = positions.astype(jnp.float32)[:, None] * frequencies[None, :]
    cosine = jnp.cos(angles)[:, None, :]
    sine_part = jnp.sin(angles)[:, None, :]
    lower_half = tensor[..., :half_dim]
    upper_half = tensor[..., half_dim:]
    return jnp.concatenate(
        [
            lower_half * cosine - upper_half * sine_part,
            upper_half * cosine + lower_half * sine_part,
        ],
        axis=-1,
    )


def attention_kernel(bounds_ref, q_ref, k_ref, v_ref, kseg_ref, qseg_ref, qidx_ref, o_ref, m_sc, l_sc, acc_sc):
    step = pl.program_id(0)
    kv_heads, group_size = q_ref.shape[0], q_ref.shape[1]

    @pl.when(step == 0)
    def _():
        m_sc[...] = jnp.full(m_sc.shape, -1e30, jnp.float32)
        l_sc[...] = jnp.zeros(l_sc.shape, jnp.float32)
        acc_sc[...] = jnp.zeros(acc_sc.shape, jnp.float32)

    chunk = bounds_ref[0] + step

    @pl.when(chunk <= bounds_ref[1])
    def _():
        key_index = chunk * KEY_CHUNK + lax.broadcasted_iota(jnp.int32, (1, KEY_CHUNK), 1)
        allowed = (qseg_ref[...] == kseg_ref[0]) & (qidx_ref[...] >= key_index)
        key_rows = k_ref[...]
        value_rows = v_ref[...]
        for head in range(kv_heads):
            for member in range(group_size):
                slot = head * group_size + member
                scores = (
                    lax.dot_general(
                        q_ref[head, member],
                        key_rows,
                        (((1,), (1,)), ((), ())),
                        preferred_element_type=jnp.float32,
                    )
                    * SCORE_SCALE
                )
                masked = jnp.where(allowed, scores, -1e30)
                running_max = m_sc[slot]
                new_max = jnp.maximum(running_max, jnp.max(masked, axis=-1, keepdims=True))
                weights = jnp.where(allowed, jnp.exp(masked - new_max), 0.0)
                factor = jnp.exp(running_max - new_max)
                l_sc[slot] = l_sc[slot] * factor + jnp.sum(weights, axis=-1, keepdims=True)
                acc_sc[slot] = acc_sc[slot] * factor + jnp.dot(
                    weights.astype(jnp.bfloat16), value_rows, preferred_element_type=jnp.float32
                )
                m_sc[slot] = new_max

    @pl.when(step == pl.num_programs(0) - 1)
    def _():
        o_ref[...] = acc_sc[...] / l_sc[...]


def chunk_attention(queries, joined, segment_ids, own_segs, query_index, first_chunk, last_chunk):
    kv_heads, group_size, tokens, head_dim = queries.shape
    total, both_width = joined.shape
    kv_width = both_width // 2
    chunks = total // KEY_CHUNK
    head_mask = jnp.eye(kv_heads, dtype=jnp.bool_)[:, None, None, :, None]
    padded_queries = jnp.where(head_mask, queries[:, :, :, None, :], jnp.zeros((), queries.dtype)).reshape(
        kv_heads, group_size, tokens, kv_width
    )
    bounds = jnp.stack([first_chunk, last_chunk]).astype(jnp.int32)

    def key_map(step, bounds_ref):
        return (jnp.minimum(bounds_ref[0] + step, bounds_ref[1]), 0)

    def value_map(step, bounds_ref):
        return (jnp.minimum(bounds_ref[0] + step, bounds_ref[1]), 1)

    def seg_map(step, bounds_ref):
        return (jnp.minimum(bounds_ref[0] + step, bounds_ref[1]), 0, 0)

    def whole(step, bounds_ref):
        return (0, 0, 0, 0)

    def whole2(step, bounds_ref):
        return (0, 0)

    def whole3(step, bounds_ref):
        return (0, 0, 0)

    spec = pltpu.PrefetchScalarGridSpec(
        num_scalar_prefetch=1,
        grid=(chunks,),
        in_specs=[
            pl.BlockSpec((kv_heads, group_size, tokens, kv_width), whole),
            pl.BlockSpec((KEY_CHUNK, kv_width), key_map),
            pl.BlockSpec((KEY_CHUNK, kv_width), value_map),
            pl.BlockSpec((1, 1, KEY_CHUNK), seg_map),
            pl.BlockSpec((tokens, 1), whole2),
            pl.BlockSpec((tokens, 1), whole2),
        ],
        out_specs=pl.BlockSpec((kv_heads * group_size, tokens, kv_width), whole3),
        scratch_shapes=[
            pltpu.VMEM((kv_heads * group_size, tokens, 1), jnp.float32),
            pltpu.VMEM((kv_heads * group_size, tokens, 1), jnp.float32),
            pltpu.VMEM((kv_heads * group_size, tokens, kv_width), jnp.float32),
        ],
    )
    out = pl.pallas_call(
        attention_kernel,
        grid_spec=spec,
        out_shape=jax.ShapeDtypeStruct((kv_heads * group_size, tokens, kv_width), jnp.float32),
        compiler_params=pltpu.CompilerParams(dimension_semantics=("arbitrary",)),
    )(
        bounds,
        padded_queries,
        joined,
        joined,
        segment_ids.reshape(chunks, 1, KEY_CHUNK),
        own_segs.reshape(tokens, 1),
        query_index.reshape(tokens, 1),
    )
    out = out.reshape(kv_heads, group_size, tokens, kv_heads, head_dim)
    return jnp.stack([out[head, :, :, head] for head in range(kv_heads)])


def tp_sum_into(partial, base):
    swap = [(0, 1), (1, 0)]
    core = lax.axis_index("tc")
    rows, width = partial.shape
    halves = partial.reshape(rows, 2, width // 2)
    mine = lax.dynamic_index_in_dim(halves, core, axis=1, keepdims=False)
    theirs = lax.dynamic_index_in_dim(halves, 1 - core, axis=1, keepdims=False)
    pair = mine.astype(jnp.float32) + lax.ppermute(theirs, "tc", swap).astype(jnp.float32)
    pair = pair.astype(jnp.bfloat16)
    summed = pair.astype(jnp.float32) + lax.ppermute(pair, "tz", swap).astype(jnp.float32)
    base_half = lax.dynamic_index_in_dim(base.reshape(rows, 2, width // 2), core, axis=1, keepdims=False)
    own_out = (base_half.astype(jnp.float32) + summed).astype(jnp.bfloat16)
    other = lax.ppermute(own_out, "tc", swap)
    return jnp.where(
        core == 0,
        jnp.concatenate([own_out, other], axis=1),
        jnp.concatenate([other, own_out], axis=1),
    )


def per_device(
    hidden,
    segment_ids,
    routes,
    gates,
    norm_attn,
    norm_moe,
    w_query,
    w_key,
    w_value,
    w_out,
    w_gate,
    w_up,
    w_down,
):
    tokens = hidden.shape[0]
    model_width = hidden.shape[1]
    total_tokens = segment_ids.shape[0]
    first_row = lax.axis_index(SUB_AXES) * tokens
    own_segs = lax.dynamic_slice_in_dim(segment_ids, first_row, tokens)
    seg_starts = jnp.sum(
        (segment_ids[None, :] < jnp.arange(SEG_VALUES, dtype=jnp.int32)[:, None]).astype(jnp.int32),
        axis=1,
    )
    query_index = first_row + jnp.arange(tokens, dtype=jnp.int32)
    positions = query_index - seg_starts[own_segs]
    normed = normalize(hidden, norm_attn).astype(jnp.bfloat16)
    query_heads = w_query.shape[1] // HEAD_DIM
    kv_heads = w_key.shape[1] // HEAD_DIM
    group_size = query_heads // kv_heads
    queries = jnp.dot(normed, w_query, preferred_element_type=jnp.float32).reshape(
        tokens, query_heads, HEAD_DIM
    )
    queries = (
        rotary(queries, positions)
        .astype(jnp.bfloat16)
        .reshape(tokens, kv_heads, group_size, HEAD_DIM)
        .transpose(1, 2, 0, 3)
    )
    key_raw = jnp.dot(normed, w_key, preferred_element_type=jnp.float32).reshape(
        tokens, kv_heads, HEAD_DIM
    )
    value_proj = jnp.dot(normed, w_value, preferred_element_type=jnp.float32).astype(jnp.bfloat16)
    kv_cache = jnp.stack(
        [key_raw.reshape(tokens, kv_heads * HEAD_DIM).astype(jnp.bfloat16), value_proj], axis=1
    )
    key_rot = rotary(key_raw, positions).astype(jnp.bfloat16)
    kv_width = kv_heads * HEAD_DIM
    joined = jnp.concatenate([key_rot.reshape(tokens, kv_width), value_proj], axis=1)
    for axis_name in SUB_AXES[::-1]:
        joined = lax.all_gather(joined, axis_name, axis=0, tiled=True)
    last_query = first_row + tokens - 1
    lowest_seg = own_segs[0]
    chunk_ends = segment_ids[KEY_CHUNK - 1 :: KEY_CHUNK]
    first_chunk = jnp.sum((chunk_ends < lowest_seg).astype(jnp.int32))
    last_chunk = last_query // KEY_CHUNK

    route_count = routes.shape[1]
    slots_dev = w_gate.shape[0]
    seq_count = lax.axis_size(SUB_AXES)
    slot_total = slots_dev * seq_count
    copies = slot_total // EXPERTS
    block_rows = tokens // copies
    capacity = 2 * block_rows * route_count // EXPERTS
    copy_of = (jnp.arange(tokens, dtype=jnp.int32) // block_rows)[:, None]
    slot_of = routes + EXPERTS * copy_of
    flat_expert = routes.reshape(copies, block_rows * route_count)
    onehot = (
        flat_expert[:, :, None] == jnp.arange(EXPERTS, dtype=jnp.int32)[None, None, :]
    ).astype(jnp.bfloat16)
    flat_rows = block_rows * route_count
    strictly_before = (
        jnp.arange(flat_rows, dtype=jnp.int32)[None, :] < jnp.arange(flat_rows, dtype=jnp.int32)[:, None]
    ).astype(jnp.bfloat16)
    before = jnp.einsum("ij,cje->cie", strictly_before, onehot, preferred_element_type=jnp.float32)
    slot_rank = (
        jnp.sum(before * onehot.astype(jnp.float32), axis=2).astype(jnp.int32).reshape(tokens, route_count)
    )
    half = capacity // 2
    core = lax.axis_index("tc")
    swap = [(0, 1), (1, 0)]
    own_route = (slot_rank // half) == core
    local_target = jnp.where(own_route, slot_of * half + slot_rank - core * half, -1)
    row_ids = jnp.arange(slot_total * half, dtype=jnp.int32)
    picks = local_target.T[:, None, :] == row_ids[None, :, None]
    dispatch = jnp.any(picks, axis=0).astype(jnp.bfloat16)
    joined, local_target, dispatch = lax.optimization_barrier((joined, local_target, dispatch))
    attended = chunk_attention(
        queries, joined, segment_ids, own_segs, query_index, first_chunk, last_chunk
    )
    attended = (
        attended.transpose(2, 0, 1, 3)
        .reshape(tokens, query_heads * HEAD_DIM)
    )
    attended = attended.astype(jnp.bfloat16)
    partial_out = jnp.dot(attended, w_out, preferred_element_type=jnp.float32)
    residual = tp_sum_into(partial_out.astype(jnp.bfloat16), hidden)
    normed_moe = normalize(residual, norm_moe).astype(jnp.bfloat16)
    outbound = jnp.dot(dispatch, normed_moe, preferred_element_type=jnp.float32).astype(jnp.bfloat16)
    outbound = outbound.reshape(seq_count, slots_dev, half, model_width)
    arrived_own = lax.all_to_all(outbound, SUB_AXES, split_axis=0, concat_axis=0, tiled=True)
    arrived_other = lax.ppermute(arrived_own, "tc", swap)
    def expert_rows(arrived):
        gate_val = jnp.einsum("jsrd,sdf->jsrf", arrived, w_gate, preferred_element_type=jnp.float32)
        up_val = jnp.einsum("jsrd,sdf->jsrf", arrived, w_up, preferred_element_type=jnp.float32)
        activated = (jax.nn.silu(gate_val) * up_val).astype(jnp.bfloat16)
        group_part = jnp.einsum("jsrf,sfd->jsrd", activated, w_down, preferred_element_type=jnp.float32)
        return group_part.astype(jnp.bfloat16)

    sibling_part = lax.ppermute(expert_rows(arrived_other), "tc", swap)
    own_part = expert_rows(arrived_own)
    pair_sum = (own_part.astype(jnp.float32) + sibling_part.astype(jnp.float32)).astype(
        jnp.bfloat16
    )
    returned = lax.all_to_all(pair_sum, SUB_AXES, split_axis=0, concat_axis=0, tiled=True).reshape(
        slot_total * half, model_width
    )
    weighting = jnp.sum(
        jnp.where(local_target.T[:, :, None] == row_ids[None, None, :], gates.T[:, :, None], 0.0),
        axis=0,
    )
    combined = jnp.dot(
        weighting, returned, preferred_element_type=jnp.float32, precision=lax.Precision.HIGHEST
    )
    hidden_out = tp_sum_into(combined.astype(jnp.bfloat16), residual)
    return (hidden_out, kv_cache)


def solution(mesh):
    seq_size, tp_size = mesh.devices.shape
    side = round(seq_size ** (1 / 3))
    sub_mesh = Mesh(
        mesh.devices.reshape(side, side, seq_size // side // side, tp_size // 2, 2), SUB_AXES + TP_AXES
    )
    return jax.shard_map(
        per_device,
        mesh=sub_mesh,
        in_specs=(
            P(SUB_AXES, None),
            P(),
            P(SUB_AXES, None),
            P(SUB_AXES, None),
            P(),
            P(),
            P(None, TP_AXES),
            P(None, TP_AXES),
            P(None, TP_AXES),
            P(TP_AXES, None),
            P(SUB_AXES, None, TP_AXES),
            P(SUB_AXES, None, TP_AXES),
            P(SUB_AXES, TP_AXES, None),
        ),
        out_specs=(P(SUB_AXES, None), P(SUB_AXES, None, TP_AXES)),
        check_vma=False,
    )
```

```python
import jax
import jax.numpy as jnp
from jax import lax
from jax.experimental import pallas as pl
from jax.experimental.pallas import tpu as pltpu
from jax.sharding import Mesh
from jax.sharding import PartitionSpec as P

HEAD_DIM = 64
EXPERTS = 32
SEG_VALUES = 8
KEY_CHUNK = 1024

EPS = 1e-06
SCORE_SCALE = 0.015625
SUB_AXES = ("sy", "sz", "sx")
TP_AXES = ("tz", "tc")


def normalize(values, gain):
    widened = values.astype(jnp.float32)
    return (
        widened
        * lax.rsqrt(jnp.mean(widened * widened, axis=-1, keepdims=True) + EPS)
        * gain.astype(jnp.float32)
    )


def rotary(tensor, positions):
    half_dim = tensor.shape[-1] // 2
    frequencies = 10000.0 ** (-jnp.arange(half_dim, dtype=jnp.float32) * 2.0 / tensor.shape[-1])
    angles = positions.astype(jnp.float32)[:, None] * frequencies[None, :]
    cosine = jnp.cos(angles)[:, None, :]
    sine_part = jnp.sin(angles)[:, None, :]
    lower_half = tensor[..., :half_dim]
    upper_half = tensor[..., half_dim:]
    return jnp.concatenate(
        [
            lower_half * cosine - upper_half * sine_part,
            upper_half * cosine + lower_half * sine_part,
        ],
        axis=-1,
    )


def attention_kernel(bounds_ref, q_ref, k_ref, v_ref, kseg_ref, qseg_ref, qidx_ref, o_ref, m_sc, l_sc, acc_sc):
    step = pl.program_id(0)
    kv_heads, group_size = q_ref.shape[0], q_ref.shape[1]

    @pl.when(step == 0)
    def _():
        m_sc[...] = jnp.full(m_sc.shape, -1e30, jnp.float32)
        l_sc[...] = jnp.zeros(l_sc.shape, jnp.float32)
        acc_sc[...] = jnp.zeros(acc_sc.shape, jnp.float32)

    chunk = bounds_ref[0] + step

    @pl.when(chunk <= bounds_ref[1])
    def _():
        key_index = chunk * KEY_CHUNK + lax.broadcasted_iota(jnp.int32, (1, KEY_CHUNK), 1)
        allowed = (qseg_ref[...] == kseg_ref[0]) & (qidx_ref[...] >= key_index)
        key_rows = k_ref[...]
        value_rows = v_ref[...]
        for head in range(kv_heads):
            for member in range(group_size):
                slot = head * group_size + member
                scores = (
                    lax.dot_general(
                        q_ref[head, member],
                        key_rows,
                        (((1,), (1,)), ((), ())),
                        preferred_element_type=jnp.float32,
                    )
                    * SCORE_SCALE
                )
                masked = jnp.where(allowed, scores, -1e30)
                running_max = m_sc[slot]
                new_max = jnp.maximum(running_max, jnp.max(masked, axis=-1, keepdims=True))
                weights = jnp.where(allowed, jnp.exp(masked - new_max), 0.0)
                factor = jnp.exp(running_max - new_max)
                l_sc[slot] = l_sc[slot] * factor + jnp.sum(weights, axis=-1, keepdims=True)
                acc_sc[slot] = acc_sc[slot] * factor + jnp.dot(
                    weights.astype(jnp.bfloat16), value_rows, preferred_element_type=jnp.float32
                )
                m_sc[slot] = new_max

    @pl.when(step == pl.num_programs(0) - 1)
    def _():
        o_ref[...] = acc_sc[...] / l_sc[...]


def chunk_attention(queries, joined, segment_ids, own_segs, query_index, first_chunk, last_chunk):
    kv_heads, group_size, tokens, head_dim = queries.shape
    total, both_width = joined.shape
    kv_width = both_width // 2
    chunks = total // KEY_CHUNK
    head_mask = jnp.eye(kv_heads, dtype=jnp.bool_)[:, None, None, :, None]
    padded_queries = jnp.where(head_mask, queries[:, :, :, None, :], jnp.zeros((), queries.dtype)).reshape(
        kv_heads, group_size, tokens, kv_width
    )
    bounds = jnp.stack([first_chunk, last_chunk]).astype(jnp.int32)

    def key_map(step, bounds_ref):
        return (jnp.minimum(bounds_ref[0] + step, bounds_ref[1]), 0)

    def value_map(step, bounds_ref):
        return (jnp.minimum(bounds_ref[0] + step, bounds_ref[1]), 1)

    def seg_map(step, bounds_ref):
        return (jnp.minimum(bounds_ref[0] + step, bounds_ref[1]), 0, 0)

    def whole(step, bounds_ref):
        return (0, 0, 0, 0)

    def whole2(step, bounds_ref):
        return (0, 0)

    def whole3(step, bounds_ref):
        return (0, 0, 0)

    spec = pltpu.PrefetchScalarGridSpec(
        num_scalar_prefetch=1,
        grid=(chunks,),
        in_specs=[
            pl.BlockSpec((kv_heads, group_size, tokens, kv_width), whole),
            pl.BlockSpec((KEY_CHUNK, kv_width), key_map),
            pl.BlockSpec((KEY_CHUNK, kv_width), value_map),
            pl.BlockSpec((1, 1, KEY_CHUNK), seg_map),
            pl.BlockSpec((tokens, 1), whole2),
            pl.BlockSpec((tokens, 1), whole2),
        ],
        out_specs=pl.BlockSpec((kv_heads * group_size, tokens, kv_width), whole3),
        scratch_shapes=[
            pltpu.VMEM((kv_heads * group_size, tokens, 1), jnp.float32),
            pltpu.VMEM((kv_heads * group_size, tokens, 1), jnp.float32),
            pltpu.VMEM((kv_heads * group_size, tokens, kv_width), jnp.float32),
        ],
    )
    out = pl.pallas_call(
        attention_kernel,
        grid_spec=spec,
        out_shape=jax.ShapeDtypeStruct((kv_heads * group_size, tokens, kv_width), jnp.float32),
        compiler_params=pltpu.CompilerParams(dimension_semantics=("arbitrary",)),
    )(
        bounds,
        padded_queries,
        joined,
        joined,
        segment_ids.reshape(chunks, 1, KEY_CHUNK),
        own_segs.reshape(tokens, 1),
        query_index.reshape(tokens, 1),
    )
    out = out.reshape(kv_heads, group_size, tokens, kv_heads, head_dim)
    return jnp.stack([out[head, :, :, head] for head in range(kv_heads)])


def tp_sum(partial):
    swap = [(0, 1), (1, 0)]
    core = lax.axis_index("tc")
    rows, width = partial.shape
    halves = partial.reshape(rows, 2, width // 2)
    mine = lax.dynamic_index_in_dim(halves, core, axis=1, keepdims=False)
    theirs = lax.dynamic_index_in_dim(halves, 1 - core, axis=1, keepdims=False)
    pair = mine.astype(jnp.float32) + lax.ppermute(theirs, "tc", swap).astype(jnp.float32)
    pair = pair.astype(jnp.bfloat16)
    summed = pair.astype(jnp.float32) + lax.ppermute(pair, "tz", swap).astype(jnp.float32)
    other = lax.ppermute(summed, "tc", swap)
    return jnp.where(
        core == 0,
        jnp.concatenate([summed, other], axis=1),
        jnp.concatenate([other, summed], axis=1),
    )


def per_device(
    hidden,
    segment_ids,
    routes,
    gates,
    norm_attn,
    norm_moe,
    w_query,
    w_key,
    w_value,
    w_out,
    w_gate,
    w_up,
    w_down,
):
    tokens = hidden.shape[0]
    model_width = hidden.shape[1]
    total_tokens = segment_ids.shape[0]
    first_row = lax.axis_index(SUB_AXES) * tokens
    own_segs = lax.dynamic_slice_in_dim(segment_ids, first_row, tokens)
    seg_starts = jnp.sum(
        (segment_ids[None, :] < jnp.arange(SEG_VALUES, dtype=jnp.int32)[:, None]).astype(jnp.int32),
        axis=1,
    )
    query_index = first_row + jnp.arange(tokens, dtype=jnp.int32)
    positions = query_index - seg_starts[own_segs]
    normed = normalize(hidden, norm_attn).astype(jnp.bfloat16)
    query_heads = w_query.shape[1] // HEAD_DIM
    kv_heads = w_key.shape[1] // HEAD_DIM
    group_size = query_heads // kv_heads
    queries = jnp.dot(normed, w_query, preferred_element_type=jnp.float32).reshape(
        tokens, query_heads, HEAD_DIM
    )
    queries = (
        rotary(queries, positions)
        .astype(jnp.bfloat16)
        .reshape(tokens, kv_heads, group_size, HEAD_DIM)
        .transpose(1, 2, 0, 3)
    )
    key_raw = jnp.dot(normed, w_key, preferred_element_type=jnp.float32).reshape(
        tokens, kv_heads, HEAD_DIM
    )
    value_proj = jnp.dot(normed, w_value, preferred_element_type=jnp.float32).astype(jnp.bfloat16)
    kv_cache = jnp.stack(
        [key_raw.reshape(tokens, kv_heads * HEAD_DIM).astype(jnp.bfloat16), value_proj], axis=1
    )
    key_rot = rotary(key_raw, positions).astype(jnp.bfloat16)
    kv_width = kv_heads * HEAD_DIM
    joined = jnp.concatenate([key_rot.reshape(tokens, kv_width), value_proj], axis=1)
    for axis_name in SUB_AXES[::-1]:
        joined = lax.all_gather(joined, axis_name, axis=0, tiled=True)
    last_query = first_row + tokens - 1
    lowest_seg = own_segs[0]
    chunk_ends = segment_ids[KEY_CHUNK - 1 :: KEY_CHUNK]
    first_chunk = jnp.sum((chunk_ends < lowest_seg).astype(jnp.int32))
    last_chunk = last_query // KEY_CHUNK

    route_count = routes.shape[1]
    slots_dev = w_gate.shape[0]
    seq_count = lax.axis_size(SUB_AXES)
    slot_total = slots_dev * seq_count
    copies = slot_total // EXPERTS
    block_rows = tokens // copies
    capacity = 2 * block_rows * route_count // EXPERTS
    copy_of = (jnp.arange(tokens, dtype=jnp.int32) // block_rows)[:, None]
    slot_of = routes + EXPERTS * copy_of
    flat_expert = routes.reshape(copies, block_rows * route_count)
    onehot = (
        flat_expert[:, :, None] == jnp.arange(EXPERTS, dtype=jnp.int32)[None, None, :]
    ).astype(jnp.bfloat16)
    flat_rows = block_rows * route_count
    strictly_before = (
        jnp.arange(flat_rows, dtype=jnp.int32)[None, :] < jnp.arange(flat_rows, dtype=jnp.int32)[:, None]
    ).astype(jnp.bfloat16)
    before = jnp.einsum("ij,cje->cie", strictly_before, onehot, preferred_element_type=jnp.float32)
    slot_rank = (
        jnp.sum(before * onehot.astype(jnp.float32), axis=2).astype(jnp.int32).reshape(tokens, route_count)
    )
    half = capacity // 2
    core = lax.axis_index("tc")
    swap = [(0, 1), (1, 0)]
    own_route = (slot_rank // half) == core
    local_target = jnp.where(own_route, slot_of * half + slot_rank - core * half, -1)
    row_ids = jnp.arange(slot_total * half, dtype=jnp.int32)
    picks = local_target.T[:, None, :] == row_ids[None, :, None]
    dispatch = jnp.any(picks, axis=0).astype(jnp.bfloat16)
    joined, local_target, dispatch = lax.optimization_barrier((joined, local_target, dispatch))
    attended = chunk_attention(
        queries, joined, segment_ids, own_segs, query_index, first_chunk, last_chunk
    )
    attended = (
        attended.transpose(2, 0, 1, 3)
        .reshape(tokens, query_heads * HEAD_DIM)
    )
    attended = attended.astype(jnp.bfloat16)
    partial_out = jnp.dot(attended, w_out, preferred_element_type=jnp.float32)
    attn_mixed = tp_sum(partial_out.astype(jnp.bfloat16))
    residual = (hidden.astype(jnp.float32) + attn_mixed).astype(jnp.bfloat16)
    normed_moe = normalize(residual, norm_moe).astype(jnp.bfloat16)
    outbound = jnp.dot(dispatch, normed_moe, preferred_element_type=jnp.float32).astype(jnp.bfloat16)
    outbound = outbound.reshape(seq_count, slots_dev, half, model_width)
    arrived_own = lax.all_to_all(outbound, SUB_AXES, split_axis=0, concat_axis=0, tiled=True)
    arrived_other = lax.ppermute(arrived_own, "tc", swap)
    def expert_rows(arrived):
        gate_val = jnp.einsum("jsrd,sdf->jsrf", arrived, w_gate, preferred_element_type=jnp.float32)
        up_val = jnp.einsum("jsrd,sdf->jsrf", arrived, w_up, preferred_element_type=jnp.float32)
        activated = (jax.nn.silu(gate_val) * up_val).astype(jnp.bfloat16)
        group_part = jnp.einsum("jsrf,sfd->jsrd", activated, w_down, preferred_element_type=jnp.float32)
        return group_part.astype(jnp.bfloat16)

    own_part = expert_rows(arrived_own)
    arrived_other, own_part = lax.optimization_barrier((arrived_other, own_part))
    sibling_part = lax.ppermute(expert_rows(arrived_other), "tc", swap)
    pair_sum = (own_part.astype(jnp.float32) + sibling_part.astype(jnp.float32)).astype(
        jnp.bfloat16
    )
    returned = lax.all_to_all(pair_sum, SUB_AXES, split_axis=0, concat_axis=0, tiled=True).reshape(
        slot_total * half, model_width
    )
    weighting = jnp.sum(
        jnp.where(local_target.T[:, :, None] == row_ids[None, None, :], gates.T[:, :, None], 0.0),
        axis=0,
    )
    combined = jnp.dot(
        weighting, returned, preferred_element_type=jnp.float32, precision=lax.Precision.HIGHEST
    )
    expert_sum = tp_sum(combined.astype(jnp.bfloat16))
    hidden_out = (residual.astype(jnp.float32) + expert_sum).astype(jnp.bfloat16)
    return (hidden_out, kv_cache)


def solution(mesh):
    seq_size, tp_size = mesh.devices.shape
    side = round(seq_size ** (1 / 3))
    sub_mesh = Mesh(
        mesh.devices.reshape(side, side, seq_size // side // side, tp_size // 2, 2), SUB_AXES + TP_AXES
    )
    return jax.shard_map(
        per_device,
        mesh=sub_mesh,
        in_specs=(
            P(SUB_AXES, None),
            P(),
            P(SUB_AXES, None),
            P(SUB_AXES, None),
            P(),
            P(),
            P(None, TP_AXES),
            P(None, TP_AXES),
            P(None, TP_AXES),
            P(TP_AXES, None),
            P(SUB_AXES, None, TP_AXES),
            P(SUB_AXES, None, TP_AXES),
            P(SUB_AXES, TP_AXES, None),
        ),
        out_specs=(P(SUB_AXES, None), P(SUB_AXES, None, TP_AXES)),
        check_vma=False,
    )
```
